512 devices in a mesh: dp: 32 (over y, x), ctx: 16 (over z, core).
Axes of the slice: x: 4, y: 8, z: 8, core: 2. Of those that a mesh axis runs over, the one named last changes fastest.
Arguments:
- q_raw: bfloat16 [32, 16, 128, 768], P('dp', 'ctx'), may hold values from -6 to 6
- k_raw: bfloat16 [32, 16, 128, 768], P('dp', 'ctx'), may hold values from -6 to 6
- values: bfloat16 [32, 16, 128, 768], P('dp', 'ctx'), may hold values from -6 to 6
- grad_out: bfloat16 [32, 16, 128, 768], P('dp', 'ctx'), may hold values from -6 to 6
- gain_q: float32 [768], replicated, may hold values from 0.6 to 3
- gain_k: float32 [768], replicated, may hold values from 0.6 to 3
- labels: int32 [6], replicated, may hold values from 0 to 1, as said below
- bands: int32 [6], replicated, may hold values from 2 to 8, as said below
- counts: int32 [32, 16], P('dp'), may hold values from 32 to 128, as said below
Outputs:
- attn_out: bfloat16 [32, 16, 128, 768], P('dp', 'ctx')
- grad_q_raw: bfloat16 [32, 16, 128, 768], P('dp', 'ctx')
- grad_k_raw: bfloat16 [32, 16, 128, 768], P('dp', 'ctx')
- grad_values: bfloat16 [32, 16, 128, 768], P('dp', 'ctx')
- grad_gain_q: float32 [768], replicated
- grad_gain_k: float32 [768], replicated
The draws below stay inside these ranges and needn't reach their ends.
Inputs may be any that keep to these rules, and one draw needn't show every extreme that they name: `labels`: exactly 3 of the 6 heads are labelled 1. `bands`: some temporal head has band 8. `counts`: every video has a frame with all 128 slots live.
All inputs are finite; a program needn't handle non-finite values.
Results may differ from the reference program's by a relative error of at most 0.015.
The reference program's roundings to bfloat16 on the way count: a program that leaves them out, or rounds other values in their place, can miss the bound.
Values may be sent and summed in bfloat16 or wider, within the bound.
No kernel may reach another device: no remote copies, remote signals or barrier semaphores. Data moves between devices by JAX's collectives and lax.ppermute only.
A program may use at most 64 MiB of HBM per device.

```python
import math
import jax
import jax.numpy as jnp
from jax import lax

HEADS = 6
HEAD_DIM = 128
TEMPORAL = 3
SLOTS = 128
WIDTH = 768
FRAMES = 16
VIDEOS = 32
SPAN = 8
N_CTX = 16


def head_tables(key):
    base_key = jax.random.fold_in(key, 5)
    head_perm = jax.random.permutation(jax.random.fold_in(base_key, 1), HEADS)
    label_set = (head_perm < TEMPORAL).astype(jnp.int32)
    band_set = jax.random.randint(jax.random.fold_in(base_key, 2), (HEADS,), 2, SPAN + 1)
    band_set = jnp.where(head_perm == 0, SPAN, band_set).astype(jnp.int32)
    return (label_set, band_set)


def draw_labels(key, part):
    return head_tables(key)[0]


def draw_bands(key, part):
    return head_tables(key)[1]


def draw_counts(key, part):
    live_counts = jax.random.randint(jax.random.fold_in(key, 9), (VIDEOS, FRAMES), SLOTS // 4, SLOTS + 1)
    full_frame = jax.random.randint(jax.random.fold_in(key, 10), (VIDEOS, 1), 0, FRAMES)
    live_counts = jnp.where(jnp.arange(FRAMES)[None, :] == full_frame, SLOTS, live_counts)
    return live_counts.astype(jnp.int32)


def draw_q_raw(key, part):
    drawn = jnp.clip(jax.random.normal(jax.random.fold_in(key, 1), (VIDEOS, FRAMES, SLOTS, WIDTH), jnp.float32), -6.0, 6.0)
    return drawn.astype(jnp.bfloat16)


def draw_k_raw(key, part):
    drawn = jnp.clip(jax.random.normal(jax.random.fold_in(key, 2), (VIDEOS, FRAMES, SLOTS, WIDTH), jnp.float32), -6.0, 6.0)
    return drawn.astype(jnp.bfloat16)


def draw_gain_q(key, part):
    gain_key = jax.random.fold_in(key, 21)
    return jax.random.uniform(gain_key, (WIDTH,), jnp.float32, 0.6, 1.4)


def draw_gain_k(key, part):
    gain_key = jax.random.fold_in(key, 22)
    return jax.random.uniform(gain_key, (WIDTH,), jnp.float32, 0.6, 1.4)


def block_scale(rng, shape, shards, low, top_value):
    def one(position, blocks):
        heights = jax.random.uniform(jax.random.fold_in(jax.random.fold_in(rng, 6), position), (blocks,), jnp.float32, low / len(shards), top_value / len(shards))
        return jnp.repeat(jnp.exp(heights), shape[position] // blocks).reshape((-1,) + (1,) * (len(shape) - position - 1))

    level = one(*shards[0])
    for cut in shards[1:]:
        level = level * one(*cut)
    return level


def gaussian(rng, shape, width, limit, cuts=(), kind=jnp.bfloat16):
    array = jax.random.normal(rng, shape, jnp.float32) * width
    if len(cuts) > 0:
        array = block_scale(rng, shape, cuts, -0.22, 0.18) * array
    return jnp.clip(array, min=-limit, max=limit).astype(kind)


def setup_inputs(seed: int = 0) -> dict:
    keys = jax.random.split(jax.random.key(seed), 10)
    q_raw = draw_q_raw(jax.random.fold_in(keys[9], 71), 0)
    k_raw = draw_k_raw(jax.random.fold_in(keys[9], 71), 0)
    values = gaussian(keys[2], (VIDEOS, FRAMES, SLOTS, WIDTH), 1.0, 6.0, ((0, 32), (1, 16)))
    grad_out = gaussian(keys[3], (VIDEOS, FRAMES, SLOTS, WIDTH), 1.0, 6.0, ((0, 32), (1, 16)))
    gain_q = draw_gain_q(jax.random.fold_in(keys[9], 71), 0)
    gain_k = draw_gain_k(jax.random.fold_in(keys[9], 71), 0)
    labels = draw_labels(jax.random.fold_in(keys[9], 71), 0)
    bands = draw_bands(jax.random.fold_in(keys[9], 71), 0)
    counts = draw_counts(jax.random.fold_in(keys[9], 71), 0)
    return {"q_raw": q_raw, "k_raw": k_raw, "values": values, "grad_out": grad_out, "gain_q": gain_q, "gain_k": gain_k, "labels": labels, "bands": bands, "counts": counts}


def normalize(raw_rows, gain_row):
    full_rows = raw_rows.astype(jnp.float32)
    inverse = lax.rsqrt(lax.optimization_barrier(jnp.mean(full_rows * full_rows, axis=-1, keepdims=True)) + 1e-06)
    unit_rows = full_rows * inverse
    return ((unit_rows * gain_row).astype(jnp.bfloat16), unit_rows, inverse)

def normalize_back(grad_rows, unit_rows, inverse, gain_row):
    scaled = grad_rows * gain_row
    return inverse * (scaled - unit_rows * lax.optimization_barrier(jnp.mean(scaled * unit_rows, axis=-1, keepdims=True)))

def attend(q_rows, k_rows, v_rows, allowed):
    factor = 1.0 / math.sqrt(q_rows.shape[-1])
    scores = jnp.einsum('hqd,hkd->hqk', q_rows.astype(jnp.float32), k_rows.astype(jnp.float32)) * factor
    scores = jnp.where(allowed, scores, -1e+30)
    row_peak = lax.optimization_barrier(jnp.max(scores, axis=-1, keepdims=True))
    exp_terms = jnp.where(allowed, jnp.exp(scores - row_peak), 0.0)
    weights = exp_terms / lax.optimization_barrier(jnp.sum(exp_terms, axis=-1, keepdims=True))
    prob_bf16 = weights.astype(jnp.bfloat16)
    mixed_rows = jnp.einsum('hqk,hkd->hqd', prob_bf16.astype(jnp.float32), v_rows.astype(jnp.float32))
    return (mixed_rows, weights, prob_bf16)

def attend_back(q_rows, k_rows, v_rows, weights, prob_bf16, upstream):
    factor = 1.0 / math.sqrt(q_rows.shape[-1])
    up_full = upstream.astype(jnp.float32)
    grad_v = jnp.einsum('hqk,hqd->hkd', prob_bf16.astype(jnp.float32), up_full)
    grad_p = jnp.einsum('hqd,hkd->hqk', up_full, v_rows.astype(jnp.float32))
    centre = lax.optimization_barrier(jnp.sum(weights * grad_p, axis=-1, keepdims=True))
    grad_s = (weights * (grad_p - centre)).astype(jnp.bfloat16).astype(jnp.float32)
    grad_q = jnp.einsum('hqk,hkd->hqd', grad_s, k_rows.astype(jnp.float32)) * factor
    grad_k = jnp.einsum('hqk,hqd->hkd', grad_s, q_rows.astype(jnp.float32)) * factor
    return (grad_q, grad_k, grad_v)

def spatial_frame(packed):
    q_rows, k_rows, v_rows, up_rows, length = packed
    slot_live = jnp.arange(SLOTS) < length
    near_count = HEADS - TEMPORAL
    allowed = jnp.broadcast_to(slot_live[None, None, :], (near_count, SLOTS, SLOTS))
    q_first = jnp.transpose(q_rows, (1, 0, 2))
    k_first = jnp.transpose(k_rows, (1, 0, 2))
    v_first = jnp.transpose(v_rows, (1, 0, 2))
    u_first = jnp.transpose(up_rows, (1, 0, 2))
    mixed_rows, weights, prob_bf16 = attend(q_first, k_first, v_first, allowed)
    mixed_rows = jnp.where(slot_live[None, :, None], mixed_rows, 0.0).astype(jnp.bfloat16)
    grad_q, grad_k, grad_v = attend_back(q_first, k_first, v_first, weights, prob_bf16, u_first)
    return (jnp.transpose(mixed_rows, (1, 0, 2)), jnp.transpose(grad_q, (1, 0, 2)), jnp.transpose(grad_k, (1, 0, 2)), jnp.transpose(grad_v, (1, 0, 2)))

def temporal_part(q_far, k_far, v_far, up_far, lengths, far_bands):
    padding = ((SPAN, SPAN), (0, 0), (0, 0), (0, 0))
    k_pad = jnp.pad(k_far, padding)
    v_pad = jnp.pad(v_far, padding)

    def heads_first(block):
        return jnp.transpose(block, (2, 0, 1, 3)).reshape(TEMPORAL, -1, HEAD_DIM)

    def step_block(carry, block_id):
        start = (block_id * SPAN).astype(jnp.int32)
        q_blk = heads_first(lax.dynamic_slice_in_dim(q_far, start, SPAN, 0))
        u_blk = heads_first(lax.dynamic_slice_in_dim(up_far, start, SPAN, 0))
        k_win = heads_first(lax.dynamic_slice_in_dim(k_pad, start, 3 * SPAN, 0))
        v_win = heads_first(lax.dynamic_slice_in_dim(v_pad, start, 3 * SPAN, 0))
        q_pos = start + jnp.arange(SPAN, dtype=jnp.int32)
        k_pos = start - SPAN + jnp.arange(3 * SPAN, dtype=jnp.int32)
        q_live = (q_pos[:, None] < lengths[None, :]).reshape(-1)
        k_live = ((k_pos[:, None] >= 0) & (k_pos[:, None] < SLOTS) & (k_pos[:, None] < lengths[None, :])).reshape(-1)
        pos_gap = jnp.abs(jnp.repeat(q_pos, FRAMES)[:, None] - jnp.repeat(k_pos, FRAMES)[None, :])
        allowed = (pos_gap[None] <= far_bands[:, None, None]) & k_live[None, None, :]
        mixed_rows, weights, prob_bf16 = attend(q_blk, k_win, v_win, allowed)
        mixed_rows = jnp.where(q_live[None, :, None], mixed_rows, 0.0).astype(jnp.bfloat16)
        grad_q, grad_k, grad_v = attend_back(q_blk, k_win, v_win, weights, prob_bf16, u_blk)
        window = jnp.stack([grad_k, grad_v]).reshape(2, TEMPORAL, 3 * SPAN, FRAMES, HEAD_DIM)
        window = jnp.transpose(window, (0, 2, 3, 1, 4))
        current = lax.dynamic_slice_in_dim(carry, start, 3 * SPAN, 1)
        carry = lax.dynamic_update_slice_in_dim(carry, current + window, start, 1)
        return (carry, (mixed_rows, grad_q))
    start_carry = jnp.zeros((2, SLOTS + 2 * SPAN, FRAMES, TEMPORAL, HEAD_DIM), jnp.float32)
    final_carry, (mixed_all, grad_q_all) = lax.scan(step_block, start_carry, jnp.arange(N_CTX, dtype=jnp.int32))

    def to_layout(stacked):
        shaped = stacked.reshape(N_CTX, TEMPORAL, SPAN, FRAMES, HEAD_DIM)
        return jnp.transpose(shaped, (0, 2, 3, 1, 4)).reshape(SLOTS, FRAMES, TEMPORAL, HEAD_DIM)
    own_grads = final_carry[:, SPAN:SPAN + SLOTS]
    return (to_layout(mixed_all), to_layout(grad_q_all), own_grads[0], own_grads[1])

def reference(q_raw, k_raw, values, grad_out, gain_q, gain_k, labels, bands, counts):
    head_order = jnp.argsort(labels, stable=True).astype(jnp.int32)
    near_heads = head_order[:HEADS - TEMPORAL]
    far_heads = head_order[HEADS - TEMPORAL:]
    far_bands = jnp.take(bands, far_heads)

    def split_heads(tensor):
        return tensor.reshape(FRAMES, SLOTS, HEADS, HEAD_DIM)

    def place_heads(near_part, far_part, kind_type):
        whole = jnp.zeros((FRAMES, SLOTS, HEADS, HEAD_DIM), kind_type)
        whole = whole.at[:, :, near_heads].set(near_part).at[:, :, far_heads].set(far_part)
        return whole.reshape(FRAMES, SLOTS, WIDTH)

    def one_video(packed):
        q_in, k_in, v_in, up_in, lengths = packed
        q_norm, q_unit, q_inv = normalize(q_in, gain_q)
        k_norm, k_unit, k_inv = normalize(k_in, gain_k)
        slot_live = jnp.arange(SLOTS)[None, :] < lengths[:, None]
        up_live = jnp.where(slot_live[:, :, None], up_in, jnp.zeros((), jnp.bfloat16))
        tensors = [split_heads(q_norm), split_heads(k_norm), split_heads(v_in), split_heads(up_live)]
        near_in = [jnp.take(tensor, near_heads, axis=2) for tensor in tensors]
        far_in = [jnp.transpose(jnp.take(tensor, far_heads, axis=2), (1, 0, 2, 3)) for tensor in tensors]
        near_out, near_gq, near_gk, near_gv = lax.map(spatial_frame, (near_in[0], near_in[1], near_in[2], near_in[3], lengths))
        far_out, far_gq, far_gk, far_gv = temporal_part(far_in[0], far_in[1], far_in[2], far_in[3], lengths, far_bands)

        def back_order(tensor):
            return jnp.transpose(tensor, (1, 0, 2, 3))
        attn_rows = place_heads(near_out, back_order(far_out), jnp.bfloat16)
        grad_qn = place_heads(near_gq, back_order(far_gq), jnp.float32)
        grad_kn = place_heads(near_gk, back_order(far_gk), jnp.float32)
        grad_vn = place_heads(near_gv, back_order(far_gv), jnp.float32)
        grad_q_in = normalize_back(grad_qn, q_unit, q_inv, gain_q).astype(jnp.bfloat16)
        grad_k_in = normalize_back(grad_kn, k_unit, k_inv, gain_k).astype(jnp.bfloat16)
        term_q = lax.optimization_barrier(jnp.sum(grad_qn * q_unit, axis=(0, 1)))
        term_k = lax.optimization_barrier(jnp.sum(grad_kn * k_unit, axis=(0, 1)))
        return (attn_rows, grad_q_in, grad_k_in, grad_vn.astype(jnp.bfloat16), term_q, term_k)
    attn_out, grad_q_raw, grad_k_raw, grad_values, terms_q, terms_k = lax.map(one_video, (q_raw, k_raw, values, grad_out, counts))
    return (attn_out, grad_q_raw, grad_k_raw, grad_values, lax.optimization_barrier(jnp.sum(terms_q, axis=0)), lax.optimization_barrier(jnp.sum(terms_k, axis=0)))
```

```python
import math

import jax
import jax.numpy as jnp
from jax import lax
from jax.sharding import PartitionSpec as P


def padded(shard, sides, width):
    for axis, dim in sides:
        size, length = (lax.axis_size(axis), shard.shape[dim])
        up = [(i, (i + 1) % size) for i in range(size - 1)]
        down = [(j, i) for i, j in up]
        last = lax.slice_in_dim(shard, length - width, length, axis=dim)
        leading = lax.slice_in_dim(shard, 0, width, axis=dim)
        before = lax.ppermute(last, axis, up)
        after = lax.ppermute(leading, axis, down)
        shard = jnp.concatenate([before, shard, after], axis=dim)
    return shard


def passed_along(shard, axis, by):
    length = lax.axis_size(axis)
    pairs = [(i, i + by) for i in range(length) if 0 <= i + by < length]
    return lax.ppermute(shard, axis, pairs)


def butterfly_sum(x, axes):
    for axis in axes:
        size = lax.axis_size(axis)
        step = 1
        while step < size:
            x = x + lax.ppermute(x, axis, [(i, i ^ step) for i in range(size)])
            step *= 2
    return x


def normalize(raw_rows, gain_row):
    full_rows = raw_rows.astype(jnp.float32)
    inverse = lax.rsqrt(jnp.mean(full_rows * full_rows, axis=-1, keepdims=True) + 1e-06)
    unit_rows = full_rows * inverse
    return ((unit_rows * gain_row).astype(jnp.bfloat16), unit_rows, inverse)


def normalize_back(grad_rows, unit_rows, inverse, gain_row):
    scaled = grad_rows * gain_row
    return inverse * (scaled - unit_rows * jnp.mean(scaled * unit_rows, axis=-1, keepdims=True))


def attend(q_rows, k_rows, v_rows, allowed):
    factor = 1.0 / math.sqrt(q_rows.shape[-1])
    scores = jnp.einsum("hqd,hkd->hqk", q_rows, k_rows, preferred_element_type=jnp.float32) * factor
    scores = jnp.where(allowed, scores, -1e30)
    row_peak = jnp.max(scores, axis=-1, keepdims=True)
    exp_terms = jnp.where(allowed, jnp.exp(scores - row_peak), 0.0)
    weights = exp_terms / jnp.sum(exp_terms, axis=-1, keepdims=True)
    prob_bf16 = weights.astype(jnp.bfloat16)
    mixed_rows = jnp.einsum("hqk,hkd->hqd", prob_bf16, v_rows, preferred_element_type=jnp.float32)
    return (mixed_rows, weights, prob_bf16)


def attend_back(q_rows, k_rows, v_rows, weights, prob_bf16, upstream):
    factor = 1.0 / math.sqrt(q_rows.shape[-1])
    grad_v = jnp.einsum("hqk,hqd->hkd", prob_bf16, upstream, preferred_element_type=jnp.float32)
    grad_p = jnp.einsum("hqd,hkd->hqk", upstream, v_rows, preferred_element_type=jnp.float32)
    centre = jnp.sum(weights * grad_p, axis=-1, keepdims=True)
    grad_s = (weights * (grad_p - centre)).astype(jnp.bfloat16)
    grad_q = jnp.einsum("hqk,hkd->hqd", grad_s, k_rows, preferred_element_type=jnp.float32) * factor
    grad_k = jnp.einsum("hqk,hqd->hkd", grad_s, q_rows, preferred_element_type=jnp.float32) * factor
    return (grad_q, grad_k, grad_v)


def body(q_raw, k_raw, values, grad_out, gain_q, gain_k, labels, bands, counts):
    frame_count = lax.axis_size("ctx")
    own_frame = lax.axis_index("ctx")
    head_count = labels.shape[0]
    channels = q_raw.shape[3]
    head_size = channels // head_count
    slot_count = q_raw.shape[2]
    pos_span = slot_count // frame_count
    lengths = counts[0]
    frame_ids = jnp.arange(frame_count)
    own_length = jnp.sum(jnp.where(frame_ids == own_frame, lengths, 0))
    slot_live = jnp.arange(slot_count) < own_length
    q_norm, q_unit, q_inv = normalize(q_raw[0, 0], gain_q)
    k_norm, k_unit, k_inv = normalize(k_raw[0, 0], gain_k)
    v_rows = values[0, 0]
    up_rows = jnp.where(slot_live[:, None], grad_out[0, 0], jnp.zeros((), jnp.bfloat16))
    far_count = head_count // 2
    head_order = jnp.argsort(labels, stable=True).astype(jnp.int32)
    near_heads = head_order[: head_count - far_count]
    far_heads = head_order[head_count - far_count :]
    back_order = jnp.argsort(head_order).astype(jnp.int32)

    def take_heads(row_block, chosen):
        return jnp.take(row_block.reshape(slot_count, head_count, head_size), chosen, axis=1)

    def heads_first(row_block, chosen):
        return jnp.transpose(take_heads(row_block, chosen), (1, 0, 2))

    def as_sent(row_block):
        return take_heads(row_block, far_heads).reshape(1, slot_count, far_count * head_size)

    def to_space(block, extent):
        shaped = block.reshape(frame_count, extent, far_count, head_size)
        return jnp.transpose(shaped, (2, 1, 0, 3)).reshape(
            far_count, extent * frame_count, head_size
        )

    def to_time(block):
        shaped = block.reshape(far_count, pos_span, frame_count, head_size)
        return jnp.transpose(shaped, (2, 1, 0, 3)).reshape(
            frame_count, pos_span, far_count * head_size
        )

    def grads_to_time(block):
        return jnp.transpose(block, (2, 1, 0, 3)).reshape(
            frame_count, pos_span, far_count * head_size
        )

    def head_gains(gain_row, chosen):
        return jnp.take(gain_row.reshape(head_count, head_size), chosen, axis=0)

    def spread(near_part, far_part):
        return jnp.take(jnp.concatenate([near_part, far_part], axis=0), back_order, axis=0)

    wide = far_count * head_size
    sent = lax.all_to_all(
        jnp.concatenate([as_sent(q_norm), as_sent(k_norm), as_sent(v_rows), as_sent(up_rows)], axis=2),
        "ctx",
        split_axis=1,
        concat_axis=0,
        tiled=True,
    )
    sent_q, sent_k, sent_v, sent_up = (sent[..., i * wide : (i + 1) * wide] for i in range(4))

    near_q = heads_first(q_norm, near_heads)
    near_k = heads_first(k_norm, near_heads)
    near_v = heads_first(v_rows, near_heads)
    near_up = heads_first(up_rows, near_heads)
    near_allowed = jnp.broadcast_to(
        slot_live[None, None, :], (near_q.shape[0], slot_count, slot_count)
    )
    near_out, near_w, near_p = attend(near_q, near_k, near_v, near_allowed)
    near_out = jnp.where(slot_live[None, :, None], near_out, 0.0).astype(jnp.bfloat16)
    near_gq, near_gk, near_gv = attend_back(near_q, near_k, near_v, near_w, near_p, near_up)
    near_term_q = jnp.sum(near_gq * heads_first(q_unit, near_heads), axis=1)
    near_term_k = jnp.sum(near_gk * heads_first(k_unit, near_heads), axis=1)

    band_pair = padded(jnp.stack([sent_k, sent_v]), (("ctx", 2),), pos_span)
    far_q = to_space(sent_q, pos_span)
    far_k = to_space(band_pair[0], 3 * pos_span)
    far_v = to_space(band_pair[1], 3 * pos_span)
    far_up = to_space(sent_up, pos_span)
    q_pos = own_frame * pos_span + jnp.arange(pos_span)
    k_pos = own_frame * pos_span - pos_span + jnp.arange(3 * pos_span)
    q_live = (q_pos[:, None] < lengths[None, :]).reshape(-1)
    k_live = (
        (k_pos[:, None] >= 0) & (k_pos[:, None] < slot_count) & (k_pos[:, None] < lengths[None, :])
    ).reshape(-1)
    pos_gap = jnp.abs(
        jnp.repeat(q_pos, frame_count)[:, None] - jnp.repeat(k_pos, frame_count)[None, :]
    )
    far_bands = jnp.take(bands, far_heads)
    far_allowed = (pos_gap[None] <= far_bands[:, None, None]) & k_live[None, None, :]
    far_out, far_w, far_p = attend(far_q, far_k, far_v, far_allowed)
    far_out = jnp.where(q_live[None, :, None], far_out, 0.0).astype(jnp.bfloat16)
    far_gq, far_gk, far_gv = attend_back(far_q, far_k, far_v, far_w, far_p, far_up)

    far_term_q = jnp.sum(far_gq * far_q.astype(jnp.float32), axis=1) / head_gains(gain_q, far_heads)
    far_term_k = jnp.sum(far_gk * far_k.astype(jnp.float32), axis=1) / head_gains(gain_k, far_heads)
    terms = jnp.stack([spread(near_term_q, far_term_q), spread(near_term_k, far_term_k)])
    totals = butterfly_sum(terms, ("ctx", "dp")).reshape(2, channels)

    key_grads = jnp.stack([far_gk, far_gv]).reshape(
        2, far_count, 3 * pos_span, frame_count, head_size
    )
    from_upper = passed_along(key_grads[:, :, :pos_span].astype(jnp.bfloat16), "ctx", -1).astype(
        jnp.float32
    )
    from_lower = passed_along(
        key_grads[:, :, 2 * pos_span :].astype(jnp.bfloat16), "ctx", 1
    ).astype(jnp.float32)
    own_grads = key_grads[:, :, pos_span : 2 * pos_span] + from_upper + from_lower
    back = lax.all_to_all(
        jnp.concatenate(
            [
                to_time(far_out),
                to_time(far_gq).astype(jnp.bfloat16),
                grads_to_time(own_grads[0]).astype(jnp.bfloat16),
                grads_to_time(own_grads[1]).astype(jnp.bfloat16),
            ],
            axis=2,
        ),
        "ctx",
        split_axis=0,
        concat_axis=1,
        tiled=True,
    )
    back_out, back_q, back_k, back_v = (back[..., i * wide : (i + 1) * wide] for i in range(4))

    def merged(near_part, far_back, kind):
        far_rows = far_back.reshape(slot_count, far_count, head_size).astype(kind)
        near_rows = jnp.transpose(near_part, (1, 0, 2)).astype(kind)
        both = jnp.concatenate([near_rows, far_rows], axis=1)
        return jnp.take(both, back_order, axis=1).reshape(slot_count, channels)

    attn_rows = merged(near_out, back_out, jnp.bfloat16)
    grad_qn = merged(near_gq, back_q, jnp.float32)
    grad_kn = merged(near_gk, back_k, jnp.float32)
    grad_vn = merged(near_gv, back_v, jnp.float32)
    grad_q_rows = normalize_back(grad_qn, q_unit, q_inv, gain_q).astype(jnp.bfloat16)
    grad_k_rows = normalize_back(grad_kn, k_unit, k_inv, gain_k).astype(jnp.bfloat16)

    def as_shard(row_block):
        return row_block.reshape(1, 1, slot_count, channels)

    return (
        as_shard(attn_rows),
        as_shard(grad_q_rows),
        as_shard(grad_k_rows),
        as_shard(grad_vn.astype(jnp.bfloat16)),
        totals[0],
        totals[1],
    )


def solution(mesh):
    placed = (
        P("dp", "ctx", None, None),
        P("dp", "ctx", None, None),
        P("dp", "ctx", None, None),
        P("dp", "ctx", None, None),
        P(),
        P(),
        P(),
        P(),
        P("dp", None),
    )
    return jax.shard_map(
        body,
        mesh=mesh,
        in_specs=placed,
        out_specs=(
            P("dp", "ctx", None, None),
            P("dp", "ctx", None, None),
            P("dp", "ctx", None, None),
            P("dp", "ctx", None, None),
            P(),
            P(),
        ),
        check_vma=False,
    )
```

```python
import math

import jax
import jax.numpy as jnp
from jax import lax
from jax.sharding import PartitionSpec as P


def padded(shard, sides, width):
    for axis, dim in sides:
        size, length = (lax.axis_size(axis), shard.shape[dim])
        up = [(i, (i + 1) % size) for i in range(size - 1)]
        down = [(j, i) for i, j in up]
        last = lax.slice_in_dim(shard, length - width, length, axis=dim)
        leading = lax.slice_in_dim(shard, 0, width, axis=dim)
        before = lax.ppermute(last, axis, up)
        after = lax.ppermute(leading, axis, down)
        shard = jnp.concatenate([before, shard, after], axis=dim)
    return shard


def passed_along(shard, axis, by):
    length = lax.axis_size(axis)
    pairs = [(i, i + by) for i in range(length) if 0 <= i + by < length]
    return lax.ppermute(shard, axis, pairs)


def butterfly_sum(x, axes):
    for axis in axes:
        size = lax.axis_size(axis)
        step = 1
        while step < size:
            x = x + lax.ppermute(x, axis, [(i, i ^ step) for i in range(size)])
            step *= 2
    return x


def normalize(raw_rows, gain_row):
    full_rows = raw_rows.astype(jnp.float32)
    inverse = lax.rsqrt(jnp.mean(full_rows * full_rows, axis=-1, keepdims=True) + 1e-06)
    unit_rows = full_rows * inverse
    return ((unit_rows * gain_row).astype(jnp.bfloat16), unit_rows, inverse)


def normalize_back(grad_rows, unit_rows, inverse, gain_row):
    scaled = grad_rows * gain_row
    return inverse * (scaled - unit_rows * jnp.mean(scaled * unit_rows, axis=-1, keepdims=True))


def attend(q_rows, k_rows, v_rows, allowed):
    factor = 1.0 / math.sqrt(q_rows.shape[-1])
    scores = jnp.einsum("hqd,hkd->hqk", q_rows, k_rows, preferred_element_type=jnp.float32) * factor
    scores = jnp.where(allowed, scores, -1e30)
    row_peak = jnp.max(scores, axis=-1, keepdims=True)
    exp_terms = jnp.where(allowed, jnp.exp(scores - row_peak), 0.0)
    weights = exp_terms / jnp.sum(exp_terms, axis=-1, keepdims=True)
    prob_bf16 = weights.astype(jnp.bfloat16)
    mixed_rows = jnp.einsum("hqk,hkd->hqd", prob_bf16, v_rows, preferred_element_type=jnp.float32)
    return (mixed_rows, weights, prob_bf16)


def attend_back(q_rows, k_rows, v_rows, weights, prob_bf16, upstream):
    factor = 1.0 / math.sqrt(q_rows.shape[-1])
    grad_v = jnp.einsum("hqk,hqd->hkd", prob_bf16, upstream, preferred_element_type=jnp.float32)
    grad_p = jnp.einsum("hqd,hkd->hqk", upstream, v_rows, preferred_element_type=jnp.float32)
    centre = jnp.sum(weights * grad_p, axis=-1, keepdims=True)
    grad_s = (weights * (grad_p - centre)).astype(jnp.bfloat16)
    grad_q = jnp.einsum("hqk,hkd->hqd", grad_s, k_rows, preferred_element_type=jnp.float32) * factor
    grad_k = jnp.einsum("hqk,hqd->hkd", grad_s, q_rows, preferred_element_type=jnp.float32) * factor
    return (grad_q, grad_k, grad_v)


def body(q_raw, k_raw, values, grad_out, gain_q, gain_k, labels, bands, counts):
    frame_count = lax.axis_size("ctx")
    own_frame = lax.axis_index("ctx")
    head_count = labels.shape[0]
    channels = q_raw.shape[3]
    head_size = channels // head_count
    slot_count = q_raw.shape[2]
    pos_span = slot_count // frame_count
    lengths = counts[0]
    frame_ids = jnp.arange(frame_count)
    own_length = jnp.sum(jnp.where(frame_ids == own_frame, lengths, 0))
    slot_live = jnp.arange(slot_count) < own_length
    q_norm, q_unit, q_inv = normalize(q_raw[0, 0], gain_q)
    k_norm, k_unit, k_inv = normalize(k_raw[0, 0], gain_k)
    v_rows = values[0, 0]
    up_rows = jnp.where(slot_live[:, None], grad_out[0, 0], jnp.zeros((), jnp.bfloat16))
    far_count = head_count // 2
    near_count = head_count - far_count
    ids = jnp.arange(head_count)
    before = (labels[None, :] < labels[:, None]) | (
        (labels[None, :] == labels[:, None]) & (ids[None, :] < ids[:, None])
    )
    back_order = jnp.sum(before.astype(jnp.int32), axis=1)
    head_order = jnp.sum(jnp.where(back_order[None, :] == ids[:, None], ids[None, :], 0), axis=1)
    far_heads = head_order[near_count:]
    wide = far_count * head_size

    def sorted_heads(block):
        shaped = block.reshape(block.shape[:-1] + (head_count, head_size))
        return jnp.take(shaped, head_order, axis=-2)

    def heads_first(block):
        return jnp.transpose(block, (1, 0, 2))

    def to_space(block, extent):
        shaped = block.reshape(frame_count, extent, far_count, head_size)
        return jnp.transpose(shaped, (2, 1, 0, 3)).reshape(
            far_count, extent * frame_count, head_size
        )

    def to_time(block, extent):
        shaped = block.reshape(far_count, extent, frame_count, head_size)
        return jnp.transpose(shaped, (2, 1, 0, 3)).reshape(frame_count, extent, wide)

    def windows(rows):
        blocks = jnp.pad(rows, ((pos_span, pos_span), (0, 0))).reshape(frame_count + 2, pos_span, wide)
        return jnp.concatenate([blocks[:-2], blocks[1:-1], blocks[2:]], axis=1)

    def head_gains(gain_row):
        return jnp.take(gain_row.reshape(head_count, head_size), far_heads, axis=0)

    def spread(near_part, far_part):
        return jnp.take(jnp.concatenate([near_part, far_part], axis=0), back_order, axis=0)

    picked = sorted_heads(jnp.stack([q_norm, k_norm, v_rows, up_rows]))
    units = sorted_heads(jnp.stack([q_unit, k_unit]))[:, :, :near_count]
    far_rows = picked[:, :, near_count:].reshape(4, slot_count, wide)

    outgoing = jnp.concatenate(
        [
            far_rows[0].reshape(frame_count, pos_span, wide),
            far_rows[3].reshape(frame_count, pos_span, wide),
            windows(far_rows[1]),
            windows(far_rows[2]),
        ],
        axis=1,
    )
    sent = lax.all_to_all(outgoing, "ctx", split_axis=0, concat_axis=0, tiled=True)

    near_q, near_k, near_v, near_up = (heads_first(picked[i, :, :near_count]) for i in range(4))
    near_allowed = jnp.broadcast_to(
        slot_live[None, None, :], (near_count, slot_count, slot_count)
    )
    near_out, near_w, near_p = attend(near_q, near_k, near_v, near_allowed)
    near_out = jnp.where(slot_live[None, :, None], near_out, 0.0).astype(jnp.bfloat16)
    near_gq, near_gk, near_gv = attend_back(near_q, near_k, near_v, near_w, near_p, near_up)
    near_term_q = jnp.sum(near_gq * heads_first(units[0]), axis=1)
    near_term_k = jnp.sum(near_gk * heads_first(units[1]), axis=1)

    far_q = to_space(sent[:, :pos_span], pos_span)
    far_up = to_space(sent[:, pos_span : 2 * pos_span], pos_span)
    far_k = to_space(sent[:, 2 * pos_span : 5 * pos_span], 3 * pos_span)
    far_v = to_space(sent[:, 5 * pos_span :], 3 * pos_span)
    q_pos = own_frame * pos_span + jnp.arange(pos_span)
    k_pos = own_frame * pos_span - pos_span + jnp.arange(3 * pos_span)
    q_live = (q_pos[:, None] < lengths[None, :]).reshape(-1)
    k_live = (
        (k_pos[:, None] >= 0) & (k_pos[:, None] < slot_count) & (k_pos[:, None] < lengths[None, :])
    ).reshape(-1)
    pos_gap = jnp.abs(
        jnp.repeat(q_pos, frame_count)[:, None] - jnp.repeat(k_pos, frame_count)[None, :]
    )
    far_bands = jnp.take(bands, far_heads)
    far_allowed = (pos_gap[None] <= far_bands[:, None, None]) & k_live[None, None, :]
    far_out, far_w, far_p = attend(far_q, far_k, far_v, far_allowed)
    far_out = jnp.where(q_live[None, :, None], far_out, 0.0).astype(jnp.bfloat16)
    far_gq, far_gk, far_gv = attend_back(far_q, far_k, far_v, far_w, far_p, far_up)

    far_term_q = jnp.sum(far_gq * far_q.astype(jnp.float32), axis=1) / head_gains(gain_q)
    far_term_k = jnp.sum(far_gk * far_k.astype(jnp.float32), axis=1) / head_gains(gain_k)
    terms = jnp.stack([spread(near_term_q, far_term_q), spread(near_term_k, far_term_k)])
    terms_hi = terms.astype(jnp.bfloat16)
    terms_lo = (terms - terms_hi.astype(jnp.float32)).astype(jnp.bfloat16)
    term_rows = jnp.stack([terms_hi, terms_lo]).reshape(-1, wide)
    term_count = term_rows.shape[0]

    back = lax.all_to_all(
        jnp.concatenate(
            [
                to_time(far_out, pos_span),
                to_time(far_gq, pos_span).astype(jnp.bfloat16),
                to_time(far_gk, 3 * pos_span).astype(jnp.bfloat16),
                to_time(far_gv, 3 * pos_span).astype(jnp.bfloat16),
                jnp.broadcast_to(term_rows[None], (frame_count, term_count, wide)),
            ],
            axis=1,
        ),
        "ctx",
        split_axis=0,
        concat_axis=0,
        tiled=True,
    )
    got_terms = back[:, 8 * pos_span :].reshape(frame_count, 2, 2, head_count, head_size)
    got_terms = got_terms[:, 0].astype(jnp.float32) + got_terms[:, 1].astype(jnp.float32)
    totals = butterfly_sum(jnp.sum(got_terms, axis=0), ("dp",)).reshape(2, channels)

    def summed(window_rows):
        parts = window_rows.astype(jnp.float32).reshape(frame_count, 3, pos_span, wide)
        zero = jnp.zeros((1, pos_span, wide), jnp.float32)
        below = jnp.concatenate([zero, parts[:-1, 2]], axis=0)
        above = jnp.concatenate([parts[1:, 0], zero], axis=0)
        return (parts[:, 1] + above + below).reshape(slot_count, wide)

    back_out = back[:, :pos_span].reshape(slot_count, wide)
    back_q = back[:, pos_span : 2 * pos_span].reshape(slot_count, wide)
    back_k = summed(back[:, 2 * pos_span : 5 * pos_span])
    back_v = summed(back[:, 5 * pos_span : 8 * pos_span])

    near_rows = jnp.stack([near_out.astype(jnp.float32), near_gq, near_gk, near_gv])
    near_rows = jnp.transpose(near_rows, (0, 2, 1, 3))
    far_back = jnp.stack(
        [back_out.astype(jnp.float32), back_q.astype(jnp.float32), back_k, back_v]
    ).reshape(4, slot_count, far_count, head_size)
    whole = jnp.take(jnp.concatenate([near_rows, far_back], axis=2), back_order, axis=2)
    whole = whole.reshape(4, slot_count, channels)
    attn_rows = whole[0].astype(jnp.bfloat16)
    grad_qn, grad_kn, grad_vn = whole[1], whole[2], whole[3]
    grad_q_rows = normalize_back(grad_qn, q_unit, q_inv, gain_q).astype(jnp.bfloat16)
    grad_k_rows = normalize_back(grad_kn, k_unit, k_inv, gain_k).astype(jnp.bfloat16)

    def as_shard(row_block):
        return row_block.reshape(1, 1, slot_count, channels)

    return (
        as_shard(attn_rows),
        as_shard(grad_q_rows),
        as_shard(grad_k_rows),
        as_shard(grad_vn.astype(jnp.bfloat16)),
        totals[0],
        totals[1],
    )


def solution(mesh):
    placed = (
        P("dp", "ctx", None, None),
        P("dp", "ctx", None, None),
        P("dp", "ctx", None, None),
        P("dp", "ctx", None, None),
        P(),
        P(),
        P(),
        P(),
        P("dp", None),
    )
    return jax.shard_map(
        body,
        mesh=mesh,
        in_specs=placed,
        out_specs=(
            P("dp", "ctx", None, None),
            P("dp", "ctx", None, None),
            P("dp", "ctx", None, None),
            P("dp", "ctx", None, None),
            P(),
            P(),
        ),
        check_vma=False,
    )
```

```python
import math

import jax
import jax.numpy as jnp
from jax import lax
from jax.sharding import PartitionSpec as P


def padded(shard, sides, width):
    for axis, dim in sides:
        size, length = (lax.axis_size(axis), shard.shape[dim])
        up = [(i, (i + 1) % size) for i in range(size - 1)]
        down = [(j, i) for i, j in up]
        last = lax.slice_in_dim(shard, length - width, length, axis=dim)
        leading = lax.slice_in_dim(shard, 0, width, axis=dim)
        before = lax.ppermute(last, axis, up)
        after = lax.ppermute(leading, axis, down)
        shard = jnp.concatenate([before, shard, after], axis=dim)
    return shard


def passed_along(shard, axis, by):
    length = lax.axis_size(axis)
    pairs = [(i, i + by) for i in range(length) if 0 <= i + by < length]
    return lax.ppermute(shard, axis, pairs)


def butterfly_sum(x, axes):
    for axis in axes:
        size = lax.axis_size(axis)
        step = 1
        while step < size:
            x = x + lax.ppermute(x, axis, [(i, i ^ step) for i in range(size)])
            step *= 2
    return x


def normalize(raw_rows, gain_row):
    full_rows = raw_rows.astype(jnp.float32)
    inverse = lax.rsqrt(jnp.mean(full_rows * full_rows, axis=-1, keepdims=True) + 1e-06)
    unit_rows = full_rows * inverse
    return ((unit_rows * gain_row).astype(jnp.bfloat16), unit_rows, inverse)


def normalize_back(grad_rows, unit_rows, inverse, gain_row):
    scaled = grad_rows * gain_row
    return inverse * (scaled - unit_rows * jnp.mean(scaled * unit_rows, axis=-1, keepdims=True))


def attend(q_rows, k_rows, v_rows, allowed):
    factor = 1.0 / math.sqrt(q_rows.shape[-1])
    scores = jnp.einsum("hqd,hkd->hqk", q_rows, k_rows, preferred_element_type=jnp.float32) * factor
    scores = jnp.where(allowed, scores, -1e30)
    row_peak = jnp.max(scores, axis=-1, keepdims=True)
    exp_terms = jnp.where(allowed, jnp.exp(scores - row_peak), 0.0)
    weights = exp_terms / jnp.sum(exp_terms, axis=-1, keepdims=True)
    prob_bf16 = weights.astype(jnp.bfloat16)
    mixed_rows = jnp.einsum("hqk,hkd->hqd", prob_bf16, v_rows, preferred_element_type=jnp.float32)
    return (mixed_rows, weights, prob_bf16)


def attend_back(q_rows, k_rows, v_rows, weights, prob_bf16, upstream):
    factor = 1.0 / math.sqrt(q_rows.shape[-1])
    grad_v = jnp.einsum("hqk,hqd->hkd", prob_bf16, upstream, preferred_element_type=jnp.float32)
    grad_p = jnp.einsum("hqd,hkd->hqk", upstream, v_rows, preferred_element_type=jnp.float32)
    centre = jnp.sum(weights * grad_p, axis=-1, keepdims=True)
    grad_s = (weights * (grad_p - centre)).astype(jnp.bfloat16)
    grad_q = jnp.einsum("hqk,hkd->hqd", grad_s, k_rows, preferred_element_type=jnp.float32) * factor
    grad_k = jnp.einsum("hqk,hqd->hkd", grad_s, q_rows, preferred_element_type=jnp.float32) * factor
    return (grad_q, grad_k, grad_v)


def body(q_raw, k_raw, values, grad_out, gain_q, gain_k, labels, bands, counts):
    frame_count = lax.axis_size("ctx")
    own_frame = lax.axis_index("ctx")
    head_count = labels.shape[0]
    channels = q_raw.shape[3]
    head_size = channels // head_count
    slot_count = q_raw.shape[2]
    pos_span = slot_count // frame_count
    lengths = counts[0]
    frame_ids = jnp.arange(frame_count)
    own_length = jnp.sum(jnp.where(frame_ids == own_frame, lengths, 0))
    slot_live = jnp.arange(slot_count) < own_length
    q_norm, q_unit, q_inv = normalize(q_raw[0, 0], gain_q)
    k_norm, k_unit, k_inv = normalize(k_raw[0, 0], gain_k)
    v_rows = values[0, 0]
    up_rows = jnp.where(slot_live[:, None], grad_out[0, 0], jnp.zeros((), jnp.bfloat16))
    far_count = head_count // 2
    near_count = head_count - far_count
    ids = jnp.arange(head_count)
    before = (labels[None, :] < labels[:, None]) | (
        (labels[None, :] == labels[:, None]) & (ids[None, :] < ids[:, None])
    )
    back_order = jnp.sum(before.astype(jnp.int32), axis=1)
    head_order = jnp.sum(jnp.where(back_order[None, :] == ids[:, None], ids[None, :], 0), axis=1)
    far_heads = head_order[near_count:]
    wide = far_count * head_size

    def sorted_heads(block):
        shaped = block.reshape(block.shape[:-1] + (head_count, head_size))
        return jnp.take(shaped, head_order, axis=-2)

    def heads_first(block):
        return jnp.transpose(block, (1, 0, 2))

    def to_space(block, extent):
        shaped = block.reshape(frame_count, extent, far_count, head_size)
        return jnp.transpose(shaped, (2, 1, 0, 3)).reshape(
            far_count, extent * frame_count, head_size
        )

    def to_time(block, extent):
        shaped = block.reshape(far_count, extent, frame_count, head_size)
        return jnp.transpose(shaped, (2, 1, 0, 3)).reshape(frame_count, extent, wide)

    def windows(rows):
        blocks = jnp.pad(rows, ((pos_span, pos_span), (0, 0))).reshape(frame_count + 2, pos_span, wide)
        return jnp.concatenate([blocks[:-2], blocks[1:-1], blocks[2:]], axis=1)

    def head_gains(gain_row):
        return jnp.take(gain_row.reshape(head_count, head_size), far_heads, axis=0)

    def spread(near_part, far_part):
        return jnp.take(jnp.concatenate([near_part, far_part], axis=0), back_order, axis=0)

    picked = sorted_heads(jnp.stack([q_norm, k_norm, v_rows, up_rows]))
    units = sorted_heads(jnp.stack([q_unit, k_unit]))[:, :, :near_count]
    far_rows = picked[:, :, near_count:].reshape(4, slot_count, wide)

    outgoing = jnp.concatenate(
        [
            far_rows[0].reshape(frame_count, pos_span, wide),
            far_rows[3].reshape(frame_count, pos_span, wide),
            windows(far_rows[1]),
            windows(far_rows[2]),
        ],
        axis=1,
    )
    sent = lax.all_to_all(outgoing, "ctx", split_axis=0, concat_axis=0, tiled=True)

    near_q, near_k, near_v, near_up = (heads_first(picked[i, :, :near_count]) for i in range(4))
    near_allowed = jnp.broadcast_to(
        slot_live[None, None, :], (near_count, slot_count, slot_count)
    )
    near_out, near_w, near_p = attend(near_q, near_k, near_v, near_allowed)
    near_out = jnp.where(slot_live[None, :, None], near_out, 0.0).astype(jnp.bfloat16)
    near_gq, near_gk, near_gv = attend_back(near_q, near_k, near_v, near_w, near_p, near_up)
    near_term_q = jnp.sum(near_gq * heads_first(units[0]), axis=1)
    near_term_k = jnp.sum(near_gk * heads_first(units[1]), axis=1)

    far_q = to_space(sent[:, :pos_span], pos_span)
    far_up = to_space(sent[:, pos_span : 2 * pos_span], pos_span)
    far_k = to_space(sent[:, 2 * pos_span : 5 * pos_span], 3 * pos_span)
    far_v = to_space(sent[:, 5 * pos_span :], 3 * pos_span)
    q_pos = own_frame * pos_span + jnp.arange(pos_span)
    k_pos = own_frame * pos_span - pos_span + jnp.arange(3 * pos_span)
    q_live = (q_pos[:, None] < lengths[None, :]).reshape(-1)
    k_live = (
        (k_pos[:, None] >= 0) & (k_pos[:, None] < slot_count) & (k_pos[:, None] < lengths[None, :])
    ).reshape(-1)
    pos_gap = jnp.abs(
        jnp.repeat(q_pos, frame_count)[:, None] - jnp.repeat(k_pos, frame_count)[None, :]
    )
    far_bands = jnp.take(bands, far_heads)
    far_allowed = (pos_gap[None] <= far_bands[:, None, None]) & k_live[None, None, :]
    far_out, far_w, far_p = attend(far_q, far_k, far_v, far_allowed)
    far_out = jnp.where(q_live[None, :, None], far_out, 0.0).astype(jnp.bfloat16)
    far_gq, far_gk, far_gv = attend_back(far_q, far_k, far_v, far_w, far_p, far_up)

    far_term_q = jnp.sum(far_gq * far_q.astype(jnp.float32), axis=1) / head_gains(gain_q)
    far_term_k = jnp.sum(far_gk * far_k.astype(jnp.float32), axis=1) / head_gains(gain_k)
    terms = jnp.stack([spread(near_term_q, far_term_q), spread(near_term_k, far_term_k)])
    terms_hi = terms.astype(jnp.bfloat16)
    terms_lo = (terms - terms_hi.astype(jnp.float32)).astype(jnp.bfloat16)
    term_rows = jnp.stack([terms_hi, terms_lo]).reshape(-1, wide)
    term_count = term_rows.shape[0]

    back = lax.all_to_all(
        jnp.concatenate(
            [
                to_time(far_out, pos_span),
                to_time(far_gq, pos_span).astype(jnp.bfloat16),
                to_time(far_gk, 3 * pos_span).astype(jnp.bfloat16),
                to_time(far_gv, 3 * pos_span).astype(jnp.bfloat16),
                jnp.broadcast_to(term_rows[None], (frame_count, term_count, wide)),
            ],
            axis=1,
        ),
        "ctx",
        split_axis=0,
        concat_axis=0,
        tiled=True,
    )
    got_terms = back[:, 8 * pos_span :].reshape(frame_count, 2, 2, head_count, head_size)
    got_terms = got_terms[:, 0].astype(jnp.float32) + got_terms[:, 1].astype(jnp.float32)
    video_count = lax.axis_size("dp")
    video_terms = jnp.sum(got_terms, axis=0)
    all_videos = lax.all_to_all(
        jnp.broadcast_to(video_terms[None], (video_count,) + video_terms.shape),
        "dp",
        split_axis=0,
        concat_axis=0,
        tiled=True,
    )
    totals = jnp.sum(all_videos, axis=0).reshape(2, channels)

    def summed(window_rows):
        parts = window_rows.astype(jnp.float32).reshape(frame_count, 3, pos_span, wide)
        zero = jnp.zeros((1, pos_span, wide), jnp.float32)
        below = jnp.concatenate([zero, parts[:-1, 2]], axis=0)
        above = jnp.concatenate([parts[1:, 0], zero], axis=0)
        return (parts[:, 1] + above + below).reshape(slot_count, wide)

    back_out = back[:, :pos_span].reshape(slot_count, wide)
    back_q = back[:, pos_span : 2 * pos_span].reshape(slot_count, wide)
    back_k = summed(back[:, 2 * pos_span : 5 * pos_span])
    back_v = summed(back[:, 5 * pos_span : 8 * pos_span])

    near_rows = jnp.stack([near_out.astype(jnp.float32), near_gq, near_gk, near_gv])
    near_rows = jnp.transpose(near_rows, (0, 2, 1, 3))
    far_back = jnp.stack(
        [back_out.astype(jnp.float32), back_q.astype(jnp.float32), back_k, back_v]
    ).reshape(4, slot_count, far_count, head_size)
    whole = jnp.take(jnp.concatenate([near_rows, far_back], axis=2), back_order, axis=2)
    whole = whole.reshape(4, slot_count, channels)
    attn_rows = whole[0].astype(jnp.bfloat16)
    grad_qn, grad_kn, grad_vn = whole[1], whole[2], whole[3]
    grad_q_rows = normalize_back(grad_qn, q_unit, q_inv, gain_q).astype(jnp.bfloat16)
    grad_k_rows = normalize_back(grad_kn, k_unit, k_inv, gain_k).astype(jnp.bfloat16)

    def as_shard(row_block):
        return row_block.reshape(1, 1, slot_count, channels)

    return (
        as_shard(attn_rows),
        as_shard(grad_q_rows),
        as_shard(grad_k_rows),
        as_shard(grad_vn.astype(jnp.bfloat16)),
        totals[0],
        totals[1],
    )


def solution(mesh):
    placed = (
        P("dp", "ctx", None, None),
        P("dp", "ctx", None, None),
        P("dp", "ctx", None, None),
        P("dp", "ctx", None, None),
        P(),
        P(),
        P(),
        P(),
        P("dp", None),
    )
    return jax.shard_map(
        body,
        mesh=mesh,
        in_specs=placed,
        out_specs=(
            P("dp", "ctx", None, None),
            P("dp", "ctx", None, None),
            P("dp", "ctx", None, None),
            P("dp", "ctx", None, None),
            P(),
            P(),
        ),
        check_vma=False,
    )
```

```python
import math

import jax
import numpy as np
import jax.numpy as jnp
from jax import lax
from jax.sharding import PartitionSpec as P


def normalize(raw_rows, gain_row):
    full_rows = raw_rows.astype(jnp.float32)
    inverse = lax.rsqrt(jnp.mean(full_rows * full_rows, axis=-1, keepdims=True) + 1e-06)
    unit_rows = full_rows * inverse
    return ((unit_rows * gain_row).astype(jnp.bfloat16), unit_rows, inverse)


def normalize_back(grad_rows, unit_rows, inverse, gain_row):
    scaled = grad_rows * gain_row
    return inverse * (scaled - unit_rows * jnp.mean(scaled * unit_rows, axis=-1, keepdims=True))


def attend(q_rows, k_rows, v_rows, allowed):
    factor = 1.0 / math.sqrt(q_rows.shape[-1])
    scores = jnp.einsum("hqd,hkd->hqk", q_rows, k_rows, preferred_element_type=jnp.float32) * factor
    scores = jnp.where(allowed, scores, -1e30)
    row_peak = jnp.max(scores, axis=-1, keepdims=True)
    exp_terms = jnp.where(allowed, jnp.exp(scores - row_peak), 0.0)
    weights = exp_terms / jnp.sum(exp_terms, axis=-1, keepdims=True)
    prob_bf16 = weights.astype(jnp.bfloat16)
    mixed_rows = jnp.einsum("hqk,hkd->hqd", prob_bf16, v_rows, preferred_element_type=jnp.float32)
    return (mixed_rows, weights, prob_bf16)


def attend_back(q_rows, k_rows, v_rows, weights, prob_bf16, upstream):
    factor = 1.0 / math.sqrt(q_rows.shape[-1])
    grad_v = jnp.einsum("hqk,hqd->hkd", prob_bf16, upstream, preferred_element_type=jnp.float32)
    grad_p = jnp.einsum("hqd,hkd->hqk", upstream, v_rows, preferred_element_type=jnp.float32)
    centre = jnp.sum(weights * grad_p, axis=-1, keepdims=True)
    grad_s = (weights * (grad_p - centre)).astype(jnp.bfloat16)
    grad_q = jnp.einsum("hqk,hkd->hqd", grad_s, k_rows, preferred_element_type=jnp.float32) * factor
    grad_k = jnp.einsum("hqk,hqd->hkd", grad_s, q_rows, preferred_element_type=jnp.float32) * factor
    return (grad_q, grad_k, grad_v)


def body(q_raw, k_raw, values, grad_out, gain_q, gain_k, labels, bands, counts):
    frame_count = lax.axis_size("ctx")
    own_frame = lax.axis_index("ctx")
    head_count = labels.shape[0]
    channels = q_raw.shape[3]
    head_size = channels // head_count
    slot_count = q_raw.shape[2]
    pos_span = slot_count // frame_count
    lengths = counts[0]
    frame_ids = jnp.arange(frame_count)
    own_length = jnp.sum(jnp.where(frame_ids == own_frame, lengths, 0))
    slot_live = jnp.arange(slot_count) < own_length
    q_norm, q_unit, q_inv = normalize(q_raw[0, 0], gain_q)
    k_norm, k_unit, k_inv = normalize(k_raw[0, 0], gain_k)
    v_rows = values[0, 0]
    up_rows = jnp.where(slot_live[:, None], grad_out[0, 0], jnp.zeros((), jnp.bfloat16))
    far_count = head_count // 2
    near_count = head_count - far_count
    ids = jnp.arange(head_count)
    before = (labels[None, :] < labels[:, None]) | (
        (labels[None, :] == labels[:, None]) & (ids[None, :] < ids[:, None])
    )
    back_order = jnp.sum(before.astype(jnp.int32), axis=1)
    head_order = jnp.sum(jnp.where(back_order[None, :] == ids[:, None], ids[None, :], 0), axis=1)
    far_heads = head_order[near_count:]
    wide = far_count * head_size

    def sorted_heads(block):
        shaped = block.reshape(block.shape[:-1] + (head_count, head_size))
        return jnp.take(shaped, head_order, axis=-2)

    def heads_first(block):
        return jnp.transpose(block, (1, 0, 2))

    def to_space(block, extent):
        shaped = block.reshape(frame_count, extent, far_count, head_size)
        return jnp.transpose(shaped, (2, 1, 0, 3)).reshape(
            far_count, extent * frame_count, head_size
        )

    def to_time(block, extent):
        shaped = block.reshape(far_count, extent, frame_count, head_size)
        return jnp.transpose(shaped, (2, 1, 0, 3)).reshape(frame_count, extent, wide)

    def to_time_pair(block, extent):
        shaped = block.reshape(2, far_count, extent, frame_count, head_size)
        return jnp.transpose(shaped, (3, 0, 2, 1, 4)).reshape(frame_count, 2 * extent, wide)

    def head_gains(gain_row):
        return jnp.take(gain_row.reshape(head_count, head_size), far_heads, axis=0)

    def spread(near_part, far_part):
        return jnp.take(jnp.concatenate([near_part, far_part], axis=0), back_order, axis=0)

    picked = sorted_heads(jnp.stack([q_norm, k_norm, v_rows, up_rows]))
    units = sorted_heads(jnp.stack([q_unit, k_unit]))[:, :, :near_count]
    far_rows = picked[:, :, near_count:].reshape(4, slot_count, wide)

    row_count = 4 * slot_count
    table = np.full((frame_count, 8 * pos_span), row_count, np.int32)
    for dest in range(frame_count):
        for j in range(pos_span):
            table[dest, j] = dest * pos_span + j
            table[dest, pos_span + j] = 3 * slot_count + dest * pos_span + j
        for j in range(3 * pos_span):
            pos = dest * pos_span - pos_span + j
            if 0 <= pos < slot_count:
                table[dest, 2 * pos_span + j] = slot_count + pos
                table[dest, 5 * pos_span + j] = 2 * slot_count + pos
    outgoing = jnp.take(far_rows.reshape(row_count, wide), table, axis=0, mode="fill", fill_value=0)
    sent = lax.all_to_all(outgoing, "ctx", split_axis=0, concat_axis=0, tiled=True)

    near_q, near_k, near_v, near_up = (heads_first(picked[i, :, :near_count]) for i in range(4))
    near_allowed = jnp.broadcast_to(
        slot_live[None, None, :], (near_count, slot_count, slot_count)
    )
    near_out, near_w, near_p = attend(near_q, near_k, near_v, near_allowed)
    near_out = jnp.where(slot_live[None, :, None], near_out, 0.0).astype(jnp.bfloat16)
    near_gq, near_gk, near_gv = attend_back(near_q, near_k, near_v, near_w, near_p, near_up)
    near_term_q = jnp.sum(near_gq * heads_first(units[0]), axis=1)
    near_term_k = jnp.sum(near_gk * heads_first(units[1]), axis=1)

    far_q = to_space(sent[:, :pos_span], pos_span)
    far_up = to_space(sent[:, pos_span : 2 * pos_span], pos_span)
    far_k = to_space(sent[:, 2 * pos_span : 5 * pos_span], 3 * pos_span)
    far_v = to_space(sent[:, 5 * pos_span :], 3 * pos_span)
    q_pos = own_frame * pos_span + jnp.arange(pos_span)
    k_pos = own_frame * pos_span - pos_span + jnp.arange(3 * pos_span)
    q_live = (q_pos[:, None] < lengths[None, :]).reshape(-1)
    k_live = (
        (k_pos[:, None] >= 0) & (k_pos[:, None] < slot_count) & (k_pos[:, None] < lengths[None, :])
    ).reshape(-1)
    pos_gap = jnp.abs(
        jnp.repeat(q_pos, frame_count)[:, None] - jnp.repeat(k_pos, frame_count)[None, :]
    )
    far_bands = jnp.take(bands, far_heads)
    far_allowed = (pos_gap[None] <= far_bands[:, None, None]) & k_live[None, None, :]
    far_out, far_w, far_p = attend(far_q, far_k, far_v, far_allowed)
    far_out = jnp.where(q_live[None, :, None], far_out, 0.0).astype(jnp.bfloat16)
    far_gq, far_gk, far_gv = attend_back(far_q, far_k, far_v, far_w, far_p, far_up)

    far_term_q = jnp.sum(far_gq * far_q.astype(jnp.float32), axis=1) / head_gains(gain_q)
    far_term_k = jnp.sum(far_gk * far_k.astype(jnp.float32), axis=1) / head_gains(gain_k)
    terms = jnp.stack([spread(near_term_q, far_term_q), spread(near_term_k, far_term_k)])
    terms_hi = terms.astype(jnp.bfloat16)
    terms_lo = (terms - terms_hi.astype(jnp.float32)).astype(jnp.bfloat16)
    term_rows = jnp.stack([terms_hi, terms_lo]).reshape(-1, wide)
    term_count = term_rows.shape[0]

    back = lax.all_to_all(
        jnp.concatenate(
            [
                to_time_pair(jnp.stack([far_out, far_gq.astype(jnp.bfloat16)]), pos_span),
                to_time_pair(jnp.stack([far_gk, far_gv]).astype(jnp.bfloat16), 3 * pos_span),
                jnp.broadcast_to(term_rows[None], (frame_count, term_count, wide)),
            ],
            axis=1,
        ),
        "ctx",
        split_axis=0,
        concat_axis=0,
        tiled=True,
    )
    got_terms = back[:, 8 * pos_span :].reshape(frame_count, 2, 2, head_count, head_size)
    got_terms = got_terms[:, 0].astype(jnp.float32) + got_terms[:, 1].astype(jnp.float32)
    video_count = lax.axis_size("dp")
    video_terms = jnp.sum(got_terms, axis=0)
    all_videos = lax.all_to_all(
        jnp.broadcast_to(video_terms[None], (video_count,) + video_terms.shape),
        "dp",
        split_axis=0,
        concat_axis=0,
        tiled=True,
    )
    totals = jnp.sum(all_videos, axis=0).reshape(2, channels)

    def summed(window_rows):
        parts = window_rows.astype(jnp.float32).reshape(frame_count, 3, pos_span, wide)
        zero = jnp.zeros((1, pos_span, wide), jnp.float32)
        below = jnp.concatenate([zero, parts[:-1, 2]], axis=0)
        above = jnp.concatenate([parts[1:, 0], zero], axis=0)
        return (parts[:, 1] + above + below).reshape(slot_count, wide)

    back_out = back[:, :pos_span].reshape(slot_count, wide)
    back_q = back[:, pos_span : 2 * pos_span].reshape(slot_count, wide)
    back_k = summed(back[:, 2 * pos_span : 5 * pos_span])
    back_v = summed(back[:, 5 * pos_span : 8 * pos_span])

    near_rows = jnp.stack([near_out.astype(jnp.float32), near_gq, near_gk, near_gv])
    near_rows = jnp.transpose(near_rows, (0, 2, 1, 3))
    far_back = jnp.stack(
        [back_out.astype(jnp.float32), back_q.astype(jnp.float32), back_k, back_v]
    ).reshape(4, slot_count, far_count, head_size)
    whole = jnp.take(jnp.concatenate([near_rows, far_back], axis=2), back_order, axis=2)
    whole = whole.reshape(4, slot_count, channels)
    attn_rows = whole[0].astype(jnp.bfloat16)
    grad_qn, grad_kn, grad_vn = whole[1], whole[2], whole[3]
    grad_q_rows = normalize_back(grad_qn, q_unit, q_inv, gain_q).astype(jnp.bfloat16)
    grad_k_rows = normalize_back(grad_kn, k_unit, k_inv, gain_k).astype(jnp.bfloat16)

    def as_shard(row_block):
        return row_block.reshape(1, 1, slot_count, channels)

    return (
        as_shard(attn_rows),
        as_shard(grad_q_rows),
        as_shard(grad_k_rows),
        as_shard(grad_vn.astype(jnp.bfloat16)),
        totals[0],
        totals[1],
    )


def solution(mesh):
    placed = (
        P("dp", "ctx", None, None),
        P("dp", "ctx", None, None),
        P("dp", "ctx", None, None),
        P("dp", "ctx", None, None),
        P(),
        P(),
        P(),
        P(),
        P("dp", None),
    )
    return jax.shard_map(
        body,
        mesh=mesh,
        in_specs=placed,
        out_specs=(
            P("dp", "ctx", None, None),
            P("dp", "ctx", None, None),
            P("dp", "ctx", None, None),
            P("dp", "ctx", None, None),
            P(),
            P(),
        ),
        check_vma=False,
    )
```

```python
import math

import jax
import numpy as np
import jax.numpy as jnp
from jax import lax
from jax.sharding import PartitionSpec as P


def normalize(raw_rows, gain_row):
    full_rows = raw_rows.astype(jnp.float32)
    inverse = lax.rsqrt(jnp.mean(full_rows * full_rows, axis=-1, keepdims=True) + 1e-06)
    unit_rows = full_rows * inverse
    return ((unit_rows * gain_row).astype(jnp.bfloat16), unit_rows, inverse)


def normalize_back(grad_rows, unit_rows, inverse, gain_row):
    scaled = grad_rows * gain_row
    return inverse * (scaled - unit_rows * jnp.mean(scaled * unit_rows, axis=-1, keepdims=True))


def attend(q_rows, k_rows, v_rows, allowed):
    factor = 1.0 / math.sqrt(q_rows.shape[-1])
    scores = jnp.einsum("hqd,hkd->hqk", q_rows, k_rows, preferred_element_type=jnp.float32) * factor
    scores = jnp.where(allowed, scores, -1e30)
    row_peak = jnp.max(scores, axis=-1, keepdims=True)
    exp_terms = jnp.where(allowed, jnp.exp(scores - row_peak), 0.0)
    weights = exp_terms / jnp.sum(exp_terms, axis=-1, keepdims=True)
    prob_bf16 = weights.astype(jnp.bfloat16)
    mixed_rows = jnp.einsum("hqk,hkd->hqd", prob_bf16, v_rows, preferred_element_type=jnp.float32)
    return (mixed_rows, weights, prob_bf16)


def attend_back(q_rows, k_rows, v_rows, weights, prob_bf16, upstream):
    factor = 1.0 / math.sqrt(q_rows.shape[-1])
    grad_v = jnp.einsum("hqk,hqd->hkd", prob_bf16, upstream, preferred_element_type=jnp.float32)
    grad_p = jnp.einsum("hqd,hkd->hqk", upstream, v_rows, preferred_element_type=jnp.float32)
    centre = jnp.sum(weights * grad_p, axis=-1, keepdims=True)
    grad_s = (weights * (grad_p - centre)).astype(jnp.bfloat16)
    grad_q = jnp.einsum("hqk,hkd->hqd", grad_s, k_rows, preferred_element_type=jnp.float32) * factor
    grad_k = jnp.einsum("hqk,hqd->hkd", grad_s, q_rows, preferred_element_type=jnp.float32) * factor
    return (grad_q, grad_k, grad_v)


def body(q_raw, k_raw, values, grad_out, gain_q, gain_k, labels, bands, counts):
    frame_count = lax.axis_size("ctx")
    own_frame = lax.axis_index("ctx")
    head_count = labels.shape[0]
    channels = q_raw.shape[3]
    head_size = channels // head_count
    slot_count = q_raw.shape[2]
    pos_span = slot_count // frame_count
    lengths = counts[0]
    frame_ids = jnp.arange(frame_count)
    own_length = jnp.sum(jnp.where(frame_ids == own_frame, lengths, 0))
    slot_live = jnp.arange(slot_count) < own_length
    q_norm, q_unit, q_inv = normalize(q_raw[0, 0], gain_q)
    k_norm, k_unit, k_inv = normalize(k_raw[0, 0], gain_k)
    v_rows = values[0, 0]
    up_rows = jnp.where(slot_live[:, None], grad_out[0, 0], jnp.zeros((), jnp.bfloat16))
    far_count = head_count // 2
    near_count = head_count - far_count
    ids = jnp.arange(head_count)
    before = (labels[None, :] < labels[:, None]) | (
        (labels[None, :] == labels[:, None]) & (ids[None, :] < ids[:, None])
    )
    back_order = jnp.sum(before.astype(jnp.int32), axis=1)
    head_order = jnp.sum(jnp.where(back_order[None, :] == ids[:, None], ids[None, :], 0), axis=1)
    far_heads = head_order[near_count:]
    wide = far_count * head_size

    def sorted_heads(block):
        shaped = block.reshape(block.shape[:-1] + (head_count, head_size))
        return jnp.take(shaped, head_order, axis=-2)

    def heads_first(block):
        return jnp.transpose(block, (1, 0, 2))

    def to_space(block, extent):
        shaped = block.reshape(frame_count, extent, far_count, head_size)
        return jnp.transpose(shaped, (2, 1, 0, 3)).reshape(
            far_count, extent * frame_count, head_size
        )

    def to_time(block, extent):
        shaped = block.reshape(far_count, extent, frame_count, head_size)
        return jnp.transpose(shaped, (2, 1, 0, 3)).reshape(frame_count, extent, wide)

    def to_time_pair(block, extent):
        shaped = block.reshape(2, far_count, extent, frame_count, head_size)
        return jnp.transpose(shaped, (3, 0, 2, 1, 4)).reshape(frame_count, 2 * extent, wide)

    def head_gains(gain_row):
        return jnp.take(gain_row.reshape(head_count, head_size), far_heads, axis=0)

    def spread(near_part, far_part):
        return jnp.take(jnp.concatenate([near_part, far_part], axis=0), back_order, axis=0)

    picked = sorted_heads(jnp.stack([q_norm, k_norm, v_rows, up_rows]))
    units = sorted_heads(jnp.stack([q_unit, k_unit]))[:, :, :near_count]
    far_rows = picked[:, :, near_count:].reshape(4, slot_count, wide)

    row_count = 4 * slot_count
    table = np.full((frame_count * 8 * pos_span,), row_count, np.int32)
    for dest in range(frame_count):
        base = dest * 8 * pos_span
        for j in range(pos_span):
            table[base + j] = dest * pos_span + j
            table[base + pos_span + j] = 3 * slot_count + dest * pos_span + j
        for j in range(3 * pos_span):
            pos = dest * pos_span - pos_span + j
            if 0 <= pos < slot_count:
                table[base + 2 * pos_span + j] = slot_count + pos
                table[base + 5 * pos_span + j] = 2 * slot_count + pos
    chooser = (jnp.asarray(table)[:, None] == jnp.arange(row_count)[None, :]).astype(jnp.bfloat16)
    outgoing = jnp.dot(chooser, far_rows.reshape(row_count, wide), preferred_element_type=jnp.float32)
    outgoing = outgoing.astype(jnp.bfloat16).reshape(frame_count, 8 * pos_span, wide)
    sent = lax.all_to_all(outgoing, "ctx", split_axis=0, concat_axis=0, tiled=True)

    near_q, near_k, near_v, near_up = (heads_first(picked[i, :, :near_count]) for i in range(4))
    near_allowed = jnp.broadcast_to(
        slot_live[None, None, :], (near_count, slot_count, slot_count)
    )
    near_out, near_w, near_p = attend(near_q, near_k, near_v, near_allowed)
    near_out = jnp.where(slot_live[None, :, None], near_out, 0.0).astype(jnp.bfloat16)
    near_gq, near_gk, near_gv = attend_back(near_q, near_k, near_v, near_w, near_p, near_up)
    near_term_q = jnp.sum(near_gq * heads_first(units[0]), axis=1)
    near_term_k = jnp.sum(near_gk * heads_first(units[1]), axis=1)

    far_q = to_space(sent[:, :pos_span], pos_span)
    far_up = to_space(sent[:, pos_span : 2 * pos_span], pos_span)
    far_k = to_space(sent[:, 2 * pos_span : 5 * pos_span], 3 * pos_span)
    far_v = to_space(sent[:, 5 * pos_span :], 3 * pos_span)
    q_pos = own_frame * pos_span + jnp.arange(pos_span)
    k_pos = own_frame * pos_span - pos_span + jnp.arange(3 * pos_span)
    q_live = (q_pos[:, None] < lengths[None, :]).reshape(-1)
    k_live = (
        (k_pos[:, None] >= 0) & (k_pos[:, None] < slot_count) & (k_pos[:, None] < lengths[None, :])
    ).reshape(-1)
    pos_gap = jnp.abs(
        jnp.repeat(q_pos, frame_count)[:, None] - jnp.repeat(k_pos, frame_count)[None, :]
    )
    far_bands = jnp.take(bands, far_heads)
    far_allowed = (pos_gap[None] <= far_bands[:, None, None]) & k_live[None, None, :]
    far_out, far_w, far_p = attend(far_q, far_k, far_v, far_allowed)
    far_out = jnp.where(q_live[None, :, None], far_out, 0.0).astype(jnp.bfloat16)
    far_gq, far_gk, far_gv = attend_back(far_q, far_k, far_v, far_w, far_p, far_up)

    far_term_q = jnp.sum(far_gq * far_q.astype(jnp.float32), axis=1) / head_gains(gain_q)
    far_term_k = jnp.sum(far_gk * far_k.astype(jnp.float32), axis=1) / head_gains(gain_k)
    terms = jnp.stack([spread(near_term_q, far_term_q), spread(near_term_k, far_term_k)])
    terms_hi = terms.astype(jnp.bfloat16)
    terms_lo = (terms - terms_hi.astype(jnp.float32)).astype(jnp.bfloat16)
    term_rows = jnp.stack([terms_hi, terms_lo]).reshape(-1, wide)
    term_count = term_rows.shape[0]

    back = lax.all_to_all(
        jnp.concatenate(
            [
                to_time_pair(jnp.stack([far_out, far_gq.astype(jnp.bfloat16)]), pos_span),
                to_time_pair(jnp.stack([far_gk, far_gv]).astype(jnp.bfloat16), 3 * pos_span),
                jnp.broadcast_to(term_rows[None], (frame_count, term_count, wide)),
            ],
            axis=1,
        ),
        "ctx",
        split_axis=0,
        concat_axis=0,
        tiled=True,
    )
    got_terms = back[:, 8 * pos_span :].reshape(frame_count, 2, 2, head_count, head_size)
    got_terms = got_terms[:, 0].astype(jnp.float32) + got_terms[:, 1].astype(jnp.float32)
    video_count = lax.axis_size("dp")
    video_terms = jnp.sum(got_terms, axis=0)
    all_videos = lax.all_to_all(
        jnp.broadcast_to(video_terms[None], (video_count,) + video_terms.shape),
        "dp",
        split_axis=0,
        concat_axis=0,
        tiled=True,
    )
    totals = jnp.sum(all_videos, axis=0).reshape(2, channels)

    def summed(window_rows):
        parts = window_rows.astype(jnp.float32).reshape(frame_count, 3, pos_span, wide)
        zero = jnp.zeros((1, pos_span, wide), jnp.float32)
        below = jnp.concatenate([zero, parts[:-1, 2]], axis=0)
        above = jnp.concatenate([parts[1:, 0], zero], axis=0)
        return (parts[:, 1] + above + below).reshape(slot_count, wide)

    back_out = back[:, :pos_span].reshape(slot_count, wide)
    back_q = back[:, pos_span : 2 * pos_span].reshape(slot_count, wide)
    back_k = summed(back[:, 2 * pos_span : 5 * pos_span])
    back_v = summed(back[:, 5 * pos_span : 8 * pos_span])

    near_rows = jnp.stack([near_out.astype(jnp.float32), near_gq, near_gk, near_gv])
    near_rows = jnp.transpose(near_rows, (0, 2, 1, 3))
    far_back = jnp.stack(
        [back_out.astype(jnp.float32), back_q.astype(jnp.float32), back_k, back_v]
    ).reshape(4, slot_count, far_count, head_size)
    whole = jnp.take(jnp.concatenate([near_rows, far_back], axis=2), back_order, axis=2)
    whole = whole.reshape(4, slot_count, channels)
    attn_rows = whole[0].astype(jnp.bfloat16)
    grad_qn, grad_kn, grad_vn = whole[1], whole[2], whole[3]
    grad_q_rows = normalize_back(grad_qn, q_unit, q_inv, gain_q).astype(jnp.bfloat16)
    grad_k_rows = normalize_back(grad_kn, k_unit, k_inv, gain_k).astype(jnp.bfloat16)

    def as_shard(row_block):
        return row_block.reshape(1, 1, slot_count, channels)

    return (
        as_shard(attn_rows),
        as_shard(grad_q_rows),
        as_shard(grad_k_rows),
        as_shard(grad_vn.astype(jnp.bfloat16)),
        totals[0],
        totals[1],
    )


def solution(mesh):
    placed = (
        P("dp", "ctx", None, None),
        P("dp", "ctx", None, None),
        P("dp", "ctx", None, None),
        P("dp", "ctx", None, None),
        P(),
        P(),
        P(),
        P(),
        P("dp", None),
    )
    return jax.shard_map(
        body,
        mesh=mesh,
        in_specs=placed,
        out_specs=(
            P("dp", "ctx", None, None),
            P("dp", "ctx", None, None),
            P("dp", "ctx", None, None),
            P("dp", "ctx", None, None),
            P(),
            P(),
        ),
        check_vma=False,
    )
```

```python
import math

import jax
import numpy as np
import jax.numpy as jnp
from jax import lax
from jax.experimental import pallas as pl
from jax.experimental.pallas import tpu as pltpu
from jax.sharding import PartitionSpec as P


def normalize(raw_rows, gain_row):
    full_rows = raw_rows.astype(jnp.float32)
    inverse = lax.rsqrt(jnp.mean(full_rows * full_rows, axis=-1, keepdims=True) + 1e-06)
    unit_rows = full_rows * inverse
    return ((unit_rows * gain_row).astype(jnp.bfloat16), unit_rows, inverse)


def normalize_back(grad_rows, unit_rows, inverse, gain_row):
    scaled = grad_rows * gain_row
    return inverse * (scaled - unit_rows * jnp.mean(scaled * unit_rows, axis=-1, keepdims=True))


def attend(q_rows, k_rows, v_rows, allowed):
    factor = 1.0 / math.sqrt(q_rows.shape[-1])
    scores = jnp.einsum("hqd,hkd->hqk", q_rows, k_rows, preferred_element_type=jnp.float32) * factor
    scores = jnp.where(allowed, scores, -1e30)
    row_peak = jnp.max(scores, axis=-1, keepdims=True)
    exp_terms = jnp.where(allowed, jnp.exp(scores - row_peak), 0.0)
    weights = exp_terms / jnp.sum(exp_terms, axis=-1, keepdims=True)
    prob_bf16 = weights.astype(jnp.bfloat16)
    mixed_rows = jnp.einsum("hqk,hkd->hqd", prob_bf16, v_rows, preferred_element_type=jnp.float32)
    return (mixed_rows, weights, prob_bf16)


def attend_back(q_rows, k_rows, v_rows, weights, prob_bf16, upstream):
    factor = 1.0 / math.sqrt(q_rows.shape[-1])
    grad_v = jnp.einsum("hqk,hqd->hkd", prob_bf16, upstream, preferred_element_type=jnp.float32)
    grad_p = jnp.einsum("hqd,hkd->hqk", upstream, v_rows, preferred_element_type=jnp.float32)
    centre = jnp.sum(weights * grad_p, axis=-1, keepdims=True)
    grad_s = (weights * (grad_p - centre)).astype(jnp.bfloat16)
    grad_q = jnp.einsum("hqk,hkd->hqd", grad_s, k_rows, preferred_element_type=jnp.float32) * factor
    grad_k = jnp.einsum("hqk,hqd->hkd", grad_s, q_rows, preferred_element_type=jnp.float32) * factor
    return (grad_q, grad_k, grad_v)


def merge_kernel(
    order_ref,
    back_ref,
    near_out_ref,
    near_q_ref,
    near_k_ref,
    near_v_ref,
    q_unit_ref,
    q_inv_ref,
    k_unit_ref,
    k_inv_ref,
    gain_q_ref,
    gain_k_ref,
    attn_ref,
    gq_ref,
    gk_ref,
    gv_ref,
):
    blocks, _, wide = back_ref.shape
    head_count = order_ref.shape[0]
    far_count, _, head_size = near_q_ref.shape
    span = near_q_ref.shape[1] // blocks
    rows = [back_ref[c].astype(jnp.float32) for c in range(blocks)]

    def plain(first):
        return jnp.concatenate([rows[c][first : first + span] for c in range(blocks)], axis=0)

    def summed(first):
        parts = []
        for c in range(blocks):
            part = rows[c][first + span : first + 2 * span]
            if c + 1 < blocks:
                part = part + rows[c + 1][first : first + span]
            if c >= 1:
                part = part + rows[c - 1][first + 2 * span : first + 3 * span]
            parts.append(part)
        return jnp.concatenate(parts, axis=0)

    far = [plain(0), plain(span), summed(2 * span), summed(5 * span)]
    near = [
        [ref[i].astype(jnp.float32) for i in range(far_count)]
        for ref in (near_out_ref, near_q_ref, near_k_ref, near_v_ref)
    ]
    whole = [[], [], [], []]
    for h in range(head_count):
        place = order_ref[h]
        for t in range(4):
            tile = far[t][:, (far_count - 1) * head_size :]
            for i in range(far_count - 2, -1, -1):
                tile = jnp.where(place == far_count + i, far[t][:, i * head_size : (i + 1) * head_size], tile)
            for i in range(far_count - 1, -1, -1):
                tile = jnp.where(place == i, near[t][i], tile)
            whole[t].append(tile)
    whole = [jnp.concatenate(parts, axis=1) for parts in whole]
    attn_ref[...] = whole[0].astype(attn_ref.dtype)
    gv_ref[...] = whole[3].astype(gv_ref.dtype)
    for grad_rows, unit_ref, inv_ref, gain_ref, out_ref in (
        (whole[1], q_unit_ref, q_inv_ref, gain_q_ref, gq_ref),
        (whole[2], k_unit_ref, k_inv_ref, gain_k_ref, gk_ref),
    ):
        unit_rows = unit_ref[...]
        scaled = grad_rows * gain_ref[...]
        centre = jnp.mean(scaled * unit_rows, axis=-1, keepdims=True)
        out_ref[...] = (inv_ref[...] * (scaled - unit_rows * centre)).astype(out_ref.dtype)


def body(q_raw, k_raw, values, grad_out, gain_q, gain_k, labels, bands, counts):
    frame_count = lax.axis_size("ctx")
    own_frame = lax.axis_index("ctx")
    head_count = labels.shape[0]
    channels = q_raw.shape[3]
    head_size = channels // head_count
    slot_count = q_raw.shape[2]
    pos_span = slot_count // frame_count
    lengths = counts[0]
    frame_ids = jnp.arange(frame_count)
    own_length = jnp.sum(jnp.where(frame_ids == own_frame, lengths, 0))
    slot_live = jnp.arange(slot_count) < own_length
    q_norm, q_unit, q_inv = normalize(q_raw[0, 0], gain_q)
    k_norm, k_unit, k_inv = normalize(k_raw[0, 0], gain_k)
    v_rows = values[0, 0]
    up_rows = jnp.where(slot_live[:, None], grad_out[0, 0], jnp.zeros((), jnp.bfloat16))
    far_count = head_count // 2
    near_count = head_count - far_count
    ids = jnp.arange(head_count)
    before = (labels[None, :] < labels[:, None]) | (
        (labels[None, :] == labels[:, None]) & (ids[None, :] < ids[:, None])
    )
    back_order = jnp.sum(before.astype(jnp.int32), axis=1)
    head_order = jnp.sum(jnp.where(back_order[None, :] == ids[:, None], ids[None, :], 0), axis=1)
    far_heads = head_order[near_count:]
    wide = far_count * head_size

    def sorted_heads(block):
        shaped = block.reshape(block.shape[:-1] + (head_count, head_size))
        return jnp.take(shaped, head_order, axis=-2)

    def heads_first(block):
        return jnp.transpose(block, (1, 0, 2))

    def to_space(block, extent):
        shaped = block.reshape(frame_count, extent, far_count, head_size)
        return jnp.transpose(shaped, (2, 1, 0, 3)).reshape(
            far_count, extent * frame_count, head_size
        )

    def to_time(block, extent):
        shaped = block.reshape(far_count, extent, frame_count, head_size)
        return jnp.transpose(shaped, (2, 1, 0, 3)).reshape(frame_count, extent, wide)

    def to_time_pair(block, extent):
        shaped = block.reshape(2, far_count, extent, frame_count, head_size)
        return jnp.transpose(shaped, (3, 0, 2, 1, 4)).reshape(frame_count, 2 * extent, wide)

    def head_gains(gain_row):
        return jnp.take(gain_row.reshape(head_count, head_size), far_heads, axis=0)

    def spread(near_part, far_part):
        return jnp.take(jnp.concatenate([near_part, far_part], axis=0), back_order, axis=0)

    picked = sorted_heads(jnp.stack([q_norm, k_norm, v_rows, up_rows]))
    units = sorted_heads(jnp.stack([q_unit, k_unit]))[:, :, :near_count]
    far_rows = picked[:, :, near_count:].reshape(4, slot_count, wide)

    row_count = 4 * slot_count
    table = np.full((frame_count * 8 * pos_span,), row_count, np.int32)
    for dest in range(frame_count):
        base = dest * 8 * pos_span
        for j in range(pos_span):
            table[base + j] = dest * pos_span + j
            table[base + pos_span + j] = 3 * slot_count + dest * pos_span + j
        for j in range(3 * pos_span):
            pos = dest * pos_span - pos_span + j
            if 0 <= pos < slot_count:
                table[base + 2 * pos_span + j] = slot_count + pos
                table[base + 5 * pos_span + j] = 2 * slot_count + pos
    chooser = (jnp.asarray(table)[:, None] == jnp.arange(row_count)[None, :]).astype(jnp.bfloat16)
    outgoing = jnp.dot(chooser, far_rows.reshape(row_count, wide), preferred_element_type=jnp.float32)
    outgoing = outgoing.astype(jnp.bfloat16).reshape(frame_count, 8 * pos_span, wide)
    sent = lax.all_to_all(outgoing, "ctx", split_axis=0, concat_axis=0, tiled=True)

    near_q, near_k, near_v, near_up = (heads_first(picked[i, :, :near_count]) for i in range(4))
    near_allowed = jnp.broadcast_to(
        slot_live[None, None, :], (near_count, slot_count, slot_count)
    )
    near_out, near_w, near_p = attend(near_q, near_k, near_v, near_allowed)
    near_out = jnp.where(slot_live[None, :, None], near_out, 0.0).astype(jnp.bfloat16)
    near_gq, near_gk, near_gv = attend_back(near_q, near_k, near_v, near_w, near_p, near_up)
    near_term_q = jnp.sum(near_gq * heads_first(units[0]), axis=1)
    near_term_k = jnp.sum(near_gk * heads_first(units[1]), axis=1)

    far_q = to_space(sent[:, :pos_span], pos_span)
    far_up = to_space(sent[:, pos_span : 2 * pos_span], pos_span)
    far_k = to_space(sent[:, 2 * pos_span : 5 * pos_span], 3 * pos_span)
    far_v = to_space(sent[:, 5 * pos_span :], 3 * pos_span)
    q_pos = own_frame * pos_span + jnp.arange(pos_span)
    k_pos = own_frame * pos_span - pos_span + jnp.arange(3 * pos_span)
    q_live = (q_pos[:, None] < lengths[None, :]).reshape(-1)
    k_live = (
        (k_pos[:, None] >= 0) & (k_pos[:, None] < slot_count) & (k_pos[:, None] < lengths[None, :])
    ).reshape(-1)
    pos_gap = jnp.abs(
        jnp.repeat(q_pos, frame_count)[:, None] - jnp.repeat(k_pos, frame_count)[None, :]
    )
    far_bands = jnp.take(bands, far_heads)
    far_allowed = (pos_gap[None] <= far_bands[:, None, None]) & k_live[None, None, :]
    far_out, far_w, far_p = attend(far_q, far_k, far_v, far_allowed)
    far_out = jnp.where(q_live[None, :, None], far_out, 0.0).astype(jnp.bfloat16)
    far_gq, far_gk, far_gv = attend_back(far_q, far_k, far_v, far_w, far_p, far_up)

    far_term_q = jnp.sum(far_gq * far_q.astype(jnp.float32), axis=1) / head_gains(gain_q)
    far_term_k = jnp.sum(far_gk * far_k.astype(jnp.float32), axis=1) / head_gains(gain_k)
    terms = jnp.stack([spread(near_term_q, far_term_q), spread(near_term_k, far_term_k)])
    terms_hi = terms.astype(jnp.bfloat16)
    terms_lo = (terms - terms_hi.astype(jnp.float32)).astype(jnp.bfloat16)
    term_rows = jnp.stack([terms_hi, terms_lo]).reshape(-1, wide)
    term_count = term_rows.shape[0]

    back = lax.all_to_all(
        jnp.concatenate(
            [
                to_time_pair(jnp.stack([far_out, far_gq.astype(jnp.bfloat16)]), pos_span),
                to_time_pair(jnp.stack([far_gk, far_gv]).astype(jnp.bfloat16), 3 * pos_span),
                jnp.broadcast_to(term_rows[None], (frame_count, term_count, wide)),
            ],
            axis=1,
        ),
        "ctx",
        split_axis=0,
        concat_axis=0,
        tiled=True,
    )
    got_terms = back[:, 8 * pos_span :].reshape(frame_count, 2, 2, head_count, head_size)
    got_terms = got_terms[:, 0].astype(jnp.float32) + got_terms[:, 1].astype(jnp.float32)
    video_count = lax.axis_size("dp")
    video_terms = jnp.sum(got_terms, axis=0)
    all_videos = lax.all_to_all(
        jnp.broadcast_to(video_terms[None], (video_count,) + video_terms.shape),
        "dp",
        split_axis=0,
        concat_axis=0,
        tiled=True,
    )
    totals = jnp.sum(all_videos, axis=0).reshape(2, channels)

    slot_bytes = slot_count * channels
    merge = pl.pallas_call(
        merge_kernel,
        out_shape=[jax.ShapeDtypeStruct((slot_count, channels), jnp.bfloat16)] * 4,
        in_specs=[pl.BlockSpec(memory_space=pltpu.SMEM)] + [pl.BlockSpec(memory_space=pltpu.VMEM)] * 11,
        out_specs=[pl.BlockSpec(memory_space=pltpu.VMEM)] * 4,
        cost_estimate=pl.CostEstimate(
            flops=40 * slot_bytes, bytes_accessed=30 * slot_bytes, transcendentals=0
        ),
    )
    attn_rows, grad_q_rows, grad_k_rows, grad_v_rows = merge(
        back_order,
        back,
        near_out,
        near_gq,
        near_gk,
        near_gv,
        q_unit,
        q_inv,
        k_unit,
        k_inv,
        gain_q.reshape(1, channels),
        gain_k.reshape(1, channels),
    )

    def as_shard(row_block):
        return row_block.reshape(1, 1, slot_count, channels)

    return (
        as_shard(attn_rows),
        as_shard(grad_q_rows),
        as_shard(grad_k_rows),
        as_shard(grad_v_rows),
        totals[0],
        totals[1],
    )


def solution(mesh):
    placed = (
        P("dp", "ctx", None, None),
        P("dp", "ctx", None, None),
        P("dp", "ctx", None, None),
        P("dp", "ctx", None, None),
        P(),
        P(),
        P(),
        P(),
        P("dp", None),
    )
    return jax.shard_map(
        body,
        mesh=mesh,
        in_specs=placed,
        out_specs=(
            P("dp", "ctx", None, None),
            P("dp", "ctx", None, None),
            P("dp", "ctx", None, None),
            P("dp", "ctx", None, None),
            P(),
            P(),
        ),
        check_vma=False,
    )
```

```python
import math

import jax
import jax.numpy as jnp
from jax import lax
from jax.experimental import pallas as pl
from jax.experimental.pallas import tpu as pltpu
from jax.sharding import PartitionSpec as P


def normalize(raw_rows, gain_row):
    full_rows = raw_rows.astype(jnp.float32)
    inverse = lax.rsqrt(jnp.mean(full_rows * full_rows, axis=-1, keepdims=True) + 1e-06)
    unit_rows = full_rows * inverse
    return ((unit_rows * gain_row).astype(jnp.bfloat16), unit_rows, inverse)


def normalize_back(grad_rows, unit_rows, inverse, gain_row):
    scaled = grad_rows * gain_row
    return inverse * (scaled - unit_rows * jnp.mean(scaled * unit_rows, axis=-1, keepdims=True))


def attend(q_rows, k_rows, v_rows, allowed):
    factor = 1.0 / math.sqrt(q_rows.shape[-1])
    scores = jnp.einsum("hqd,hkd->hqk", q_rows, k_rows, preferred_element_type=jnp.float32) * factor
    scores = jnp.where(allowed, scores, -1e30)
    row_peak = jnp.max(scores, axis=-1, keepdims=True)
    exp_terms = jnp.where(allowed, jnp.exp(scores - row_peak), 0.0)
    weights = exp_terms / jnp.sum(exp_terms, axis=-1, keepdims=True)
    prob_bf16 = weights.astype(jnp.bfloat16)
    mixed_rows = jnp.einsum("hqk,hkd->hqd", prob_bf16, v_rows, preferred_element_type=jnp.float32)
    return (mixed_rows, weights, prob_bf16)


def attend_back(q_rows, k_rows, v_rows, weights, prob_bf16, upstream):
    factor = 1.0 / math.sqrt(q_rows.shape[-1])
    grad_v = jnp.einsum("hqk,hqd->hkd", prob_bf16, upstream, preferred_element_type=jnp.float32)
    grad_p = jnp.einsum("hqd,hkd->hqk", upstream, v_rows, preferred_element_type=jnp.float32)
    centre = jnp.sum(weights * grad_p, axis=-1, keepdims=True)
    grad_s = (weights * (grad_p - centre)).astype(jnp.bfloat16)
    grad_q = jnp.einsum("hqk,hkd->hqd", grad_s, k_rows, preferred_element_type=jnp.float32) * factor
    grad_k = jnp.einsum("hqk,hqd->hkd", grad_s, q_rows, preferred_element_type=jnp.float32) * factor
    return (grad_q, grad_k, grad_v)


def send_kernel(order_ref, length_ref, q_ref, k_ref, v_ref, up_ref, gain_q_ref, gain_k_ref, out_ref):
    frames, _, wide = out_ref.shape
    slots, channels = q_ref.shape
    head_count = order_ref.shape[0]
    head_size = channels // head_count
    far_count = wide // head_size
    near_count = head_count - far_count
    span = slots // frames

    def normed(ref, gain_ref):
        rows = ref[...].astype(jnp.float32)
        inverse = lax.rsqrt(jnp.mean(rows * rows, axis=-1, keepdims=True) + 1e-06)
        return ((rows * inverse) * gain_ref[...]).astype(jnp.bfloat16).astype(jnp.float32)

    def far_of(rows):
        blocks = [rows[:, h * head_size : (h + 1) * head_size] for h in range(head_count)]
        picked = []
        for j in range(far_count):
            source = order_ref[near_count + j]
            tile = blocks[head_count - 1]
            for h in range(head_count - 2, -1, -1):
                tile = jnp.where(source == h, blocks[h], tile)
            picked.append(tile)
        return jnp.concatenate(picked, axis=1)

    live = lax.broadcasted_iota(jnp.int32, (slots, 1), 0) < length_ref[0]
    q_far = far_of(normed(q_ref, gain_q_ref))
    k_far = far_of(normed(k_ref, gain_k_ref))
    v_far = far_of(v_ref[...].astype(jnp.float32))
    up_far = jnp.where(live, far_of(up_ref[...].astype(jnp.float32)), 0.0)
    zero = jnp.zeros((span, wide), jnp.float32)
    k_pad = jnp.concatenate([zero, k_far, zero], axis=0)
    v_pad = jnp.concatenate([zero, v_far, zero], axis=0)
    for d in range(frames):
        rows = slice(d * span, (d + 1) * span)
        window = slice(d * span, d * span + 3 * span)
        out_ref[d] = jnp.concatenate(
            [q_far[rows], up_far[rows], k_pad[window], v_pad[window]], axis=0
        ).astype(out_ref.dtype)


def merge_kernel(
    order_ref,
    back_ref,
    near_out_ref,
    near_q_ref,
    near_k_ref,
    near_v_ref,
    q_unit_ref,
    q_inv_ref,
    k_unit_ref,
    k_inv_ref,
    gain_q_ref,
    gain_k_ref,
    attn_ref,
    gq_ref,
    gk_ref,
    gv_ref,
):
    blocks, _, wide = back_ref.shape
    head_count = order_ref.shape[0]
    far_count, _, head_size = near_q_ref.shape
    span = near_q_ref.shape[1] // blocks
    rows = [back_ref[c].astype(jnp.float32) for c in range(blocks)]

    def plain(first):
        return jnp.concatenate([rows[c][first : first + span] for c in range(blocks)], axis=0)

    def summed(first):
        parts = []
        for c in range(blocks):
            part = rows[c][first + span : first + 2 * span]
            if c + 1 < blocks:
                part = part + rows[c + 1][first : first + span]
            if c >= 1:
                part = part + rows[c - 1][first + 2 * span : first + 3 * span]
            parts.append(part)
        return jnp.concatenate(parts, axis=0)

    far = [plain(0), plain(span), summed(2 * span), summed(5 * span)]
    near = [
        [ref[i].astype(jnp.float32) for i in range(far_count)]
        for ref in (near_out_ref, near_q_ref, near_k_ref, near_v_ref)
    ]
    whole = [[], [], [], []]
    for h in range(head_count):
        place = order_ref[h]
        for t in range(4):
            tile = far[t][:, (far_count - 1) * head_size :]
            for i in range(far_count - 2, -1, -1):
                tile = jnp.where(place == far_count + i, far[t][:, i * head_size : (i + 1) * head_size], tile)
            for i in range(far_count - 1, -1, -1):
                tile = jnp.where(place == i, near[t][i], tile)
            whole[t].append(tile)
    whole = [jnp.concatenate(parts, axis=1) for parts in whole]
    attn_ref[...] = whole[0].astype(attn_ref.dtype)
    gv_ref[...] = whole[3].astype(gv_ref.dtype)
    for grad_rows, unit_ref, inv_ref, gain_ref, out_ref in (
        (whole[1], q_unit_ref, q_inv_ref, gain_q_ref, gq_ref),
        (whole[2], k_unit_ref, k_inv_ref, gain_k_ref, gk_ref),
    ):
        unit_rows = unit_ref[...]
        scaled = grad_rows * gain_ref[...]
        centre = jnp.mean(scaled * unit_rows, axis=-1, keepdims=True)
        out_ref[...] = (inv_ref[...] * (scaled - unit_rows * centre)).astype(out_ref.dtype)


def body(q_raw, k_raw, values, grad_out, gain_q, gain_k, labels, bands, counts):
    frame_count = lax.axis_size("ctx")
    own_frame = lax.axis_index("ctx")
    head_count = labels.shape[0]
    channels = q_raw.shape[3]
    head_size = channels // head_count
    slot_count = q_raw.shape[2]
    pos_span = slot_count // frame_count
    lengths = counts[0]
    frame_ids = jnp.arange(frame_count)
    own_length = jnp.sum(jnp.where(frame_ids == own_frame, lengths, 0))
    slot_live = jnp.arange(slot_count) < own_length
    q_norm, q_unit, q_inv = normalize(q_raw[0, 0], gain_q)
    k_norm, k_unit, k_inv = normalize(k_raw[0, 0], gain_k)
    v_rows = values[0, 0]
    up_rows = jnp.where(slot_live[:, None], grad_out[0, 0], jnp.zeros((), jnp.bfloat16))
    far_count = head_count // 2
    near_count = head_count - far_count
    ids = jnp.arange(head_count)
    before = (labels[None, :] < labels[:, None]) | (
        (labels[None, :] == labels[:, None]) & (ids[None, :] < ids[:, None])
    )
    back_order = jnp.sum(before.astype(jnp.int32), axis=1)
    head_order = jnp.sum(jnp.where(back_order[None, :] == ids[:, None], ids[None, :], 0), axis=1)
    far_heads = head_order[near_count:]
    wide = far_count * head_size

    def sorted_heads(block):
        shaped = block.reshape(block.shape[:-1] + (head_count, head_size))
        return jnp.take(shaped, head_order, axis=-2)

    def heads_first(block):
        return jnp.transpose(block, (1, 0, 2))

    def to_space(block, extent):
        shaped = block.reshape(frame_count, extent, far_count, head_size)
        return jnp.transpose(shaped, (2, 1, 0, 3)).reshape(
            far_count, extent * frame_count, head_size
        )

    def to_time(block, extent):
        shaped = block.reshape(far_count, extent, frame_count, head_size)
        return jnp.transpose(shaped, (2, 1, 0, 3)).reshape(frame_count, extent, wide)

    def to_time_pair(block, extent):
        shaped = block.reshape(2, far_count, extent, frame_count, head_size)
        return jnp.transpose(shaped, (3, 0, 2, 1, 4)).reshape(frame_count, 2 * extent, wide)

    def spread(near_part, far_part):
        return jnp.take(jnp.concatenate([near_part, far_part], axis=0), back_order, axis=0)

    picked = sorted_heads(jnp.stack([q_norm, k_norm, v_rows, up_rows]))
    units = sorted_heads(jnp.stack([q_unit, k_unit]))[:, :, :near_count]

    send = pl.pallas_call(
        send_kernel,
        out_shape=jax.ShapeDtypeStruct((frame_count, 8 * pos_span, wide), jnp.bfloat16),
        in_specs=[pl.BlockSpec(memory_space=pltpu.SMEM)] * 2 + [pl.BlockSpec(memory_space=pltpu.VMEM)] * 6,
        out_specs=pl.BlockSpec(memory_space=pltpu.VMEM),
        cost_estimate=pl.CostEstimate(
            flops=40 * slot_count * channels, bytes_accessed=12 * slot_count * channels, transcendentals=0
        ),
    )
    outgoing = send(
        head_order,
        own_length.reshape(1),
        q_raw[0, 0],
        k_raw[0, 0],
        v_rows,
        grad_out[0, 0],
        gain_q.reshape(1, channels),
        gain_k.reshape(1, channels),
    )
    sent = lax.all_to_all(outgoing, "ctx", split_axis=0, concat_axis=0, tiled=True)

    near_q, near_k, near_v, near_up = (heads_first(picked[i, :, :near_count]) for i in range(4))
    near_allowed = jnp.broadcast_to(
        slot_live[None, None, :], (near_count, slot_count, slot_count)
    )
    near_out, near_w, near_p = attend(near_q, near_k, near_v, near_allowed)
    near_out = jnp.where(slot_live[None, :, None], near_out, 0.0).astype(jnp.bfloat16)
    near_gq, near_gk, near_gv = attend_back(near_q, near_k, near_v, near_w, near_p, near_up)
    near_term_q = jnp.sum(near_gq * heads_first(units[0]), axis=1)
    near_term_k = jnp.sum(near_gk * heads_first(units[1]), axis=1)

    far_q = to_space(sent[:, :pos_span], pos_span)
    far_up = to_space(sent[:, pos_span : 2 * pos_span], pos_span)
    far_k = to_space(sent[:, 2 * pos_span : 5 * pos_span], 3 * pos_span)
    far_v = to_space(sent[:, 5 * pos_span :], 3 * pos_span)
    q_pos = own_frame * pos_span + jnp.arange(pos_span)
    k_pos = own_frame * pos_span - pos_span + jnp.arange(3 * pos_span)
    q_live = (q_pos[:, None] < lengths[None, :]).reshape(-1)
    k_live = (
        (k_pos[:, None] >= 0) & (k_pos[:, None] < slot_count) & (k_pos[:, None] < lengths[None, :])
    ).reshape(-1)
    pos_gap = jnp.abs(
        jnp.repeat(q_pos, frame_count)[:, None] - jnp.repeat(k_pos, frame_count)[None, :]
    )
    far_bands = jnp.take(bands, far_heads)
    far_allowed = (pos_gap[None] <= far_bands[:, None, None]) & k_live[None, None, :]
    far_out, far_w, far_p = attend(far_q, far_k, far_v, far_allowed)
    far_out = jnp.where(q_live[None, :, None], far_out, 0.0).astype(jnp.bfloat16)
    far_gq, far_gk, far_gv = attend_back(far_q, far_k, far_v, far_w, far_p, far_up)

    far_term_q = jnp.sum(far_gq * far_q.astype(jnp.float32), axis=1)
    far_term_k = jnp.sum(far_gk * far_k.astype(jnp.float32), axis=1)
    terms = jnp.stack([spread(near_term_q, far_term_q), spread(near_term_k, far_term_k)])
    head_gain = jnp.stack([gain_q, gain_k]).reshape(2, head_count, head_size)
    is_far = (back_order >= near_count)[None, :, None]
    terms = jnp.where(is_far, terms / head_gain, terms)
    terms_hi = terms.astype(jnp.bfloat16)
    terms_lo = (terms - terms_hi.astype(jnp.float32)).astype(jnp.bfloat16)
    term_rows = jnp.stack([terms_hi, terms_lo]).reshape(-1, wide)
    term_count = term_rows.shape[0]

    back = lax.all_to_all(
        jnp.concatenate(
            [
                to_time_pair(jnp.stack([far_out, far_gq.astype(jnp.bfloat16)]), pos_span),
                to_time_pair(jnp.stack([far_gk, far_gv]).astype(jnp.bfloat16), 3 * pos_span),
                jnp.broadcast_to(term_rows[None], (frame_count, term_count, wide)),
            ],
            axis=1,
        ),
        "ctx",
        split_axis=0,
        concat_axis=0,
        tiled=True,
    )
    got_terms = back[:, 8 * pos_span :].reshape(frame_count, 2, 2, head_count, head_size)
    got_terms = got_terms[:, 0].astype(jnp.float32) + got_terms[:, 1].astype(jnp.float32)
    video_count = lax.axis_size("dp")
    video_terms = jnp.sum(got_terms, axis=0)
    all_videos = lax.all_to_all(
        jnp.broadcast_to(video_terms[None], (video_count,) + video_terms.shape),
        "dp",
        split_axis=0,
        concat_axis=0,
        tiled=True,
    )
    totals = jnp.sum(all_videos, axis=0).reshape(2, channels)

    slot_bytes = slot_count * channels
    merge = pl.pallas_call(
        merge_kernel,
        out_shape=[jax.ShapeDtypeStruct((slot_count, channels), jnp.bfloat16)] * 4,
        in_specs=[pl.BlockSpec(memory_space=pltpu.SMEM)] + [pl.BlockSpec(memory_space=pltpu.VMEM)] * 11,
        out_specs=[pl.BlockSpec(memory_space=pltpu.VMEM)] * 4,
        cost_estimate=pl.CostEstimate(
            flops=40 * slot_bytes, bytes_accessed=30 * slot_bytes, transcendentals=0
        ),
    )
    attn_rows, grad_q_rows, grad_k_rows, grad_v_rows = merge(
        back_order,
        back,
        near_out,
        near_gq,
        near_gk,
        near_gv,
        q_unit,
        q_inv,
        k_unit,
        k_inv,
        gain_q.reshape(1, channels),
        gain_k.reshape(1, channels),
    )

    def as_shard(row_block):
        return row_block.reshape(1, 1, slot_count, channels)

    return (
        as_shard(attn_rows),
        as_shard(grad_q_rows),
        as_shard(grad_k_rows),
        as_shard(grad_v_rows),
        totals[0],
        totals[1],
    )


def solution(mesh):
    placed = (
        P("dp", "ctx", None, None),
        P("dp", "ctx", None, None),
        P("dp", "ctx", None, None),
        P("dp", "ctx", None, None),
        P(),
        P(),
        P(),
        P(),
        P("dp", None),
    )
    return jax.shard_map(
        body,
        mesh=mesh,
        in_specs=placed,
        out_specs=(
            P("dp", "ctx", None, None),
            P("dp", "ctx", None, None),
            P("dp", "ctx", None, None),
            P("dp", "ctx", None, None),
            P(),
            P(),
        ),
        check_vma=False,
    )
```

```python
import math

import jax
import jax.numpy as jnp
from jax import lax
from jax.experimental import pallas as pl
from jax.experimental.pallas import tpu as pltpu
from jax.sharding import PartitionSpec as P


def normalize(raw_rows, gain_row):
    full_rows = raw_rows.astype(jnp.float32)
    inverse = lax.rsqrt(jnp.mean(full_rows * full_rows, axis=-1, keepdims=True) + 1e-06)
    unit_rows = full_rows * inverse
    return ((unit_rows * gain_row).astype(jnp.bfloat16), unit_rows, inverse)


def normalize_back(grad_rows, unit_rows, inverse, gain_row):
    scaled = grad_rows * gain_row
    return inverse * (scaled - unit_rows * jnp.mean(scaled * unit_rows, axis=-1, keepdims=True))


def attend(q_rows, k_rows, v_rows, allowed):
    factor = 1.0 / math.sqrt(q_rows.shape[-1])
    scores = jnp.einsum("hqd,hkd->hqk", q_rows, k_rows, preferred_element_type=jnp.float32) * factor
    scores = jnp.where(allowed, scores, -1e30)
    row_peak = jnp.max(scores, axis=-1, keepdims=True)
    exp_terms = jnp.where(allowed, jnp.exp(scores - row_peak), 0.0)
    weights = exp_terms / jnp.sum(exp_terms, axis=-1, keepdims=True)
    prob_bf16 = weights.astype(jnp.bfloat16)
    mixed_rows = jnp.einsum("hqk,hkd->hqd", prob_bf16, v_rows, preferred_element_type=jnp.float32)
    return (mixed_rows, weights, prob_bf16)


def attend_back(q_rows, k_rows, v_rows, weights, prob_bf16, upstream):
    factor = 1.0 / math.sqrt(q_rows.shape[-1])
    grad_v = jnp.einsum("hqk,hqd->hkd", prob_bf16, upstream, preferred_element_type=jnp.float32)
    grad_p = jnp.einsum("hqd,hkd->hqk", upstream, v_rows, preferred_element_type=jnp.float32)
    centre = jnp.sum(weights * grad_p, axis=-1, keepdims=True)
    grad_s = (weights * (grad_p - centre)).astype(jnp.bfloat16)
    grad_q = jnp.einsum("hqk,hkd->hqd", grad_s, k_rows, preferred_element_type=jnp.float32) * factor
    grad_k = jnp.einsum("hqk,hqd->hkd", grad_s, q_rows, preferred_element_type=jnp.float32) * factor
    return (grad_q, grad_k, grad_v)


def send_kernel(label_ref, length_ref, q_ref, k_ref, v_ref, up_ref, gain_ref, out_ref):
    frames, _, wide = out_ref.shape
    slots, channels = q_ref.shape
    head_count = label_ref.shape[0]
    head_size = channels // head_count
    far_count = wide // head_size
    span = slots // frames
    sources = [0] * far_count
    seen = 0
    for h in range(head_count):
        temporal = label_ref[h] == 1
        for j in range(far_count):
            sources[j] = jnp.where(temporal & (seen == j), h, sources[j])
        seen = seen + temporal.astype(jnp.int32)

    def normed(ref, which):
        rows = ref[...].astype(jnp.float32)
        inverse = lax.rsqrt(jnp.mean(rows * rows, axis=-1, keepdims=True) + 1e-06)
        return ((rows * inverse) * gain_ref[which : which + 1, :]).astype(jnp.bfloat16).astype(jnp.float32)

    def far_of(rows):
        blocks = [rows[:, h * head_size : (h + 1) * head_size] for h in range(head_count)]
        picked = []
        for j in range(far_count):
            source = sources[j]
            tile = blocks[head_count - 1]
            for h in range(head_count - 2, -1, -1):
                tile = jnp.where(source == h, blocks[h], tile)
            picked.append(tile)
        return jnp.concatenate(picked, axis=1)

    live = lax.broadcasted_iota(jnp.int32, (slots, 1), 0) < length_ref[lax.axis_index("ctx")]
    q_far = far_of(normed(q_ref, 0))
    k_far = far_of(normed(k_ref, 1))
    v_far = far_of(v_ref[...].astype(jnp.float32))
    up_far = jnp.where(live, far_of(up_ref[...].astype(jnp.float32)), 0.0)
    zero = jnp.zeros((span, wide), jnp.float32)
    k_pad = jnp.concatenate([zero, k_far, zero], axis=0)
    v_pad = jnp.concatenate([zero, v_far, zero], axis=0)
    for d in range(frames):
        rows = slice(d * span, (d + 1) * span)
        window = slice(d * span, d * span + 3 * span)
        out_ref[d] = jnp.concatenate(
            [q_far[rows], up_far[rows], k_pad[window], v_pad[window]], axis=0
        ).astype(out_ref.dtype)


def merge_kernel(
    order_ref,
    back_ref,
    near_out_ref,
    near_q_ref,
    near_k_ref,
    near_v_ref,
    q_unit_ref,
    q_inv_ref,
    k_unit_ref,
    k_inv_ref,
    gain_q_ref,
    gain_k_ref,
    attn_ref,
    gq_ref,
    gk_ref,
    gv_ref,
):
    blocks, _, wide = back_ref.shape
    head_count = order_ref.shape[0]
    far_count, _, head_size = near_q_ref.shape
    span = near_q_ref.shape[1] // blocks
    rows = [back_ref[c].astype(jnp.float32) for c in range(blocks)]

    def plain(first):
        return jnp.concatenate([rows[c][first : first + span] for c in range(blocks)], axis=0)

    def summed(first):
        parts = []
        for c in range(blocks):
            part = rows[c][first + span : first + 2 * span]
            if c + 1 < blocks:
                part = part + rows[c + 1][first : first + span]
            if c >= 1:
                part = part + rows[c - 1][first + 2 * span : first + 3 * span]
            parts.append(part)
        return jnp.concatenate(parts, axis=0)

    far = [plain(0), plain(span), summed(2 * span), summed(5 * span)]
    near = [
        [ref[i].astype(jnp.float32) for i in range(far_count)]
        for ref in (near_out_ref, near_q_ref, near_k_ref, near_v_ref)
    ]
    whole = [[], [], [], []]
    for h in range(head_count):
        place = order_ref[h]
        for t in range(4):
            tile = far[t][:, (far_count - 1) * head_size :]
            for i in range(far_count - 2, -1, -1):
                tile = jnp.where(place == far_count + i, far[t][:, i * head_size : (i + 1) * head_size], tile)
            for i in range(far_count - 1, -1, -1):
                tile = jnp.where(place == i, near[t][i], tile)
            whole[t].append(tile)
    whole = [jnp.concatenate(parts, axis=1) for parts in whole]
    attn_ref[...] = whole[0].astype(attn_ref.dtype)
    gv_ref[...] = whole[3].astype(gv_ref.dtype)
    for grad_rows, unit_ref, inv_ref, gain_ref, out_ref in (
        (whole[1], q_unit_ref, q_inv_ref, gain_q_ref, gq_ref),
        (whole[2], k_unit_ref, k_inv_ref, gain_k_ref, gk_ref),
    ):
        unit_rows = unit_ref[...]
        scaled = grad_rows * gain_ref[...]
        centre = jnp.mean(scaled * unit_rows, axis=-1, keepdims=True)
        out_ref[...] = (inv_ref[...] * (scaled - unit_rows * centre)).astype(out_ref.dtype)


def body(q_raw, k_raw, values, grad_out, gain_q, gain_k, labels, bands, counts):
    frame_count = lax.axis_size("ctx")
    own_frame = lax.axis_index("ctx")
    head_count = labels.shape[0]
    channels = q_raw.shape[3]
    head_size = channels // head_count
    slot_count = q_raw.shape[2]
    pos_span = slot_count // frame_count
    lengths = counts[0]
    frame_ids = jnp.arange(frame_count)
    own_length = jnp.sum(jnp.where(frame_ids == own_frame, lengths, 0))
    slot_live = jnp.arange(slot_count) < own_length
    q_norm, q_unit, q_inv = normalize(q_raw[0, 0], gain_q)
    k_norm, k_unit, k_inv = normalize(k_raw[0, 0], gain_k)
    v_rows = values[0, 0]
    up_rows = jnp.where(slot_live[:, None], grad_out[0, 0], jnp.zeros((), jnp.bfloat16))
    far_count = head_count // 2
    near_count = head_count - far_count
    ids = jnp.arange(head_count)
    before = (labels[None, :] < labels[:, None]) | (
        (labels[None, :] == labels[:, None]) & (ids[None, :] < ids[:, None])
    )
    back_order = jnp.sum(before.astype(jnp.int32), axis=1)
    head_order = jnp.sum(jnp.where(back_order[None, :] == ids[:, None], ids[None, :], 0), axis=1)
    far_heads = head_order[near_count:]
    wide = far_count * head_size

    def sorted_heads(block):
        shaped = block.reshape(block.shape[:-1] + (head_count, head_size))
        return jnp.take(shaped, head_order, axis=-2)

    def heads_first(block):
        return jnp.transpose(block, (1, 0, 2))

    def to_space(block, extent):
        shaped = block.reshape(frame_count, extent, far_count, head_size)
        return jnp.transpose(shaped, (2, 1, 0, 3)).reshape(
            far_count, extent * frame_count, head_size
        )

    def to_time(block, extent):
        shaped = block.reshape(far_count, extent, frame_count, head_size)
        return jnp.transpose(shaped, (2, 1, 0, 3)).reshape(frame_count, extent, wide)

    def to_time_pair(block, extent):
        shaped = block.reshape(2, far_count, extent, frame_count, head_size)
        return jnp.transpose(shaped, (3, 0, 2, 1, 4)).reshape(frame_count, 2 * extent, wide)

    def spread(near_part, far_part):
        both = jnp.concatenate([near_part, far_part], axis=0)
        result = both[head_count - 1 :]
        for i in range(head_count - 2, -1, -1):
            result = jnp.where((back_order == i)[:, None], both[i : i + 1], result)
        return result

    picked = sorted_heads(jnp.stack([q_norm, k_norm, v_rows, up_rows]))
    units = sorted_heads(jnp.stack([q_unit, k_unit]))[:, :, :near_count]

    send = pl.pallas_call(
        send_kernel,
        out_shape=jax.ShapeDtypeStruct((frame_count, 8 * pos_span, wide), jnp.bfloat16),
        in_specs=[pl.BlockSpec(memory_space=pltpu.SMEM)] * 2 + [pl.BlockSpec(memory_space=pltpu.VMEM)] * 5,
        out_specs=pl.BlockSpec(memory_space=pltpu.VMEM),
        cost_estimate=pl.CostEstimate(
            flops=40 * slot_count * channels, bytes_accessed=12 * slot_count * channels, transcendentals=0
        ),
    )
    outgoing = send(
        labels, lengths, q_raw[0, 0], k_raw[0, 0], v_rows, grad_out[0, 0], jnp.stack([gain_q, gain_k])
    )
    sent = lax.all_to_all(outgoing, "ctx", split_axis=0, concat_axis=0, tiled=True)

    near_q, near_k, near_v, near_up = (heads_first(picked[i, :, :near_count]) for i in range(4))
    near_allowed = jnp.broadcast_to(
        slot_live[None, None, :], (near_count, slot_count, slot_count)
    )
    near_out, near_w, near_p = attend(near_q, near_k, near_v, near_allowed)
    near_out = jnp.where(slot_live[None, :, None], near_out, 0.0).astype(jnp.bfloat16)
    near_gq, near_gk, near_gv = attend_back(near_q, near_k, near_v, near_w, near_p, near_up)
    near_term_q = jnp.sum(near_gq * heads_first(units[0]), axis=1)
    near_term_k = jnp.sum(near_gk * heads_first(units[1]), axis=1)

    far_q = to_space(sent[:, :pos_span], pos_span)
    far_up = to_space(sent[:, pos_span : 2 * pos_span], pos_span)
    far_k = to_space(sent[:, 2 * pos_span : 5 * pos_span], 3 * pos_span)
    far_v = to_space(sent[:, 5 * pos_span :], 3 * pos_span)
    q_pos = own_frame * pos_span + jnp.arange(pos_span)
    k_pos = own_frame * pos_span - pos_span + jnp.arange(3 * pos_span)
    q_live = (q_pos[:, None] < lengths[None, :]).reshape(-1)
    k_live = (
        (k_pos[:, None] >= 0) & (k_pos[:, None] < slot_count) & (k_pos[:, None] < lengths[None, :])
    ).reshape(-1)
    pos_gap = jnp.abs(
        jnp.repeat(q_pos, frame_count)[:, None] - jnp.repeat(k_pos, frame_count)[None, :]
    )
    far_bands = jnp.take(bands, far_heads)
    far_allowed = (pos_gap[None] <= far_bands[:, None, None]) & k_live[None, None, :]
    far_out, far_w, far_p = attend(far_q, far_k, far_v, far_allowed)
    far_out = jnp.where(q_live[None, :, None], far_out, 0.0).astype(jnp.bfloat16)
    far_gq, far_gk, far_gv = attend_back(far_q, far_k, far_v, far_w, far_p, far_up)

    far_term_q = jnp.sum(far_gq * far_q.astype(jnp.float32), axis=1)
    far_term_k = jnp.sum(far_gk * far_k.astype(jnp.float32), axis=1)
    terms = jnp.stack([spread(near_term_q, far_term_q), spread(near_term_k, far_term_k)])
    head_gain = jnp.stack([gain_q, gain_k]).reshape(2, head_count, head_size)
    is_far = (back_order >= near_count)[None, :, None]
    terms = jnp.where(is_far, terms / head_gain, terms)
    terms_hi = terms.astype(jnp.bfloat16)
    terms_lo = (terms - terms_hi.astype(jnp.float32)).astype(jnp.bfloat16)
    term_rows = jnp.stack([terms_hi, terms_lo]).reshape(-1, wide)
    term_count = term_rows.shape[0]

    back = lax.all_to_all(
        jnp.concatenate(
            [
                to_time_pair(jnp.stack([far_out, far_gq.astype(jnp.bfloat16)]), pos_span),
                to_time_pair(jnp.stack([far_gk, far_gv]).astype(jnp.bfloat16), 3 * pos_span),
                jnp.broadcast_to(term_rows[None], (frame_count, term_count, wide)),
            ],
            axis=1,
        ),
        "ctx",
        split_axis=0,
        concat_axis=0,
        tiled=True,
    )
    got_terms = back[:, 8 * pos_span :].reshape(frame_count, 2, 2, head_count, head_size)
    got_terms = got_terms[:, 0].astype(jnp.float32) + got_terms[:, 1].astype(jnp.float32)
    video_count = lax.axis_size("dp")
    video_terms = jnp.sum(got_terms, axis=0)
    all_videos = lax.all_to_all(
        jnp.broadcast_to(video_terms[None], (video_count,) + video_terms.shape),
        "dp",
        split_axis=0,
        concat_axis=0,
        tiled=True,
    )
    totals = jnp.sum(all_videos, axis=0).reshape(2, channels)

    slot_bytes = slot_count * channels
    merge = pl.pallas_call(
        merge_kernel,
        out_shape=[jax.ShapeDtypeStruct((slot_count, channels), jnp.bfloat16)] * 4,
        in_specs=[pl.BlockSpec(memory_space=pltpu.SMEM)] + [pl.BlockSpec(memory_space=pltpu.VMEM)] * 11,
        out_specs=[pl.BlockSpec(memory_space=pltpu.VMEM)] * 4,
        cost_estimate=pl.CostEstimate(
            flops=40 * slot_bytes, bytes_accessed=30 * slot_bytes, transcendentals=0
        ),
    )
    attn_rows, grad_q_rows, grad_k_rows, grad_v_rows = merge(
        back_order,
        back,
        near_out,
        near_gq,
        near_gk,
        near_gv,
        q_unit,
        q_inv,
        k_unit,
        k_inv,
        gain_q.reshape(1, channels),
        gain_k.reshape(1, channels),
    )

    def as_shard(row_block):
        return row_block.reshape(1, 1, slot_count, channels)

    return (
        as_shard(attn_rows),
        as_shard(grad_q_rows),
        as_shard(grad_k_rows),
        as_shard(grad_v_rows),
        totals[0],
        totals[1],
    )


def solution(mesh):
    placed = (
        P("dp", "ctx", None, None),
        P("dp", "ctx", None, None),
        P("dp", "ctx", None, None),
        P("dp", "ctx", None, None),
        P(),
        P(),
        P(),
        P(),
        P("dp", None),
    )
    return jax.shard_map(
        body,
        mesh=mesh,
        in_specs=placed,
        out_specs=(
            P("dp", "ctx", None, None),
            P("dp", "ctx", None, None),
            P("dp", "ctx", None, None),
            P("dp", "ctx", None, None),
            P(),
            P(),
        ),
        check_vma=False,
    )
```

```python
import math

import jax
import jax.numpy as jnp
from jax import lax
from jax.experimental import pallas as pl
from jax.experimental.pallas import tpu as pltpu
from jax.sharding import PartitionSpec as P


def normalize(raw_rows, gain_row):
    full_rows = raw_rows.astype(jnp.float32)
    inverse = lax.rsqrt(jnp.mean(full_rows * full_rows, axis=-1, keepdims=True) + 1e-06)
    unit_rows = full_rows * inverse
    return ((unit_rows * gain_row).astype(jnp.bfloat16), unit_rows, inverse)


def normalize_back(grad_rows, unit_rows, inverse, gain_row):
    scaled = grad_rows * gain_row
    return inverse * (scaled - unit_rows * jnp.mean(scaled * unit_rows, axis=-1, keepdims=True))


def attend(q_rows, k_rows, v_rows, allowed):
    factor = 1.0 / math.sqrt(q_rows.shape[-1])
    scores = jnp.einsum("hqd,hkd->hqk", q_rows, k_rows, preferred_element_type=jnp.float32) * factor
    scores = jnp.where(allowed, scores, -1e30)
    row_peak = jnp.max(scores, axis=-1, keepdims=True)
    exp_terms = jnp.where(allowed, jnp.exp(scores - row_peak), 0.0)
    weights = exp_terms / jnp.sum(exp_terms, axis=-1, keepdims=True)
    prob_bf16 = weights.astype(jnp.bfloat16)
    mixed_rows = jnp.einsum("hqk,hkd->hqd", prob_bf16, v_rows, preferred_element_type=jnp.float32)
    return (mixed_rows, weights, prob_bf16)


def attend_back(q_rows, k_rows, v_rows, weights, prob_bf16, upstream):
    factor = 1.0 / math.sqrt(q_rows.shape[-1])
    grad_v = jnp.einsum("hqk,hqd->hkd", prob_bf16, upstream, preferred_element_type=jnp.float32)
    grad_p = jnp.einsum("hqd,hkd->hqk", upstream, v_rows, preferred_element_type=jnp.float32)
    centre = jnp.sum(weights * grad_p, axis=-1, keepdims=True)
    grad_s = (weights * (grad_p - centre)).astype(jnp.bfloat16)
    grad_q = jnp.einsum("hqk,hkd->hqd", grad_s, k_rows, preferred_element_type=jnp.float32) * factor
    grad_k = jnp.einsum("hqk,hqd->hkd", grad_s, q_rows, preferred_element_type=jnp.float32) * factor
    return (grad_q, grad_k, grad_v)


def send_kernel(label_ref, length_ref, q_ref, k_ref, v_ref, up_ref, gain_q_ref, gain_k_ref, out_ref):
    frames, _, wide = out_ref.shape
    slots, channels = q_ref.shape
    head_count = label_ref.shape[0]
    head_size = channels // head_count
    far_count = wide // head_size
    span = slots // frames
    sources = [0] * far_count
    seen = 0
    for h in range(head_count):
        temporal = label_ref[h] == 1
        for j in range(far_count):
            sources[j] = jnp.where(temporal & (seen == j), h, sources[j])
        seen = seen + temporal.astype(jnp.int32)

    def normed(ref, gain_ref):
        rows = ref[...].astype(jnp.float32)
        inverse = lax.rsqrt(jnp.mean(rows * rows, axis=-1, keepdims=True) + 1e-06)
        gain_row = gain_ref[...].reshape(1, channels)
        return ((rows * inverse) * gain_row).astype(jnp.bfloat16).astype(jnp.float32)

    def far_of(rows):
        blocks = [rows[:, h * head_size : (h + 1) * head_size] for h in range(head_count)]
        picked = []
        for j in range(far_count):
            source = sources[j]
            tile = blocks[head_count - 1]
            for h in range(head_count - 2, -1, -1):
                tile = jnp.where(source == h, blocks[h], tile)
            picked.append(tile)
        return jnp.concatenate(picked, axis=1)

    live = lax.broadcasted_iota(jnp.int32, (slots, 1), 0) < length_ref[lax.axis_index("ctx")]
    q_far = far_of(normed(q_ref, gain_q_ref))
    k_far = far_of(normed(k_ref, gain_k_ref))
    v_far = far_of(v_ref[...].astype(jnp.float32))
    up_far = jnp.where(live, far_of(up_ref[...].astype(jnp.float32)), 0.0)
    zero = jnp.zeros((span, wide), jnp.float32)
    k_pad = jnp.concatenate([zero, k_far, zero], axis=0)
    v_pad = jnp.concatenate([zero, v_far, zero], axis=0)
    for d in range(frames):
        rows = slice(d * span, (d + 1) * span)
        window = slice(d * span, d * span + 3 * span)
        out_ref[d] = jnp.concatenate(
            [q_far[rows], up_far[rows], k_pad[window], v_pad[window]], axis=0
        ).astype(out_ref.dtype)


def merge_kernel(
    order_ref,
    back_ref,
    near_out_ref,
    near_q_ref,
    near_k_ref,
    near_v_ref,
    q_unit_ref,
    q_inv_ref,
    k_unit_ref,
    k_inv_ref,
    gain_q_ref,
    gain_k_ref,
    attn_ref,
    gq_ref,
    gk_ref,
    gv_ref,
):
    blocks, _, wide = back_ref.shape
    head_count = order_ref.shape[0]
    far_count, _, head_size = near_q_ref.shape
    span = near_q_ref.shape[1] // blocks
    rows = [back_ref[c].astype(jnp.float32) for c in range(blocks)]

    def plain(first):
        return jnp.concatenate([rows[c][first : first + span] for c in range(blocks)], axis=0)

    def summed(first):
        parts = []
        for c in range(blocks):
            part = rows[c][first + span : first + 2 * span]
            if c + 1 < blocks:
                part = part + rows[c + 1][first : first + span]
            if c >= 1:
                part = part + rows[c - 1][first + 2 * span : first + 3 * span]
            parts.append(part)
        return jnp.concatenate(parts, axis=0)

    far = [plain(0), plain(span), summed(2 * span), summed(5 * span)]
    near = [
        [ref[i].astype(jnp.float32) for i in range(far_count)]
        for ref in (near_out_ref, near_q_ref, near_k_ref, near_v_ref)
    ]
    whole = [[], [], [], []]
    for h in range(head_count):
        place = order_ref[h]
        for t in range(4):
            tile = far[t][:, (far_count - 1) * head_size :]
            for i in range(far_count - 2, -1, -1):
                tile = jnp.where(place == far_count + i, far[t][:, i * head_size : (i + 1) * head_size], tile)
            for i in range(far_count - 1, -1, -1):
                tile = jnp.where(place == i, near[t][i], tile)
            whole[t].append(tile)
    whole = [jnp.concatenate(parts, axis=1) for parts in whole]
    attn_ref[...] = whole[0].astype(attn_ref.dtype)
    gv_ref[...] = whole[3].astype(gv_ref.dtype)
    for grad_rows, unit_ref, inv_ref, gain_ref, out_ref in (
        (whole[1], q_unit_ref, q_inv_ref, gain_q_ref, gq_ref),
        (whole[2], k_unit_ref, k_inv_ref, gain_k_ref, gk_ref),
    ):
        unit_rows = unit_ref[...]
        scaled = grad_rows * gain_ref[...]
        centre = jnp.mean(scaled * unit_rows, axis=-1, keepdims=True)
        out_ref[...] = (inv_ref[...] * (scaled - unit_rows * centre)).astype(out_ref.dtype)


def body(q_raw, k_raw, values, grad_out, gain_q, gain_k, labels, bands, counts):
    frame_count = lax.axis_size("ctx")
    own_frame = lax.axis_index("ctx")
    head_count = labels.shape[0]
    channels = q_raw.shape[3]
    head_size = channels // head_count
    slot_count = q_raw.shape[2]
    pos_span = slot_count // frame_count
    lengths = counts[0]
    frame_ids = jnp.arange(frame_count)
    own_length = jnp.sum(jnp.where(frame_ids == own_frame, lengths, 0))
    slot_live = jnp.arange(slot_count) < own_length
    q_norm, q_unit, q_inv = normalize(q_raw[0, 0], gain_q)
    k_norm, k_unit, k_inv = normalize(k_raw[0, 0], gain_k)
    v_rows = values[0, 0]
    up_rows = jnp.where(slot_live[:, None], grad_out[0, 0], jnp.zeros((), jnp.bfloat16))
    far_count = head_count // 2
    near_count = head_count - far_count
    ids = jnp.arange(head_count)
    before = (labels[None, :] < labels[:, None]) | (
        (labels[None, :] == labels[:, None]) & (ids[None, :] < ids[:, None])
    )
    back_order = jnp.sum(before.astype(jnp.int32), axis=1)
    head_order = jnp.sum(jnp.where(back_order[None, :] == ids[:, None], ids[None, :], 0), axis=1)
    far_heads = head_order[near_count:]
    wide = far_count * head_size

    def sorted_heads(block):
        shaped = block.reshape(block.shape[:-1] + (head_count, head_size))
        return jnp.take(shaped, head_order, axis=-2)

    def heads_first(block):
        return jnp.transpose(block, (1, 0, 2))

    def to_space(block, extent):
        shaped = block.reshape(frame_count, extent, far_count, head_size)
        return jnp.transpose(shaped, (2, 1, 0, 3)).reshape(
            far_count, extent * frame_count, head_size
        )

    def to_time(block, extent):
        shaped = block.reshape(far_count, extent, frame_count, head_size)
        return jnp.transpose(shaped, (2, 1, 0, 3)).reshape(frame_count, extent, wide)

    def to_time_pair(block, extent):
        shaped = block.reshape(2, far_count, extent, frame_count, head_size)
        return jnp.transpose(shaped, (3, 0, 2, 1, 4)).reshape(frame_count, 2 * extent, wide)

    def spread(near_part, far_part):
        both = jnp.concatenate([near_part, far_part], axis=0)
        result = both[head_count - 1 :]
        for i in range(head_count - 2, -1, -1):
            result = jnp.where((back_order == i)[:, None], both[i : i + 1], result)
        return result

    picked = sorted_heads(jnp.stack([q_norm, k_norm, v_rows, up_rows]))
    units = sorted_heads(jnp.stack([q_unit, k_unit]))[:, :, :near_count]

    send = pl.pallas_call(
        send_kernel,
        out_shape=jax.ShapeDtypeStruct((frame_count, 8 * pos_span, wide), jnp.bfloat16),
        in_specs=[pl.BlockSpec(memory_space=pltpu.SMEM)] * 2 + [pl.BlockSpec(memory_space=pltpu.VMEM)] * 6,
        out_specs=pl.BlockSpec(memory_space=pltpu.VMEM),
        cost_estimate=pl.CostEstimate(
            flops=40 * slot_count * channels, bytes_accessed=12 * slot_count * channels, transcendentals=0
        ),
    )
    outgoing = send(
        labels, lengths, q_raw[0, 0], k_raw[0, 0], v_rows, grad_out[0, 0], gain_q, gain_k
    )
    sent = lax.all_to_all(outgoing, "ctx", split_axis=0, concat_axis=0, tiled=True)

    near_q, near_k, near_v, near_up = (heads_first(picked[i, :, :near_count]) for i in range(4))
    near_allowed = jnp.broadcast_to(
        slot_live[None, None, :], (near_count, slot_count, slot_count)
    )
    near_out, near_w, near_p = attend(near_q, near_k, near_v, near_allowed)
    near_out = jnp.where(slot_live[None, :, None], near_out, 0.0).astype(jnp.bfloat16)
    near_gq, near_gk, near_gv = attend_back(near_q, near_k, near_v, near_w, near_p, near_up)
    near_term_q = jnp.sum(near_gq * heads_first(units[0]), axis=1)
    near_term_k = jnp.sum(near_gk * heads_first(units[1]), axis=1)

    far_q = to_space(sent[:, :pos_span], pos_span)
    far_up = to_space(sent[:, pos_span : 2 * pos_span], pos_span)
    far_k = to_space(sent[:, 2 * pos_span : 5 * pos_span], 3 * pos_span)
    far_v = to_space(sent[:, 5 * pos_span :], 3 * pos_span)
    q_pos = own_frame * pos_span + jnp.arange(pos_span)
    k_pos = own_frame * pos_span - pos_span + jnp.arange(3 * pos_span)
    q_live = (q_pos[:, None] < lengths[None, :]).reshape(-1)
    k_live = (
        (k_pos[:, None] >= 0) & (k_pos[:, None] < slot_count) & (k_pos[:, None] < lengths[None, :])
    ).reshape(-1)
    pos_gap = jnp.abs(
        jnp.repeat(q_pos, frame_count)[:, None] - jnp.repeat(k_pos, frame_count)[None, :]
    )
    far_bands = jnp.take(bands, far_heads)
    far_allowed = (pos_gap[None] <= far_bands[:, None, None]) & k_live[None, None, :]
    far_out, far_w, far_p = attend(far_q, far_k, far_v, far_allowed)
    far_out = jnp.where(q_live[None, :, None], far_out, 0.0).astype(jnp.bfloat16)
    far_gq, far_gk, far_gv = attend_back(far_q, far_k, far_v, far_w, far_p, far_up)

    far_term_q = jnp.sum(far_gq * far_q.astype(jnp.float32), axis=1)
    far_term_k = jnp.sum(far_gk * far_k.astype(jnp.float32), axis=1)
    terms = jnp.stack([spread(near_term_q, far_term_q), spread(near_term_k, far_term_k)])
    head_gain = jnp.stack([gain_q, gain_k]).reshape(2, head_count, head_size)
    is_far = (back_order >= near_count)[None, :, None]
    terms = jnp.where(is_far, terms / head_gain, terms)
    terms_hi = terms.astype(jnp.bfloat16)
    terms_lo = (terms - terms_hi.astype(jnp.float32)).astype(jnp.bfloat16)
    term_rows = jnp.stack([terms_hi, terms_lo]).reshape(-1, wide)
    term_count = term_rows.shape[0]

    back = lax.all_to_all(
        jnp.concatenate(
            [
                to_time_pair(jnp.stack([far_out, far_gq.astype(jnp.bfloat16)]), pos_span),
                to_time_pair(jnp.stack([far_gk, far_gv]).astype(jnp.bfloat16), 3 * pos_span),
                jnp.broadcast_to(term_rows[None], (frame_count, term_count, wide)),
            ],
            axis=1,
        ),
        "ctx",
        split_axis=0,
        concat_axis=0,
        tiled=True,
    )
    got_terms = back[:, 8 * pos_span :].reshape(frame_count, 2, 2, head_count, head_size)
    got_terms = got_terms[:, 0].astype(jnp.float32) + got_terms[:, 1].astype(jnp.float32)
    video_count = lax.axis_size("dp")
    video_terms = jnp.sum(got_terms, axis=0)
    all_videos = lax.all_to_all(
        jnp.broadcast_to(video_terms[None], (video_count,) + video_terms.shape),
        "dp",
        split_axis=0,
        concat_axis=0,
        tiled=True,
    )
    totals = jnp.sum(all_videos, axis=0).reshape(2, channels)

    slot_bytes = slot_count * channels
    merge = pl.pallas_call(
        merge_kernel,
        out_shape=[jax.ShapeDtypeStruct((slot_count, channels), jnp.bfloat16)] * 4,
        in_specs=[pl.BlockSpec(memory_space=pltpu.SMEM)] + [pl.BlockSpec(memory_space=pltpu.VMEM)] * 11,
        out_specs=[pl.BlockSpec(memory_space=pltpu.VMEM)] * 4,
        cost_estimate=pl.CostEstimate(
            flops=40 * slot_bytes, bytes_accessed=30 * slot_bytes, transcendentals=0
        ),
    )
    attn_rows, grad_q_rows, grad_k_rows, grad_v_rows = merge(
        back_order,
        back,
        near_out,
        near_gq,
        near_gk,
        near_gv,
        q_unit,
        q_inv,
        k_unit,
        k_inv,
        gain_q.reshape(1, channels),
        gain_k.reshape(1, channels),
    )

    def as_shard(row_block):
        return row_block.reshape(1, 1, slot_count, channels)

    return (
        as_shard(attn_rows),
        as_shard(grad_q_rows),
        as_shard(grad_k_rows),
        as_shard(grad_v_rows),
        totals[0],
        totals[1],
    )


def solution(mesh):
    placed = (
        P("dp", "ctx", None, None),
        P("dp", "ctx", None, None),
        P("dp", "ctx", None, None),
        P("dp", "ctx", None, None),
        P(),
        P(),
        P(),
        P(),
        P("dp", None),
    )
    return jax.shard_map(
        body,
        mesh=mesh,
        in_specs=placed,
        out_specs=(
            P("dp", "ctx", None, None),
            P("dp", "ctx", None, None),
            P("dp", "ctx", None, None),
            P("dp", "ctx", None, None),
            P(),
            P(),
        ),
        check_vma=False,
    )
```

```python
import math

import jax
import jax.numpy as jnp
from jax import lax
from jax.experimental import pallas as pl
from jax.experimental.pallas import tpu as pltpu
from jax.sharding import PartitionSpec as P


def normalize(raw_rows, gain_row):
    full_rows = raw_rows.astype(jnp.float32)
    inverse = lax.rsqrt(jnp.mean(full_rows * full_rows, axis=-1, keepdims=True) + 1e-06)
    unit_rows = full_rows * inverse
    return ((unit_rows * gain_row).astype(jnp.bfloat16), unit_rows, inverse)


def normalize_back(grad_rows, unit_rows, inverse, gain_row):
    scaled = grad_rows * gain_row
    return inverse * (scaled - unit_rows * jnp.mean(scaled * unit_rows, axis=-1, keepdims=True))


def attend(q_rows, k_rows, v_rows, allowed):
    factor = 1.0 / math.sqrt(q_rows.shape[-1])
    scores = jnp.einsum("hqd,hkd->hqk", q_rows, k_rows, preferred_element_type=jnp.float32) * factor
    scores = jnp.where(allowed, scores, -1e30)
    row_peak = jnp.max(scores, axis=-1, keepdims=True)
    exp_terms = jnp.where(allowed, jnp.exp(scores - row_peak), 0.0)
    weights = exp_terms / jnp.sum(exp_terms, axis=-1, keepdims=True)
    prob_bf16 = weights.astype(jnp.bfloat16)
    mixed_rows = jnp.einsum("hqk,hkd->hqd", prob_bf16, v_rows, preferred_element_type=jnp.float32)
    return (mixed_rows, weights, prob_bf16)


def attend_back(q_rows, k_rows, v_rows, weights, prob_bf16, upstream):
    factor = 1.0 / math.sqrt(q_rows.shape[-1])
    grad_v = jnp.einsum("hqk,hqd->hkd", prob_bf16, upstream, preferred_element_type=jnp.float32)
    grad_p = jnp.einsum("hqd,hkd->hqk", upstream, v_rows, preferred_element_type=jnp.float32)
    centre = jnp.sum(weights * grad_p, axis=-1, keepdims=True)
    grad_s = (weights * (grad_p - centre)).astype(jnp.bfloat16)
    grad_q = jnp.einsum("hqk,hkd->hqd", grad_s, k_rows, preferred_element_type=jnp.float32) * factor
    grad_k = jnp.einsum("hqk,hqd->hkd", grad_s, q_rows, preferred_element_type=jnp.float32) * factor
    return (grad_q, grad_k, grad_v)


def send_kernel(label_ref, length_ref, q_ref, k_ref, v_ref, up_ref, gain_q_ref, gain_k_ref, out_ref):
    frames, _, wide = out_ref.shape
    slots, channels = q_ref.shape
    head_count = label_ref.shape[0]
    head_size = channels // head_count
    far_count = wide // head_size
    span = slots // frames
    sources = [0] * far_count
    seen = 0
    for h in range(head_count):
        temporal = label_ref[h] == 1
        for j in range(far_count):
            sources[j] = jnp.where(temporal & (seen == j), h, sources[j])
        seen = seen + temporal.astype(jnp.int32)

    def normed(ref, gain_ref):
        rows = ref[...].astype(jnp.float32)
        inverse = lax.rsqrt(jnp.mean(rows * rows, axis=-1, keepdims=True) + 1e-06)
        gain_row = gain_ref[...].reshape(1, channels)
        return ((rows * inverse) * gain_row).astype(jnp.bfloat16).astype(jnp.float32)

    def far_of(rows):
        blocks = [rows[:, h * head_size : (h + 1) * head_size] for h in range(head_count)]
        picked = []
        for j in range(far_count):
            source = sources[j]
            tile = blocks[head_count - 1]
            for h in range(head_count - 2, -1, -1):
                tile = jnp.where(source == h, blocks[h], tile)
            picked.append(tile)
        return jnp.concatenate(picked, axis=1)

    live = lax.broadcasted_iota(jnp.int32, (slots, 1), 0) < length_ref[lax.axis_index("ctx")]
    q_far = far_of(normed(q_ref, gain_q_ref))
    k_far = far_of(normed(k_ref, gain_k_ref))
    v_far = far_of(v_ref[...].astype(jnp.float32))
    up_far = jnp.where(live, far_of(up_ref[...].astype(jnp.float32)), 0.0)
    zero = jnp.zeros((span, wide), jnp.float32)
    k_pad = jnp.concatenate([zero, k_far, zero], axis=0)
    v_pad = jnp.concatenate([zero, v_far, zero], axis=0)
    for d in range(frames):
        rows = slice(d * span, (d + 1) * span)
        window = slice(d * span, d * span + 3 * span)
        out_ref[d] = jnp.concatenate(
            [q_far[rows], up_far[rows], k_pad[window], v_pad[window]], axis=0
        ).astype(out_ref.dtype)


def merge_kernel(
    order_ref,
    back_ref,
    near_out_ref,
    near_q_ref,
    near_k_ref,
    near_v_ref,
    q_unit_ref,
    q_inv_ref,
    k_unit_ref,
    k_inv_ref,
    gain_q_ref,
    gain_k_ref,
    attn_ref,
    gq_ref,
    gk_ref,
    gv_ref,
):
    blocks, _, wide = back_ref.shape
    head_count = order_ref.shape[0]
    far_count, _, head_size = near_q_ref.shape
    span = near_q_ref.shape[1] // blocks
    rows = [back_ref[c].astype(jnp.float32) for c in range(blocks)]

    def plain(first):
        return jnp.concatenate([rows[c][first : first + span] for c in range(blocks)], axis=0)

    def summed(first):
        parts = []
        for c in range(blocks):
            part = rows[c][first + span : first + 2 * span]
            if c + 1 < blocks:
                part = part + rows[c + 1][first : first + span]
            if c >= 1:
                part = part + rows[c - 1][first + 2 * span : first + 3 * span]
            parts.append(part)
        return jnp.concatenate(parts, axis=0)

    far = [plain(0), plain(span), summed(2 * span), summed(5 * span)]
    near = [
        [ref[i].astype(jnp.float32) for i in range(far_count)]
        for ref in (near_out_ref, near_q_ref, near_k_ref, near_v_ref)
    ]
    whole = [[], [], [], []]
    for h in range(head_count):
        place = order_ref[h]
        for t in range(4):
            tile = far[t][:, (far_count - 1) * head_size :]
            for i in range(far_count - 2, -1, -1):
                tile = jnp.where(place == far_count + i, far[t][:, i * head_size : (i + 1) * head_size], tile)
            for i in range(far_count - 1, -1, -1):
                tile = jnp.where(place == i, near[t][i], tile)
            whole[t].append(tile)
    whole = [jnp.concatenate(parts, axis=1) for parts in whole]
    attn_ref[...] = whole[0].astype(attn_ref.dtype)
    gv_ref[...] = whole[3].astype(gv_ref.dtype)
    for grad_rows, unit_ref, inv_ref, gain_ref, out_ref in (
        (whole[1], q_unit_ref, q_inv_ref, gain_q_ref, gq_ref),
        (whole[2], k_unit_ref, k_inv_ref, gain_k_ref, gk_ref),
    ):
        unit_rows = unit_ref[...]
        scaled = grad_rows * gain_ref[...]
        centre = jnp.mean(scaled * unit_rows, axis=-1, keepdims=True)
        out_ref[...] = (inv_ref[...] * (scaled - unit_rows * centre)).astype(out_ref.dtype)


def body(q_raw, k_raw, values, grad_out, gain_q, gain_k, labels, bands, counts):
    frame_count = lax.axis_size("ctx")
    own_frame = lax.axis_index("ctx")
    head_count = labels.shape[0]
    channels = q_raw.shape[3]
    head_size = channels // head_count
    slot_count = q_raw.shape[2]
    pos_span = slot_count // frame_count
    lengths = counts[0]
    frame_ids = jnp.arange(frame_count)
    own_length = jnp.sum(jnp.where(frame_ids == own_frame, lengths, 0))
    slot_live = jnp.arange(slot_count) < own_length
    q_norm, q_unit, q_inv = normalize(q_raw[0, 0], gain_q)
    k_norm, k_unit, k_inv = normalize(k_raw[0, 0], gain_k)
    v_rows = values[0, 0]
    up_rows = jnp.where(slot_live[:, None], grad_out[0, 0], jnp.zeros((), jnp.bfloat16))
    far_count = head_count // 2
    near_count = head_count - far_count
    ids = jnp.arange(head_count)
    before = (labels[None, :] < labels[:, None]) | (
        (labels[None, :] == labels[:, None]) & (ids[None, :] < ids[:, None])
    )
    back_order = jnp.sum(before.astype(jnp.int32), axis=1)
    head_order = jnp.sum(jnp.where(back_order[None, :] == ids[:, None], ids[None, :], 0), axis=1)
    far_heads = head_order[near_count:]
    wide = far_count * head_size

    def sorted_heads(block):
        shaped = block.reshape(block.shape[:-1] + (head_count, head_size))
        return jnp.take(shaped, head_order, axis=-2)

    def heads_first(block):
        return jnp.transpose(block, (1, 0, 2))

    def to_space(block, extent):
        shaped = block.reshape(frame_count, extent, far_count, head_size)
        return jnp.transpose(shaped, (2, 0, 1, 3)).reshape(
            far_count, frame_count * extent, head_size
        )

    def to_time_pair(block, extent):
        shaped = block.reshape(2, far_count, frame_count, extent, head_size)
        return jnp.transpose(shaped, (2, 0, 3, 1, 4)).reshape(frame_count, 2 * extent, wide)

    def spread(near_part, far_part):
        both = jnp.concatenate([near_part, far_part], axis=0)
        result = both[head_count - 1 :]
        for i in range(head_count - 2, -1, -1):
            result = jnp.where((back_order == i)[:, None], both[i : i + 1], result)
        return result

    picked = sorted_heads(jnp.stack([q_norm, k_norm, v_rows, up_rows]))
    units = sorted_heads(jnp.stack([q_unit, k_unit]))[:, :, :near_count]

    send = pl.pallas_call(
        send_kernel,
        out_shape=jax.ShapeDtypeStruct((frame_count, 8 * pos_span, wide), jnp.bfloat16),
        in_specs=[pl.BlockSpec(memory_space=pltpu.SMEM)] * 2 + [pl.BlockSpec(memory_space=pltpu.VMEM)] * 6,
        out_specs=pl.BlockSpec(memory_space=pltpu.VMEM),
        cost_estimate=pl.CostEstimate(
            flops=40 * slot_count * channels, bytes_accessed=12 * slot_count * channels, transcendentals=0
        ),
    )
    outgoing = send(
        labels, lengths, q_raw[0, 0], k_raw[0, 0], v_rows, grad_out[0, 0], gain_q, gain_k
    )
    sent = lax.all_to_all(outgoing, "ctx", split_axis=0, concat_axis=0, tiled=True)

    near_q, near_k, near_v, near_up = (heads_first(picked[i, :, :near_count]) for i in range(4))
    near_allowed = jnp.broadcast_to(
        slot_live[None, None, :], (near_count, slot_count, slot_count)
    )
    near_out, near_w, near_p = attend(near_q, near_k, near_v, near_allowed)
    near_out = jnp.where(slot_live[None, :, None], near_out, 0.0).astype(jnp.bfloat16)
    near_gq, near_gk, near_gv = attend_back(near_q, near_k, near_v, near_w, near_p, near_up)
    near_term_q = jnp.sum(near_gq * heads_first(units[0]), axis=1)
    near_term_k = jnp.sum(near_gk * heads_first(units[1]), axis=1)

    far_q = to_space(sent[:, :pos_span], pos_span)
    far_up = to_space(sent[:, pos_span : 2 * pos_span], pos_span)
    far_k = to_space(sent[:, 2 * pos_span : 5 * pos_span], 3 * pos_span)
    far_v = to_space(sent[:, 5 * pos_span :], 3 * pos_span)
    q_pos = own_frame * pos_span + jnp.arange(pos_span)
    k_pos = own_frame * pos_span - pos_span + jnp.arange(3 * pos_span)
    q_live = (q_pos[None, :] < lengths[:, None]).reshape(-1)
    k_live = (
        (k_pos[None, :] >= 0) & (k_pos[None, :] < slot_count) & (k_pos[None, :] < lengths[:, None])
    ).reshape(-1)
    pos_gap = jnp.abs(jnp.tile(q_pos, frame_count)[:, None] - jnp.tile(k_pos, frame_count)[None, :])
    far_bands = jnp.take(bands, far_heads)
    far_allowed = (pos_gap[None] <= far_bands[:, None, None]) & k_live[None, None, :]
    far_out, far_w, far_p = attend(far_q, far_k, far_v, far_allowed)
    far_out = jnp.where(q_live[None, :, None], far_out, 0.0).astype(jnp.bfloat16)
    far_gq, far_gk, far_gv = attend_back(far_q, far_k, far_v, far_w, far_p, far_up)

    far_term_q = jnp.sum(far_gq * far_q.astype(jnp.float32), axis=1)
    far_term_k = jnp.sum(far_gk * far_k.astype(jnp.float32), axis=1)
    terms = jnp.stack([spread(near_term_q, far_term_q), spread(near_term_k, far_term_k)])
    head_gain = jnp.stack([gain_q, gain_k]).reshape(2, head_count, head_size)
    is_far = (back_order >= near_count)[None, :, None]
    terms = jnp.where(is_far, terms / head_gain, terms)
    terms_hi = terms.astype(jnp.bfloat16)
    terms_lo = (terms - terms_hi.astype(jnp.float32)).astype(jnp.bfloat16)
    term_rows = jnp.stack([terms_hi, terms_lo]).reshape(-1, wide)
    term_count = term_rows.shape[0]

    back = lax.all_to_all(
        jnp.concatenate(
            [
                to_time_pair(jnp.stack([far_out, far_gq.astype(jnp.bfloat16)]), pos_span),
                to_time_pair(jnp.stack([far_gk, far_gv]).astype(jnp.bfloat16), 3 * pos_span),
                jnp.broadcast_to(term_rows[None], (frame_count, term_count, wide)),
            ],
            axis=1,
        ),
        "ctx",
        split_axis=0,
        concat_axis=0,
        tiled=True,
    )
    got_terms = back[:, 8 * pos_span :].reshape(frame_count, 2, 2, head_count, head_size)
    got_terms = got_terms[:, 0].astype(jnp.float32) + got_terms[:, 1].astype(jnp.float32)
    video_count = lax.axis_size("dp")
    video_terms = jnp.sum(got_terms, axis=0)
    all_videos = lax.all_to_all(
        jnp.broadcast_to(video_terms[None], (video_count,) + video_terms.shape),
        "dp",
        split_axis=0,
        concat_axis=0,
        tiled=True,
    )
    totals = jnp.sum(all_videos, axis=0).reshape(2, channels)

    slot_bytes = slot_count * channels
    merge = pl.pallas_call(
        merge_kernel,
        out_shape=[jax.ShapeDtypeStruct((slot_count, channels), jnp.bfloat16)] * 4,
        in_specs=[pl.BlockSpec(memory_space=pltpu.SMEM)] + [pl.BlockSpec(memory_space=pltpu.VMEM)] * 11,
        out_specs=[pl.BlockSpec(memory_space=pltpu.VMEM)] * 4,
        cost_estimate=pl.CostEstimate(
            flops=40 * slot_bytes, bytes_accessed=30 * slot_bytes, transcendentals=0
        ),
    )
    attn_rows, grad_q_rows, grad_k_rows, grad_v_rows = merge(
        back_order,
        back,
        near_out,
        near_gq,
        near_gk,
        near_gv,
        q_unit,
        q_inv,
        k_unit,
        k_inv,
        gain_q.reshape(1, channels),
        gain_k.reshape(1, channels),
    )

    def as_shard(row_block):
        return row_block.reshape(1, 1, slot_count, channels)

    return (
        as_shard(attn_rows),
        as_shard(grad_q_rows),
        as_shard(grad_k_rows),
        as_shard(grad_v_rows),
        totals[0],
        totals[1],
    )


def solution(mesh):
    placed = (
        P("dp", "ctx", None, None),
        P("dp", "ctx", None, None),
        P("dp", "ctx", None, None),
        P("dp", "ctx", None, None),
        P(),
        P(),
        P(),
        P(),
        P("dp", None),
    )
    return jax.shard_map(
        body,
        mesh=mesh,
        in_specs=placed,
        out_specs=(
            P("dp", "ctx", None, None),
            P("dp", "ctx", None, None),
            P("dp", "ctx", None, None),
            P("dp", "ctx", None, None),
            P(),
            P(),
        ),
        check_vma=False,
    )
```

```python
import math

import jax
import jax.numpy as jnp
from jax import lax
from jax.experimental import pallas as pl
from jax.experimental.pallas import tpu as pltpu
from jax.sharding import PartitionSpec as P


def normalize(raw_rows, gain_row):
    full_rows = raw_rows.astype(jnp.float32)
    inverse = lax.rsqrt(jnp.mean(full_rows * full_rows, axis=-1, keepdims=True) + 1e-06)
    unit_rows = full_rows * inverse
    return ((unit_rows * gain_row).astype(jnp.bfloat16), unit_rows, inverse)


def normalize_back(grad_rows, unit_rows, inverse, gain_row):
    scaled = grad_rows * gain_row
    return inverse * (scaled - unit_rows * jnp.mean(scaled * unit_rows, axis=-1, keepdims=True))


def attend(q_rows, k_rows, v_rows, allowed):
    factor = 1.0 / math.sqrt(q_rows.shape[-1])
    scores = jnp.einsum("hqd,hkd->hqk", q_rows, k_rows, preferred_element_type=jnp.float32) * factor
    scores = jnp.where(allowed, scores, -1e30)
    row_peak = jnp.max(scores, axis=-1, keepdims=True)
    exp_terms = jnp.where(allowed, jnp.exp(scores - row_peak), 0.0)
    weights = exp_terms / jnp.sum(exp_terms, axis=-1, keepdims=True)
    prob_bf16 = weights.astype(jnp.bfloat16)
    mixed_rows = jnp.einsum("hqk,hkd->hqd", prob_bf16, v_rows, preferred_element_type=jnp.float32)
    return (mixed_rows, weights, prob_bf16)


def attend_back(q_rows, k_rows, v_rows, weights, prob_bf16, upstream):
    factor = 1.0 / math.sqrt(q_rows.shape[-1])
    grad_v = jnp.einsum("hqk,hqd->hkd", prob_bf16, upstream, preferred_element_type=jnp.float32)
    grad_p = jnp.einsum("hqd,hkd->hqk", upstream, v_rows, preferred_element_type=jnp.float32)
    centre = jnp.sum(weights * grad_p, axis=-1, keepdims=True)
    grad_s = (weights * (grad_p - centre)).astype(jnp.bfloat16)
    grad_q = jnp.einsum("hqk,hkd->hqd", grad_s, k_rows, preferred_element_type=jnp.float32) * factor
    grad_k = jnp.einsum("hqk,hqd->hkd", grad_s, q_rows, preferred_element_type=jnp.float32) * factor
    return (grad_q, grad_k, grad_v)


def send_kernel(label_ref, length_ref, q_ref, k_ref, v_ref, up_ref, gain_q_ref, gain_k_ref, out_ref):
    frames, _, wide = out_ref.shape
    slots, channels = q_ref.shape
    head_count = label_ref.shape[0]
    head_size = channels // head_count
    far_count = wide // head_size
    span = slots // frames
    sources = [0] * far_count
    seen = 0
    for h in range(head_count):
        temporal = label_ref[h] == 1
        for j in range(far_count):
            sources[j] = jnp.where(temporal & (seen == j), h, sources[j])
        seen = seen + temporal.astype(jnp.int32)

    def normed(ref, gain_ref):
        rows = ref[...].astype(jnp.float32)
        inverse = lax.rsqrt(jnp.mean(rows * rows, axis=-1, keepdims=True) + 1e-06)
        gain_row = gain_ref[...].reshape(1, channels)
        return ((rows * inverse) * gain_row).astype(jnp.bfloat16).astype(jnp.float32)

    def far_of(rows):
        blocks = [rows[:, h * head_size : (h + 1) * head_size] for h in range(head_count)]
        picked = []
        for j in range(far_count):
            source = sources[j]
            tile = blocks[head_count - 1]
            for h in range(head_count - 2, -1, -1):
                tile = jnp.where(source == h, blocks[h], tile)
            picked.append(tile)
        return jnp.concatenate(picked, axis=1)

    live = lax.broadcasted_iota(jnp.int32, (slots, 1), 0) < length_ref[lax.axis_index("ctx")]
    q_far = far_of(normed(q_ref, gain_q_ref))
    k_far = far_of(normed(k_ref, gain_k_ref))
    v_far = far_of(v_ref[...].astype(jnp.float32))
    up_far = jnp.where(live, far_of(up_ref[...].astype(jnp.float32)), 0.0)
    zero = jnp.zeros((span, wide), jnp.float32)
    k_pad = jnp.concatenate([zero, k_far, zero], axis=0)
    v_pad = jnp.concatenate([zero, v_far, zero], axis=0)
    for d in range(frames):
        rows = slice(d * span, (d + 1) * span)
        window = slice(d * span, d * span + 3 * span)
        out_ref[d] = jnp.concatenate(
            [q_far[rows], up_far[rows], k_pad[window], v_pad[window]], axis=0
        ).astype(out_ref.dtype)


def merge_kernel(
    order_ref,
    back_ref,
    near_out_ref,
    near_q_ref,
    near_k_ref,
    near_v_ref,
    q_unit_ref,
    q_inv_ref,
    k_unit_ref,
    k_inv_ref,
    gain_q_ref,
    gain_k_ref,
    attn_ref,
    gq_ref,
    gk_ref,
    gv_ref,
):
    blocks, _, wide = back_ref.shape
    head_count = order_ref.shape[0]
    far_count, _, head_size = near_q_ref.shape
    span = near_q_ref.shape[1] // blocks
    rows = [back_ref[c].astype(jnp.float32) for c in range(blocks)]

    def plain(first):
        return jnp.concatenate([rows[c][first : first + span] for c in range(blocks)], axis=0)

    def summed(first):
        parts = []
        for c in range(blocks):
            part = rows[c][first + span : first + 2 * span]
            if c + 1 < blocks:
                part = part + rows[c + 1][first : first + span]
            if c >= 1:
                part = part + rows[c - 1][first + 2 * span : first + 3 * span]
            parts.append(part)
        return jnp.concatenate(parts, axis=0)

    far = [plain(0), plain(span), summed(2 * span), summed(5 * span)]
    near = [
        [ref[i].astype(jnp.float32) for i in range(far_count)]
        for ref in (near_out_ref, near_q_ref, near_k_ref, near_v_ref)
    ]
    whole = [[], [], [], []]
    for h in range(head_count):
        place = order_ref[h]
        for t in range(4):
            tile = far[t][:, (far_count - 1) * head_size :]
            for i in range(far_count - 2, -1, -1):
                tile = jnp.where(place == far_count + i, far[t][:, i * head_size : (i + 1) * head_size], tile)
            for i in range(far_count - 1, -1, -1):
                tile = jnp.where(place == i, near[t][i], tile)
            whole[t].append(tile)
    whole = [jnp.concatenate(parts, axis=1) for parts in whole]
    attn_ref[...] = whole[0].astype(attn_ref.dtype)
    gv_ref[...] = whole[3].astype(gv_ref.dtype)
    for grad_rows, unit_ref, inv_ref, gain_ref, out_ref in (
        (whole[1], q_unit_ref, q_inv_ref, gain_q_ref, gq_ref),
        (whole[2], k_unit_ref, k_inv_ref, gain_k_ref, gk_ref),
    ):
        unit_rows = unit_ref[...]
        scaled = grad_rows * gain_ref[...]
        centre = jnp.mean(scaled * unit_rows, axis=-1, keepdims=True)
        out_ref[...] = (inv_ref[...] * (scaled - unit_rows * centre)).astype(out_ref.dtype)


def body(q_raw, k_raw, values, grad_out, gain_q, gain_k, labels, bands, counts):
    frame_count = lax.axis_size("ctx")
    own_frame = lax.axis_index("ctx")
    head_count = labels.shape[0]
    channels = q_raw.shape[3]
    head_size = channels // head_count
    slot_count = q_raw.shape[2]
    pos_span = slot_count // frame_count
    lengths = counts[0]
    frame_ids = jnp.arange(frame_count)
    own_length = jnp.sum(jnp.where(frame_ids == own_frame, lengths, 0))
    slot_live = jnp.arange(slot_count) < own_length
    q_norm, q_unit, q_inv = normalize(q_raw[0, 0], gain_q)
    k_norm, k_unit, k_inv = normalize(k_raw[0, 0], gain_k)
    v_rows = values[0, 0]
    up_rows = jnp.where(slot_live[:, None], grad_out[0, 0], jnp.zeros((), jnp.bfloat16))
    far_count = head_count // 2
    near_count = head_count - far_count
    ids = jnp.arange(head_count)
    before = (labels[None, :] < labels[:, None]) | (
        (labels[None, :] == labels[:, None]) & (ids[None, :] < ids[:, None])
    )
    back_order = jnp.sum(before.astype(jnp.int32), axis=1)
    head_order = jnp.sum(jnp.where(back_order[None, :] == ids[:, None], ids[None, :], 0), axis=1)
    far_heads = head_order[near_count:]
    wide = far_count * head_size

    def sorted_heads(block):
        shaped = block.reshape(block.shape[:-1] + (head_count, head_size))
        return jnp.take(shaped, head_order, axis=-2)

    def heads_first(block):
        return jnp.transpose(block, (1, 0, 2))

    def to_space(block, extent):
        shaped = block.reshape(frame_count, extent, far_count, head_size)
        return jnp.transpose(shaped, (2, 0, 1, 3)).reshape(
            far_count, frame_count * extent, head_size
        )

    def to_time_pair(block, extent):
        shaped = block.reshape(2, far_count, frame_count, extent, head_size)
        return jnp.transpose(shaped, (2, 0, 3, 1, 4)).reshape(frame_count, 2 * extent, wide)

    def spread(near_part, far_part):
        both = jnp.concatenate([near_part, far_part], axis=0)
        result = both[head_count - 1 :]
        for i in range(head_count - 2, -1, -1):
            result = jnp.where((back_order == i)[:, None], both[i : i + 1], result)
        return result

    picked = sorted_heads(jnp.stack([q_norm, k_norm, v_rows, up_rows]))
    units = sorted_heads(jnp.stack([q_unit, k_unit]))[:, :, :near_count]

    send = pl.pallas_call(
        send_kernel,
        out_shape=jax.ShapeDtypeStruct((frame_count, 8 * pos_span, wide), jnp.bfloat16),
        in_specs=[pl.BlockSpec(memory_space=pltpu.SMEM)] * 2 + [pl.BlockSpec(memory_space=pltpu.VMEM)] * 6,
        out_specs=pl.BlockSpec(memory_space=pltpu.VMEM),
        cost_estimate=pl.CostEstimate(
            flops=40 * slot_count * channels, bytes_accessed=12 * slot_count * channels, transcendentals=0
        ),
    )
    outgoing = send(
        labels, lengths, q_raw[0, 0], k_raw[0, 0], v_rows, grad_out[0, 0], gain_q, gain_k
    )
    sent = lax.all_to_all(outgoing, "ctx", split_axis=0, concat_axis=0, tiled=True)

    near_q, near_k, near_v, near_up = (heads_first(picked[i, :, :near_count]) for i in range(4))
    near_allowed = jnp.broadcast_to(
        slot_live[None, None, :], (near_count, slot_count, slot_count)
    )
    near_out, near_w, near_p = attend(near_q, near_k, near_v, near_allowed)
    near_out = jnp.where(slot_live[None, :, None], near_out, 0.0).astype(jnp.bfloat16)
    near_gq, near_gk, near_gv = attend_back(near_q, near_k, near_v, near_w, near_p, near_up)
    near_term_q = jnp.sum(near_gq * heads_first(units[0]), axis=1)
    near_term_k = jnp.sum(near_gk * heads_first(units[1]), axis=1)

    far_q = to_space(sent[:, :pos_span], pos_span)
    far_up = to_space(sent[:, pos_span : 2 * pos_span], pos_span)
    far_k = to_space(sent[:, 2 * pos_span : 5 * pos_span], 3 * pos_span)
    far_v = to_space(sent[:, 5 * pos_span :], 3 * pos_span)
    q_pos = own_frame * pos_span + jnp.arange(pos_span)
    k_pos = own_frame * pos_span - pos_span + jnp.arange(3 * pos_span)
    q_live = (q_pos[None, :] < lengths[:, None]).reshape(-1)
    k_live = (
        (k_pos[None, :] >= 0) & (k_pos[None, :] < slot_count) & (k_pos[None, :] < lengths[:, None])
    ).reshape(-1)
    pos_gap = jnp.abs(jnp.tile(q_pos, frame_count)[:, None] - jnp.tile(k_pos, frame_count)[None, :])
    far_bands = jnp.take(bands, far_heads)
    far_allowed = (pos_gap[None] <= far_bands[:, None, None]) & k_live[None, None, :]
    far_out, far_w, far_p = attend(far_q, far_k, far_v, far_allowed)
    far_out = jnp.where(q_live[None, :, None], far_out, 0.0).astype(jnp.bfloat16)
    far_gq, far_gk, far_gv = attend_back(far_q, far_k, far_v, far_w, far_p, far_up)

    far_term_q = jnp.sum(far_gq * far_q.astype(jnp.float32), axis=1)
    far_term_k = jnp.sum(far_gk * far_k.astype(jnp.float32), axis=1)
    terms = jnp.stack([spread(near_term_q, far_term_q), spread(near_term_k, far_term_k)])
    head_gain = jnp.stack([gain_q, gain_k]).reshape(2, head_count, head_size)
    is_far = (back_order >= near_count)[None, :, None]
    terms = jnp.where(is_far, terms / head_gain, terms)
    terms_hi = terms.astype(jnp.bfloat16)
    terms_lo = (terms - terms_hi.astype(jnp.float32)).astype(jnp.bfloat16)
    term_rows = jnp.stack([terms_hi, terms_lo]).reshape(-1, wide)
    term_count = term_rows.shape[0]

    back = lax.all_to_all(
        jnp.concatenate(
            [
                to_time_pair(jnp.stack([far_out, far_gq.astype(jnp.bfloat16)]), pos_span),
                to_time_pair(jnp.stack([far_gk, far_gv]).astype(jnp.bfloat16), 3 * pos_span),
                jnp.broadcast_to(term_rows[None], (frame_count, term_count, wide)),
            ],
            axis=1,
        ),
        "ctx",
        split_axis=0,
        concat_axis=0,
        tiled=True,
    )
    got_terms = back[:, 8 * pos_span :].reshape(frame_count, 2, 2, head_count, head_size)
    got_terms = got_terms[:, 0].astype(jnp.float32) + got_terms[:, 1].astype(jnp.float32)
    video_count = lax.axis_size("dp")
    video_terms = jnp.sum(got_terms, axis=0).reshape(2 * head_count, head_size)
    all_videos = lax.all_to_all(
        jnp.broadcast_to(video_terms[None], (video_count,) + video_terms.shape),
        "dp",
        split_axis=0,
        concat_axis=0,
        tiled=True,
    )
    totals = jnp.sum(all_videos, axis=0).reshape(2, channels)

    slot_bytes = slot_count * channels
    merge = pl.pallas_call(
        merge_kernel,
        out_shape=[jax.ShapeDtypeStruct((slot_count, channels), jnp.bfloat16)] * 4,
        in_specs=[pl.BlockSpec(memory_space=pltpu.SMEM)] + [pl.BlockSpec(memory_space=pltpu.VMEM)] * 11,
        out_specs=[pl.BlockSpec(memory_space=pltpu.VMEM)] * 4,
        cost_estimate=pl.CostEstimate(
            flops=40 * slot_bytes, bytes_accessed=30 * slot_bytes, transcendentals=0
        ),
    )
    attn_rows, grad_q_rows, grad_k_rows, grad_v_rows = merge(
        back_order,
        back,
        near_out,
        near_gq,
        near_gk,
        near_gv,
        q_unit,
        q_inv,
        k_unit,
        k_inv,
        gain_q.reshape(1, channels),
        gain_k.reshape(1, channels),
    )

    def as_shard(row_block):
        return row_block.reshape(1, 1, slot_count, channels)

    return (
        as_shard(attn_rows),
        as_shard(grad_q_rows),
        as_shard(grad_k_rows),
        as_shard(grad_v_rows),
        totals[0],
        totals[1],
    )


def solution(mesh):
    placed = (
        P("dp", "ctx", None, None),
        P("dp", "ctx", None, None),
        P("dp", "ctx", None, None),
        P("dp", "ctx", None, None),
        P(),
        P(),
        P(),
        P(),
        P("dp", None),
    )
    return jax.shard_map(
        body,
        mesh=mesh,
        in_specs=placed,
        out_specs=(
            P("dp", "ctx", None, None),
            P("dp", "ctx", None, None),
            P("dp", "ctx", None, None),
            P("dp", "ctx", None, None),
            P(),
            P(),
        ),
        check_vma=False,
    )
```

```python
import math

import jax
import jax.numpy as jnp
from jax import lax
from jax.experimental import pallas as pl
from jax.experimental.pallas import tpu as pltpu
from jax.sharding import PartitionSpec as P


def normalize(raw_rows, gain_row):
    full_rows = raw_rows.astype(jnp.float32)
    inverse = lax.rsqrt(jnp.mean(full_rows * full_rows, axis=-1, keepdims=True) + 1e-06)
    unit_rows = full_rows * inverse
    return ((unit_rows * gain_row).astype(jnp.bfloat16), unit_rows, inverse)


def normalize_back(grad_rows, unit_rows, inverse, gain_row):
    scaled = grad_rows * gain_row
    return inverse * (scaled - unit_rows * jnp.mean(scaled * unit_rows, axis=-1, keepdims=True))


def attend(q_rows, k_rows, v_rows, allowed):
    factor = 1.0 / math.sqrt(q_rows.shape[-1])
    scores = jnp.einsum("hqd,hkd->hqk", q_rows, k_rows, preferred_element_type=jnp.float32) * factor
    scores = jnp.where(allowed, scores, -1e30)
    row_peak = jnp.max(scores, axis=-1, keepdims=True)
    exp_terms = jnp.where(allowed, jnp.exp(scores - row_peak), 0.0)
    weights = exp_terms / jnp.sum(exp_terms, axis=-1, keepdims=True)
    prob_bf16 = weights.astype(jnp.bfloat16)
    mixed_rows = jnp.einsum("hqk,hkd->hqd", prob_bf16, v_rows, preferred_element_type=jnp.float32)
    return (mixed_rows, weights, prob_bf16)


def attend_back(q_rows, k_rows, v_rows, weights, prob_bf16, upstream):
    factor = 1.0 / math.sqrt(q_rows.shape[-1])
    grad_v = jnp.einsum("hqk,hqd->hkd", prob_bf16, upstream, preferred_element_type=jnp.float32)
    grad_p = jnp.einsum("hqd,hkd->hqk", upstream, v_rows, preferred_element_type=jnp.float32)
    centre = jnp.sum(weights * grad_p, axis=-1, keepdims=True)
    grad_s = (weights * (grad_p - centre)).astype(jnp.bfloat16)
    grad_q = jnp.einsum("hqk,hkd->hqd", grad_s, k_rows, preferred_element_type=jnp.float32) * factor
    grad_k = jnp.einsum("hqk,hqd->hkd", grad_s, q_rows, preferred_element_type=jnp.float32) * factor
    return (grad_q, grad_k, grad_v)


def send_kernel(label_ref, length_ref, q_ref, k_ref, v_ref, up_ref, gain_q_ref, gain_k_ref, out_ref):
    frames, _, wide = out_ref.shape
    slots, channels = q_ref.shape
    head_count = label_ref.shape[0]
    head_size = channels // head_count
    far_count = wide // head_size
    span = slots // frames
    sources = [0] * far_count
    seen = 0
    for h in range(head_count):
        temporal = label_ref[h] == 1
        for j in range(far_count):
            sources[j] = jnp.where(temporal & (seen == j), h, sources[j])
        seen = seen + temporal.astype(jnp.int32)

    def normed(ref, gain_ref):
        rows = ref[...].astype(jnp.float32)
        inverse = lax.rsqrt(jnp.mean(rows * rows, axis=-1, keepdims=True) + 1e-06)
        gain_row = gain_ref[...].reshape(1, channels)
        return ((rows * inverse) * gain_row).astype(jnp.bfloat16).astype(jnp.float32)

    def far_of(rows):
        blocks = [rows[:, h * head_size : (h + 1) * head_size] for h in range(head_count)]
        picked = []
        for j in range(far_count):
            source = sources[j]
            tile = blocks[head_count - 1]
            for h in range(head_count - 2, -1, -1):
                tile = jnp.where(source == h, blocks[h], tile)
            picked.append(tile)
        return jnp.concatenate(picked, axis=1)

    def far_read(ref):
        return jnp.concatenate(
            [ref[:, pl.ds(pl.multiple_of(sources[j] * head_size, head_size), head_size)] for j in range(far_count)],
            axis=1,
        ).astype(jnp.float32)

    live = lax.broadcasted_iota(jnp.int32, (slots, 1), 0) < length_ref[lax.axis_index("ctx")]
    q_far = far_of(normed(q_ref, gain_q_ref))
    k_far = far_of(normed(k_ref, gain_k_ref))
    v_far = far_read(v_ref)
    up_far = jnp.where(live, far_read(up_ref), 0.0)
    zero = jnp.zeros((span, wide), jnp.float32)
    k_pad = jnp.concatenate([zero, k_far, zero], axis=0)
    v_pad = jnp.concatenate([zero, v_far, zero], axis=0)
    for d in range(frames):
        rows = slice(d * span, (d + 1) * span)
        window = slice(d * span, d * span + 3 * span)
        out_ref[d] = jnp.concatenate(
            [q_far[rows], up_far[rows], k_pad[window], v_pad[window]], axis=0
        ).astype(out_ref.dtype)


def merge_kernel(
    order_ref,
    back_ref,
    near_out_ref,
    near_q_ref,
    near_k_ref,
    near_v_ref,
    q_unit_ref,
    q_inv_ref,
    k_unit_ref,
    k_inv_ref,
    gain_q_ref,
    gain_k_ref,
    attn_ref,
    gq_ref,
    gk_ref,
    gv_ref,
):
    blocks, _, wide = back_ref.shape
    head_count = order_ref.shape[0]
    far_count, _, head_size = near_q_ref.shape
    span = near_q_ref.shape[1] // blocks
    rows = [back_ref[c].astype(jnp.float32) for c in range(blocks)]

    def plain(first):
        return jnp.concatenate([rows[c][first : first + span] for c in range(blocks)], axis=0)

    def summed(first):
        parts = []
        for c in range(blocks):
            part = rows[c][first + span : first + 2 * span]
            if c + 1 < blocks:
                part = part + rows[c + 1][first : first + span]
            if c >= 1:
                part = part + rows[c - 1][first + 2 * span : first + 3 * span]
            parts.append(part)
        return jnp.concatenate(parts, axis=0)

    far = [plain(0), plain(span), summed(2 * span), summed(5 * span)]
    near = [
        [ref[i].astype(jnp.float32) for i in range(far_count)]
        for ref in (near_out_ref, near_q_ref, near_k_ref, near_v_ref)
    ]
    whole = [[], [], [], []]
    for h in range(head_count):
        place = order_ref[h]
        for t in range(4):
            tile = far[t][:, (far_count - 1) * head_size :]
            for i in range(far_count - 2, -1, -1):
                tile = jnp.where(place == far_count + i, far[t][:, i * head_size : (i + 1) * head_size], tile)
            for i in range(far_count - 1, -1, -1):
                tile = jnp.where(place == i, near[t][i], tile)
            whole[t].append(tile)
    whole = [jnp.concatenate(parts, axis=1) for parts in whole]
    attn_ref[...] = whole[0].astype(attn_ref.dtype)
    gv_ref[...] = whole[3].astype(gv_ref.dtype)
    for grad_rows, unit_ref, inv_ref, gain_ref, out_ref in (
        (whole[1], q_unit_ref, q_inv_ref, gain_q_ref, gq_ref),
        (whole[2], k_unit_ref, k_inv_ref, gain_k_ref, gk_ref),
    ):
        unit_rows = unit_ref[...]
        scaled = grad_rows * gain_ref[...]
        centre = jnp.mean(scaled * unit_rows, axis=-1, keepdims=True)
        out_ref[...] = (inv_ref[...] * (scaled - unit_rows * centre)).astype(out_ref.dtype)


def body(q_raw, k_raw, values, grad_out, gain_q, gain_k, labels, bands, counts):
    frame_count = lax.axis_size("ctx")
    own_frame = lax.axis_index("ctx")
    head_count = labels.shape[0]
    channels = q_raw.shape[3]
    head_size = channels // head_count
    slot_count = q_raw.shape[2]
    pos_span = slot_count // frame_count
    lengths = counts[0]
    frame_ids = jnp.arange(frame_count)
    own_length = jnp.sum(jnp.where(frame_ids == own_frame, lengths, 0))
    slot_live = jnp.arange(slot_count) < own_length
    q_norm, q_unit, q_inv = normalize(q_raw[0, 0], gain_q)
    k_norm, k_unit, k_inv = normalize(k_raw[0, 0], gain_k)
    v_rows = values[0, 0]
    up_rows = jnp.where(slot_live[:, None], grad_out[0, 0], jnp.zeros((), jnp.bfloat16))
    far_count = head_count // 2
    near_count = head_count - far_count
    ids = jnp.arange(head_count)
    before = (labels[None, :] < labels[:, None]) | (
        (labels[None, :] == labels[:, None]) & (ids[None, :] < ids[:, None])
    )
    back_order = jnp.sum(before.astype(jnp.int32), axis=1)
    head_order = jnp.sum(jnp.where(back_order[None, :] == ids[:, None], ids[None, :], 0), axis=1)
    far_heads = head_order[near_count:]
    wide = far_count * head_size

    def sorted_heads(block):
        shaped = block.reshape(block.shape[:-1] + (head_count, head_size))
        return jnp.take(shaped, head_order, axis=-2)

    def heads_first(block):
        return jnp.transpose(block, (1, 0, 2))

    def to_space(block, extent):
        shaped = block.reshape(frame_count, extent, far_count, head_size)
        return jnp.transpose(shaped, (2, 0, 1, 3)).reshape(
            far_count, frame_count * extent, head_size
        )

    def to_time_pair(block, extent):
        shaped = block.reshape(2, far_count, frame_count, extent, head_size)
        return jnp.transpose(shaped, (2, 0, 3, 1, 4)).reshape(frame_count, 2 * extent, wide)

    def spread(near_part, far_part):
        both = jnp.concatenate([near_part, far_part], axis=0)
        result = both[head_count - 1 :]
        for i in range(head_count - 2, -1, -1):
            result = jnp.where((back_order == i)[:, None], both[i : i + 1], result)
        return result

    picked = sorted_heads(jnp.stack([q_norm, k_norm, v_rows, up_rows]))
    units = sorted_heads(jnp.stack([q_unit, k_unit]))[:, :, :near_count]

    send = pl.pallas_call(
        send_kernel,
        out_shape=jax.ShapeDtypeStruct((frame_count, 8 * pos_span, wide), jnp.bfloat16),
        in_specs=[pl.BlockSpec(memory_space=pltpu.SMEM)] * 2 + [pl.BlockSpec(memory_space=pltpu.VMEM)] * 6,
        out_specs=pl.BlockSpec(memory_space=pltpu.VMEM),
        cost_estimate=pl.CostEstimate(
            flops=40 * slot_count * channels, bytes_accessed=12 * slot_count * channels, transcendentals=0
        ),
    )
    outgoing = send(
        labels, lengths, q_raw[0, 0], k_raw[0, 0], v_rows, grad_out[0, 0], gain_q, gain_k
    )
    sent = lax.all_to_all(outgoing, "ctx", split_axis=0, concat_axis=0, tiled=True)

    near_q, near_k, near_v, near_up = (heads_first(picked[i, :, :near_count]) for i in range(4))
    near_allowed = jnp.broadcast_to(
        slot_live[None, None, :], (near_count, slot_count, slot_count)
    )
    near_out, near_w, near_p = attend(near_q, near_k, near_v, near_allowed)
    near_out = jnp.where(slot_live[None, :, None], near_out, 0.0).astype(jnp.bfloat16)
    near_gq, near_gk, near_gv = attend_back(near_q, near_k, near_v, near_w, near_p, near_up)
    near_term_q = jnp.sum(near_gq * heads_first(units[0]), axis=1)
    near_term_k = jnp.sum(near_gk * heads_first(units[1]), axis=1)

    far_q = to_space(sent[:, :pos_span], pos_span)
    far_up = to_space(sent[:, pos_span : 2 * pos_span], pos_span)
    far_k = to_space(sent[:, 2 * pos_span : 5 * pos_span], 3 * pos_span)
    far_v = to_space(sent[:, 5 * pos_span :], 3 * pos_span)
    q_pos = own_frame * pos_span + jnp.arange(pos_span)
    k_pos = own_frame * pos_span - pos_span + jnp.arange(3 * pos_span)
    q_live = (q_pos[None, :] < lengths[:, None]).reshape(-1)
    k_live = (
        (k_pos[None, :] >= 0) & (k_pos[None, :] < slot_count) & (k_pos[None, :] < lengths[:, None])
    ).reshape(-1)
    pos_gap = jnp.abs(jnp.tile(q_pos, frame_count)[:, None] - jnp.tile(k_pos, frame_count)[None, :])
    far_bands = jnp.take(bands, far_heads)
    far_allowed = (pos_gap[None] <= far_bands[:, None, None]) & k_live[None, None, :]
    far_out, far_w, far_p = attend(far_q, far_k, far_v, far_allowed)
    far_out = jnp.where(q_live[None, :, None], far_out, 0.0).astype(jnp.bfloat16)
    far_gq, far_gk, far_gv = attend_back(far_q, far_k, far_v, far_w, far_p, far_up)

    far_term_q = jnp.sum(far_gq * far_q.astype(jnp.float32), axis=1)
    far_term_k = jnp.sum(far_gk * far_k.astype(jnp.float32), axis=1)
    terms = jnp.stack([spread(near_term_q, far_term_q), spread(near_term_k, far_term_k)])
    head_gain = jnp.stack([gain_q, gain_k]).reshape(2, head_count, head_size)
    is_far = (back_order >= near_count)[None, :, None]
    terms = jnp.where(is_far, terms / head_gain, terms)
    terms_hi = terms.astype(jnp.bfloat16)
    terms_lo = (terms - terms_hi.astype(jnp.float32)).astype(jnp.bfloat16)
    term_rows = jnp.stack([terms_hi, terms_lo]).reshape(-1, wide)
    term_count = term_rows.shape[0]

    back = lax.all_to_all(
        jnp.concatenate(
            [
                to_time_pair(jnp.stack([far_out, far_gq.astype(jnp.bfloat16)]), pos_span),
                to_time_pair(jnp.stack([far_gk, far_gv]).astype(jnp.bfloat16), 3 * pos_span),
                jnp.broadcast_to(term_rows[None], (frame_count, term_count, wide)),
            ],
            axis=1,
        ),
        "ctx",
        split_axis=0,
        concat_axis=0,
        tiled=True,
    )
    got_terms = back[:, 8 * pos_span :].reshape(frame_count, 2, 2, head_count, head_size)
    got_terms = got_terms[:, 0].astype(jnp.float32) + got_terms[:, 1].astype(jnp.float32)
    video_count = lax.axis_size("dp")
    video_terms = jnp.sum(got_terms, axis=0)
    all_videos = lax.all_to_all(
        jnp.broadcast_to(video_terms[None], (video_count,) + video_terms.shape),
        "dp",
        split_axis=0,
        concat_axis=0,
        tiled=True,
    )
    totals = jnp.sum(all_videos, axis=0).reshape(2, channels)

    slot_bytes = slot_count * channels
    merge = pl.pallas_call(
        merge_kernel,
        out_shape=[jax.ShapeDtypeStruct((slot_count, channels), jnp.bfloat16)] * 4,
        in_specs=[pl.BlockSpec(memory_space=pltpu.SMEM)] + [pl.BlockSpec(memory_space=pltpu.VMEM)] * 11,
        out_specs=[pl.BlockSpec(memory_space=pltpu.VMEM)] * 4,
        cost_estimate=pl.CostEstimate(
            flops=40 * slot_bytes, bytes_accessed=30 * slot_bytes, transcendentals=0
        ),
    )
    attn_rows, grad_q_rows, grad_k_rows, grad_v_rows = merge(
        back_order,
        back,
        near_out,
        near_gq,
        near_gk,
        near_gv,
        q_unit,
        q_inv,
        k_unit,
        k_inv,
        gain_q.reshape(1, channels),
        gain_k.reshape(1, channels),
    )

    def as_shard(row_block):
        return row_block.reshape(1, 1, slot_count, channels)

    return (
        as_shard(attn_rows),
        as_shard(grad_q_rows),
        as_shard(grad_k_rows),
        as_shard(grad_v_rows),
        totals[0],
        totals[1],
    )


def solution(mesh):
    placed = (
        P("dp", "ctx", None, None),
        P("dp", "ctx", None, None),
        P("dp", "ctx", None, None),
        P("dp", "ctx", None, None),
        P(),
        P(),
        P(),
        P(),
        P("dp", None),
    )
    return jax.shard_map(
        body,
        mesh=mesh,
        in_specs=placed,
        out_specs=(
            P("dp", "ctx", None, None),
            P("dp", "ctx", None, None),
            P("dp", "ctx", None, None),
            P("dp", "ctx", None, None),
            P(),
            P(),
        ),
        check_vma=False,
    )
```

```python
import math

import jax
import jax.numpy as jnp
from jax import lax
from jax.experimental import pallas as pl
from jax.experimental.pallas import tpu as pltpu
from jax.sharding import PartitionSpec as P


def normalize(raw_rows, gain_row):
    full_rows = raw_rows.astype(jnp.float32)
    inverse = lax.rsqrt(jnp.mean(full_rows * full_rows, axis=-1, keepdims=True) + 1e-06)
    unit_rows = full_rows * inverse
    return ((unit_rows * gain_row).astype(jnp.bfloat16), unit_rows, inverse)


def normalize_back(grad_rows, unit_rows, inverse, gain_row):
    scaled = grad_rows * gain_row
    return inverse * (scaled - unit_rows * jnp.mean(scaled * unit_rows, axis=-1, keepdims=True))


def attend(q_rows, k_rows, v_rows, allowed):
    factor = 1.0 / math.sqrt(q_rows.shape[-1])
    scores = jnp.einsum("hqd,hkd->hqk", q_rows, k_rows, preferred_element_type=jnp.float32) * factor
    scores = jnp.where(allowed, scores, -1e30)
    row_peak = jnp.max(scores, axis=-1, keepdims=True)
    exp_terms = jnp.where(allowed, jnp.exp(scores - row_peak), 0.0)
    weights = exp_terms / jnp.sum(exp_terms, axis=-1, keepdims=True)
    prob_bf16 = weights.astype(jnp.bfloat16)
    mixed_rows = jnp.einsum("hqk,hkd->hqd", prob_bf16, v_rows, preferred_element_type=jnp.float32)
    return (mixed_rows, weights, prob_bf16)


def attend_back(q_rows, k_rows, v_rows, weights, prob_bf16, upstream):
    factor = 1.0 / math.sqrt(q_rows.shape[-1])
    grad_v = jnp.einsum("hqk,hqd->hkd", prob_bf16, upstream, preferred_element_type=jnp.float32)
    grad_p = jnp.einsum("hqd,hkd->hqk", upstream, v_rows, preferred_element_type=jnp.float32)
    centre = jnp.sum(weights * grad_p, axis=-1, keepdims=True)
    grad_s = (weights * (grad_p - centre)).astype(jnp.bfloat16)
    grad_q = jnp.einsum("hqk,hkd->hqd", grad_s, k_rows, preferred_element_type=jnp.float32) * factor
    grad_k = jnp.einsum("hqk,hqd->hkd", grad_s, q_rows, preferred_element_type=jnp.float32) * factor
    return (grad_q, grad_k, grad_v)


def send_kernel(label_ref, length_ref, q_ref, k_ref, v_ref, up_ref, gain_q_ref, gain_k_ref, out_ref):
    frames, _, wide = out_ref.shape
    slots, channels = q_ref.shape
    head_count = label_ref.shape[0]
    head_size = channels // head_count
    far_count = wide // head_size
    span = slots // frames
    sources = [0] * far_count
    seen = 0
    for h in range(head_count):
        temporal = label_ref[h] == 1
        for j in range(far_count):
            sources[j] = jnp.where(temporal & (seen == j), h, sources[j])
        seen = seen + temporal.astype(jnp.int32)

    def normed(ref, gain_ref):
        rows = ref[...].astype(jnp.float32)
        inverse = lax.rsqrt(jnp.mean(rows * rows, axis=-1, keepdims=True) + 1e-06)
        gain_row = gain_ref[...].reshape(1, channels)
        return ((rows * inverse) * gain_row).astype(jnp.bfloat16).astype(jnp.float32)

    def far_of(rows):
        blocks = [rows[:, h * head_size : (h + 1) * head_size] for h in range(head_count)]
        picked = []
        for j in range(far_count):
            source = sources[j]
            tile = blocks[head_count - 1]
            for h in range(head_count - 2, -1, -1):
                tile = jnp.where(source == h, blocks[h], tile)
            picked.append(tile)
        return jnp.concatenate(picked, axis=1)

    def far_read(ref):
        return jnp.concatenate(
            [ref[:, pl.ds(pl.multiple_of(sources[j] * head_size, head_size), head_size)] for j in range(far_count)],
            axis=1,
        ).astype(jnp.float32)

    live = lax.broadcasted_iota(jnp.int32, (slots, 1), 0) < length_ref[lax.axis_index("ctx")]
    def far_normed(ref, gain_ref):
        rows = ref[...].astype(jnp.float32)
        inverse = lax.rsqrt(jnp.mean(rows * rows, axis=-1, keepdims=True) + 1e-06)
        parts = []
        for j in range(far_count):
            lanes = pl.ds(pl.multiple_of(sources[j] * head_size, head_size), head_size)
            gain_part = gain_ref[lanes].reshape(1, head_size)
            parts.append(((ref[:, lanes].astype(jnp.float32) * inverse) * gain_part).astype(jnp.bfloat16))
        return jnp.concatenate(parts, axis=1).astype(jnp.float32)

    q_far = far_normed(q_ref, gain_q_ref)
    k_far = far_normed(k_ref, gain_k_ref)
    v_far = far_read(v_ref)
    up_far = jnp.where(live, far_read(up_ref), 0.0)
    zero = jnp.zeros((span, wide), jnp.float32)
    k_pad = jnp.concatenate([zero, k_far, zero], axis=0)
    v_pad = jnp.concatenate([zero, v_far, zero], axis=0)
    for d in range(frames):
        rows = slice(d * span, (d + 1) * span)
        window = slice(d * span, d * span + 3 * span)
        out_ref[d] = jnp.concatenate(
            [q_far[rows], up_far[rows], k_pad[window], v_pad[window]], axis=0
        ).astype(out_ref.dtype)


def merge_kernel(
    order_ref,
    back_ref,
    near_out_ref,
    near_q_ref,
    near_k_ref,
    near_v_ref,
    q_unit_ref,
    q_inv_ref,
    k_unit_ref,
    k_inv_ref,
    gain_q_ref,
    gain_k_ref,
    attn_ref,
    gq_ref,
    gk_ref,
    gv_ref,
):
    blocks, _, wide = back_ref.shape
    head_count = order_ref.shape[0]
    far_count, _, head_size = near_q_ref.shape
    span = near_q_ref.shape[1] // blocks
    rows = [back_ref[c].astype(jnp.float32) for c in range(blocks)]

    def plain(first):
        return jnp.concatenate([rows[c][first : first + span] for c in range(blocks)], axis=0)

    def summed(first):
        parts = []
        for c in range(blocks):
            part = rows[c][first + span : first + 2 * span]
            if c + 1 < blocks:
                part = part + rows[c + 1][first : first + span]
            if c >= 1:
                part = part + rows[c - 1][first + 2 * span : first + 3 * span]
            parts.append(part)
        return jnp.concatenate(parts, axis=0)

    far = [plain(0), plain(span), summed(2 * span), summed(5 * span)]
    near = [
        [ref[i].astype(jnp.float32) for i in range(far_count)]
        for ref in (near_out_ref, near_q_ref, near_k_ref, near_v_ref)
    ]
    whole = [[], [], [], []]
    for h in range(head_count):
        place = order_ref[h]
        for t in range(4):
            tile = far[t][:, (far_count - 1) * head_size :]
            for i in range(far_count - 2, -1, -1):
                tile = jnp.where(place == far_count + i, far[t][:, i * head_size : (i + 1) * head_size], tile)
            for i in range(far_count - 1, -1, -1):
                tile = jnp.where(place == i, near[t][i], tile)
            whole[t].append(tile)
    whole = [jnp.concatenate(parts, axis=1) for parts in whole]
    attn_ref[...] = whole[0].astype(attn_ref.dtype)
    gv_ref[...] = whole[3].astype(gv_ref.dtype)
    for grad_rows, unit_ref, inv_ref, gain_ref, out_ref in (
        (whole[1], q_unit_ref, q_inv_ref, gain_q_ref, gq_ref),
        (whole[2], k_unit_ref, k_inv_ref, gain_k_ref, gk_ref),
    ):
        unit_rows = unit_ref[...]
        scaled = grad_rows * gain_ref[...]
        centre = jnp.mean(scaled * unit_rows, axis=-1, keepdims=True)
        out_ref[...] = (inv_ref[...] * (scaled - unit_rows * centre)).astype(out_ref.dtype)


def body(q_raw, k_raw, values, grad_out, gain_q, gain_k, labels, bands, counts):
    frame_count = lax.axis_size("ctx")
    own_frame = lax.axis_index("ctx")
    head_count = labels.shape[0]
    channels = q_raw.shape[3]
    head_size = channels // head_count
    slot_count = q_raw.shape[2]
    pos_span = slot_count // frame_count
    lengths = counts[0]
    frame_ids = jnp.arange(frame_count)
    own_length = jnp.sum(jnp.where(frame_ids == own_frame, lengths, 0))
    slot_live = jnp.arange(slot_count) < own_length
    q_norm, q_unit, q_inv = normalize(q_raw[0, 0], gain_q)
    k_norm, k_unit, k_inv = normalize(k_raw[0, 0], gain_k)
    v_rows = values[0, 0]
    up_rows = jnp.where(slot_live[:, None], grad_out[0, 0], jnp.zeros((), jnp.bfloat16))
    far_count = head_count // 2
    near_count = head_count - far_count
    ids = jnp.arange(head_count)
    before = (labels[None, :] < labels[:, None]) | (
        (labels[None, :] == labels[:, None]) & (ids[None, :] < ids[:, None])
    )
    back_order = jnp.sum(before.astype(jnp.int32), axis=1)
    head_order = jnp.sum(jnp.where(back_order[None, :] == ids[:, None], ids[None, :], 0), axis=1)
    far_heads = head_order[near_count:]
    wide = far_count * head_size

    def sorted_heads(block):
        shaped = block.reshape(block.shape[:-1] + (head_count, head_size))
        return jnp.take(shaped, head_order, axis=-2)

    def heads_first(block):
        return jnp.transpose(block, (1, 0, 2))

    def to_space(block, extent):
        shaped = block.reshape(frame_count, extent, far_count, head_size)
        return jnp.transpose(shaped, (2, 0, 1, 3)).reshape(
            far_count, frame_count * extent, head_size
        )

    def to_time_pair(block, extent):
        shaped = block.reshape(2, far_count, frame_count, extent, head_size)
        return jnp.transpose(shaped, (2, 0, 3, 1, 4)).reshape(frame_count, 2 * extent, wide)

    def spread(near_part, far_part):
        both = jnp.concatenate([near_part, far_part], axis=0)
        result = both[head_count - 1 :]
        for i in range(head_count - 2, -1, -1):
            result = jnp.where((back_order == i)[:, None], both[i : i + 1], result)
        return result

    picked = sorted_heads(jnp.stack([q_norm, k_norm, v_rows, up_rows]))
    units = sorted_heads(jnp.stack([q_unit, k_unit]))[:, :, :near_count]

    send = pl.pallas_call(
        send_kernel,
        out_shape=jax.ShapeDtypeStruct((frame_count, 8 * pos_span, wide), jnp.bfloat16),
        in_specs=[pl.BlockSpec(memory_space=pltpu.SMEM)] * 2 + [pl.BlockSpec(memory_space=pltpu.VMEM)] * 6,
        out_specs=pl.BlockSpec(memory_space=pltpu.VMEM),
        cost_estimate=pl.CostEstimate(
            flops=40 * slot_count * channels, bytes_accessed=12 * slot_count * channels, transcendentals=0
        ),
    )
    outgoing = send(
        labels, lengths, q_raw[0, 0], k_raw[0, 0], v_rows, grad_out[0, 0], gain_q, gain_k
    )
    sent = lax.all_to_all(outgoing, "ctx", split_axis=0, concat_axis=0, tiled=True)

    near_q, near_k, near_v, near_up = (heads_first(picked[i, :, :near_count]) for i in range(4))
    near_allowed = jnp.broadcast_to(
        slot_live[None, None, :], (near_count, slot_count, slot_count)
    )
    near_out, near_w, near_p = attend(near_q, near_k, near_v, near_allowed)
    near_out = jnp.where(slot_live[None, :, None], near_out, 0.0).astype(jnp.bfloat16)
    near_gq, near_gk, near_gv = attend_back(near_q, near_k, near_v, near_w, near_p, near_up)
    near_term_q = jnp.sum(near_gq * heads_first(units[0]), axis=1)
    near_term_k = jnp.sum(near_gk * heads_first(units[1]), axis=1)

    far_q = to_space(sent[:, :pos_span], pos_span)
    far_up = to_space(sent[:, pos_span : 2 * pos_span], pos_span)
    far_k = to_space(sent[:, 2 * pos_span : 5 * pos_span], 3 * pos_span)
    far_v = to_space(sent[:, 5 * pos_span :], 3 * pos_span)
    q_pos = own_frame * pos_span + jnp.arange(pos_span)
    k_pos = own_frame * pos_span - pos_span + jnp.arange(3 * pos_span)
    q_live = (q_pos[None, :] < lengths[:, None]).reshape(-1)
    k_live = (
        (k_pos[None, :] >= 0) & (k_pos[None, :] < slot_count) & (k_pos[None, :] < lengths[:, None])
    ).reshape(-1)
    pos_gap = jnp.abs(jnp.tile(q_pos, frame_count)[:, None] - jnp.tile(k_pos, frame_count)[None, :])
    far_bands = jnp.take(bands, far_heads)
    far_allowed = (pos_gap[None] <= far_bands[:, None, None]) & k_live[None, None, :]
    far_out, far_w, far_p = attend(far_q, far_k, far_v, far_allowed)
    far_out = jnp.where(q_live[None, :, None], far_out, 0.0).astype(jnp.bfloat16)
    far_gq, far_gk, far_gv = attend_back(far_q, far_k, far_v, far_w, far_p, far_up)

    far_term_q = jnp.sum(far_gq * far_q.astype(jnp.float32), axis=1)
    far_term_k = jnp.sum(far_gk * far_k.astype(jnp.float32), axis=1)
    terms = jnp.stack([spread(near_term_q, far_term_q), spread(near_term_k, far_term_k)])
    head_gain = jnp.stack([gain_q, gain_k]).reshape(2, head_count, head_size)
    is_far = (back_order >= near_count)[None, :, None]
    terms = jnp.where(is_far, terms / head_gain, terms)
    terms_hi = terms.astype(jnp.bfloat16)
    terms_lo = (terms - terms_hi.astype(jnp.float32)).astype(jnp.bfloat16)
    term_rows = jnp.stack([terms_hi, terms_lo]).reshape(-1, wide)
    term_count = term_rows.shape[0]

    back = lax.all_to_all(
        jnp.concatenate(
            [
                to_time_pair(jnp.stack([far_out, far_gq.astype(jnp.bfloat16)]), pos_span),
                to_time_pair(jnp.stack([far_gk, far_gv]).astype(jnp.bfloat16), 3 * pos_span),
                jnp.broadcast_to(term_rows[None], (frame_count, term_count, wide)),
            ],
            axis=1,
        ),
        "ctx",
        split_axis=0,
        concat_axis=0,
        tiled=True,
    )
    got_terms = back[:, 8 * pos_span :].reshape(frame_count, 2, 2, head_count, head_size)
    got_terms = got_terms[:, 0].astype(jnp.float32) + got_terms[:, 1].astype(jnp.float32)
    video_count = lax.axis_size("dp")
    video_terms = jnp.sum(got_terms, axis=0)
    all_videos = lax.all_to_all(
        jnp.broadcast_to(video_terms[None], (video_count,) + video_terms.shape),
        "dp",
        split_axis=0,
        concat_axis=0,
        tiled=True,
    )
    totals = jnp.sum(all_videos, axis=0).reshape(2, channels)

    slot_bytes = slot_count * channels
    merge = pl.pallas_call(
        merge_kernel,
        out_shape=[jax.ShapeDtypeStruct((slot_count, channels), jnp.bfloat16)] * 4,
        in_specs=[pl.BlockSpec(memory_space=pltpu.SMEM)] + [pl.BlockSpec(memory_space=pltpu.VMEM)] * 11,
        out_specs=[pl.BlockSpec(memory_space=pltpu.VMEM)] * 4,
        cost_estimate=pl.CostEstimate(
            flops=40 * slot_bytes, bytes_accessed=30 * slot_bytes, transcendentals=0
        ),
    )
    attn_rows, grad_q_rows, grad_k_rows, grad_v_rows = merge(
        back_order,
        back,
        near_out,
        near_gq,
        near_gk,
        near_gv,
        q_unit,
        q_inv,
        k_unit,
        k_inv,
        gain_q.reshape(1, channels),
        gain_k.reshape(1, channels),
    )

    def as_shard(row_block):
        return row_block.reshape(1, 1, slot_count, channels)

    return (
        as_shard(attn_rows),
        as_shard(grad_q_rows),
        as_shard(grad_k_rows),
        as_shard(grad_v_rows),
        totals[0],
        totals[1],
    )


def solution(mesh):
    placed = (
        P("dp", "ctx", None, None),
        P("dp", "ctx", None, None),
        P("dp", "ctx", None, None),
        P("dp", "ctx", None, None),
        P(),
        P(),
        P(),
        P(),
        P("dp", None),
    )
    return jax.shard_map(
        body,
        mesh=mesh,
        in_specs=placed,
        out_specs=(
            P("dp", "ctx", None, None),
            P("dp", "ctx", None, None),
            P("dp", "ctx", None, None),
            P("dp", "ctx", None, None),
            P(),
            P(),
        ),
        check_vma=False,
    )
```
